128 devices in a mesh: seq: 16 (over z, y), tp: 8 (over x, core).
Axes of the slice: x: 4, y: 4, z: 4, core: 2. Of those that a mesh axis runs over, the one named last changes fastest.
Arguments:
- hidden: bfloat16 [128, 64, 2560], P(None, 'seq'), may hold values from -6 to 6
- gain_attn: bfloat16 [2560], replicated, may hold values from 0.099609375 to 1.8984375
- w_query: bfloat16 [2560, 2560], P(None, 'tp'), may hold values from -0.125 to 0.125
- w_key: bfloat16 [2560, 640], P(None, 'tp'), may hold values from -0.375 to 0.375
- w_value: bfloat16 [2560, 640], P(None, 'tp'), may hold values from -0.25 to 0.25
- w_out: bfloat16 [2560, 2560], P('tp'), may hold values from -0.125 to 0.125
- gain_ffn: bfloat16 [2560], replicated, may hold values from 0.099609375 to 1.8984375
- w_gate: bfloat16 [2560, 6912], P(None, 'tp'), may hold values from -0.125 to 0.125
- w_up: bfloat16 [2560, 6912], P(None, 'tp'), may hold values from -0.125 to 0.125
- w_down: bfloat16 [6912, 2560], P('tp'), may hold values from -0.078125 to 0.078125
- shared_pages: bfloat16 [320, 8, 2, 80, 128], P('seq', 'tp'), may hold values from -270 to 270
- leaf_pages: bfloat16 [512, 8, 2, 80, 128], P('seq', 'tp'), may hold values from -270 to 270
- root_table: int32 [4, 16], replicated, may hold values from 0 to 319, as said below
- mid_table: int32 [16, 16], replicated, may hold values from 0 to 319, as said below
- leaf_table: int32 [64, 8], replicated, may hold values from 0 to 511, as said below
- root_len: int32 [4], replicated, may hold values from 1024 to 2048, as said below
- mid_len: int32 [16], replicated, may hold values from 1 to 2048, as said below
- leaf_len: int32 [64], replicated, may hold values from 1 to 1024, as said below
- mid_parent: int32 [16], replicated, may hold values from 0 to 3
- leaf_parent: int32 [64], replicated, may hold values from 0 to 15
- slot_request: int32 [64], replicated, may hold values from 0 to 63, as said below
Outputs:
- layer_out: float32 [128, 64, 2560], P('tp', 'seq')
The draws below stay inside these ranges and needn't reach their ends.
Inputs may be any that keep to these rules, and one draw needn't show every extreme that they name: `slot_request`: A permutation of the requests. The 4 requests of slots 4 * s to 4 * s + 3 have their leaves with 4 distinct owners (see leaf_table). `leaf_table`: all pages of one request's leaf lie with one owner, the index of seq equal to page // 32; each owner holds the leaves of exactly 4 requests, and every leaf page is named once. `root_table`: with mid_table, names every shared page exactly once. Shared page g is held by the index of seq g // 20; each index holds exactly 1 page of every root. `mid_table`: with root_table, names every shared page exactly once. Each index of seq holds exactly 1 page of every middle node. `root_len`: some root reaches the largest value. `mid_len`: some middle node reaches the largest value. `leaf_len`: some leaf reaches the largest value.
All inputs are finite; a program needn't handle non-finite values.
Results may differ from the reference program's by a relative error of at most 0.009.
The reference program's roundings to bfloat16 on the way (of `normed`, `queries`, `keys`, `weights`, `attended`, `normed_ffn` and `activated`) count: a program that leaves them out, or rounds other values in their place, can miss the bound.
Values may be sent and summed in bfloat16 or wider, within the bound.
No kernel may reach another device: no remote copies, remote signals or barrier semaphores. Data moves between devices by JAX's collectives and lax.ppermute only.
A program may use at most 192 MiB of HBM per device.

```python
import jax
import jax.numpy as jnp
from jax import lax

D = 2560
QH = 32
KVH = 8
HD = 80
FF = 6912
WINDOW = 4096
PAGE = 128
NEW = 128
REQ_DEV = 4
R0P = 16
R1P = 16
R2P = 8
ROOTS = 4
MIDS = 16
REQ = 64
SHARED_PAGES = 320
LP_DEV = 32
LEAF_PAGES = 512


def dealing(key):
    group_count = REQ // REQ_DEV
    base_key = jax.random.fold_in(key, 7)
    order_key, offset_key, deal_key, rank_key, page_key = jax.random.split(base_key, 5)
    owner_order = jax.random.permutation(order_key, group_count)
    owner_offset = jax.random.permutation(offset_key, group_count)
    slot_request = jax.random.permutation(deal_key, REQ)
    slot_ids = jnp.arange(REQ)
    slot_home = owner_order[(owner_offset[slot_ids // REQ_DEV] + slot_ids % REQ_DEV) % group_count]
    inverse_deal = jnp.argsort(slot_request)
    request_home = slot_home[inverse_deal]
    shuffled = jax.random.permutation(rank_key, REQ)
    sort_keys = request_home * REQ + shuffled
    ranked = jnp.argsort(jnp.argsort(sort_keys))
    local_rank = ranked - request_home * REQ_DEV
    page_keys = jax.random.split(page_key, group_count)
    page_order = jax.vmap(lambda one_key: jax.random.permutation(one_key, LP_DEV))(page_keys)
    within = local_rank[:, None] * R2P + jnp.arange(R2P)[None, :]
    leaf_ids = request_home[:, None] * LP_DEV + page_order[request_home[:, None], within]
    return (slot_request.astype(jnp.int32), leaf_ids.astype(jnp.int32))


def shared_split(key):
    owner_count = MIDS
    per_owner = SHARED_PAGES // owner_count
    perm_key, local_key = jax.random.split(jax.random.fold_in(key, 13))
    owner_perm = jax.random.permutation(perm_key, owner_count)
    local_keys = jax.random.split(local_key, owner_count)
    local_perm = jax.vmap(lambda one_key: jax.random.permutation(one_key, per_owner))(local_keys)
    entry = jnp.arange(SHARED_PAGES)
    owner = owner_perm[entry % owner_count]
    local = local_perm[owner, entry // owner_count]
    ordering = (owner * per_owner + local).astype(jnp.int32)
    return (ordering[:ROOTS * R0P].reshape(ROOTS, R0P), ordering[ROOTS * R0P:].reshape(MIDS, R1P))


def ragged(key, salt, entries, lowest, highest):
    value_key, chosen_key = jax.random.split(jax.random.fold_in(key, salt))
    values = jax.random.randint(value_key, (entries,), lowest, highest + 1)
    chosen = jax.random.randint(chosen_key, (), 0, entries)
    return jnp.where(jnp.arange(entries) == chosen, highest, values).astype(jnp.int32)


def page_draw(key, salt, page_count):
    normal_key = jax.random.fold_in(jax.random.fold_in(key, salt), 0)
    values = jnp.clip(jax.random.normal(normal_key, (page_count, KVH, 2, HD, PAGE), jnp.float32), -6.0, 6.0)
    factor = jnp.where(jnp.arange(2)[None, None, :, None, None] == 0, 3.0, 2.0)
    return values * factor


def draw_slot_request(key, part):
    return dealing(key)[0]


def draw_leaf_table(key, part):
    return dealing(key)[1]


def draw_root_table(key, part):
    return shared_split(key)[0]


def draw_mid_table(key, part):
    return shared_split(key)[1]


def draw_root_len(key, part):
    return ragged(key, 31, ROOTS, R0P * PAGE // 2, R0P * PAGE)


def draw_mid_len(key, part):
    return ragged(key, 37, MIDS, 1, R1P * PAGE)


def draw_leaf_len(key, part):
    return ragged(key, 41, REQ, 1, R2P * PAGE)


def draw_shared_pages(key, part):
    return page_draw(key, 43, SHARED_PAGES).astype(jnp.bfloat16)


def draw_leaf_pages(key, part):
    return page_draw(key, 47, LEAF_PAGES).astype(jnp.bfloat16)


def with_ends(values, stream_key, low, largest):
    shape = values.shape
    index_at = [jax.random.randint(jax.random.fold_in(stream_key, axis), (), 0, shape[axis]) for axis in range(len(shape))]
    values = values.at[tuple(index_at)].set(low)
    longest = shape.index(max(shape))
    index_at[longest] = (index_at[longest] + 1) % shape[longest]
    return values.at[tuple(index_at)].set(largest)


def level_of(own_key, dims, cuts, low, largest):
    factor_of, own = 1.0, jax.random.fold_in(own_key, 6)
    for dim, blocks in cuts:
        heights = jnp.exp(jax.random.uniform(jax.random.fold_in(own, dim), (blocks,), jnp.float32, low / len(cuts), largest / len(cuts)))
        factor_of = factor_of * jnp.repeat(heights, dims[dim] // blocks).reshape([-1 if axis == dim else 1 for axis in range(len(dims))])
    return factor_of


def scatter_about(key, extent, spread, limit, shards=(), held_as=jnp.bfloat16):
    values = jax.random.normal(key, extent, jnp.float32) * spread
    if len(shards) > 0:
        values = level_of(key, extent, shards, -0.22, 0.18) * values
    return jnp.clip(values, min=-limit, max=limit).astype(held_as)


def setup_inputs(seed: int = 0) -> dict:
    keys = jax.random.split(jax.random.key(seed), 22)
    hidden = scatter_about(keys[0], (NEW, REQ, D), 1.0, 6.0, ((1, 16),))
    gain_attn = jnp.clip(1.0 + 0.18 * jax.random.normal(keys[1], (D,), jnp.float32), 0.099609375, 1.8984375).astype(jnp.bfloat16)
    w_query = scatter_about(keys[2], (D, QH * HD), D ** -0.5, 0.125, ((1, 8),))
    w_key = scatter_about(keys[3], (D, KVH * HD), (D // 9) ** -0.5, 0.375, ((1, 8),))
    w_value = scatter_about(keys[4], (D, KVH * HD), (D // 4) ** -0.5, 0.25, ((1, 8),))
    w_out = scatter_about(keys[5], (QH * HD, D), (QH * HD) ** -0.5, 0.125, ((0, 8),))
    gain_ffn = jnp.clip(1.0 + 0.18 * jax.random.normal(keys[6], (D,), jnp.float32), 0.099609375, 1.8984375).astype(jnp.bfloat16)
    w_gate = scatter_about(keys[7], (D, FF), D ** -0.5, 0.125, ((1, 8),))
    w_up = scatter_about(keys[8], (D, FF), D ** -0.5, 0.125, ((1, 8),))
    w_down = scatter_about(keys[9], (FF, D), FF ** -0.5, 0.078125, ((0, 8),))
    shared_pages = draw_shared_pages(jax.random.fold_in(keys[21], 71), 0)
    leaf_pages = draw_leaf_pages(jax.random.fold_in(keys[21], 71), 0)
    root_table = draw_root_table(jax.random.fold_in(keys[21], 71), 0)
    mid_table = draw_mid_table(jax.random.fold_in(keys[21], 71), 0)
    leaf_table = draw_leaf_table(jax.random.fold_in(keys[21], 71), 0)
    root_len = draw_root_len(jax.random.fold_in(keys[21], 71), 0)
    mid_len = draw_mid_len(jax.random.fold_in(keys[21], 71), 0)
    leaf_len = draw_leaf_len(jax.random.fold_in(keys[21], 71), 0)
    mid_parent = with_ends(jax.random.randint(keys[18], (MIDS,), 0, ROOTS), jax.random.fold_in(keys[18], 1), 0, ROOTS - 1).astype(jnp.int32)
    leaf_parent = with_ends(jax.random.randint(keys[19], (REQ,), 0, MIDS), jax.random.fold_in(keys[19], 1), 0, MIDS - 1).astype(jnp.int32)
    slot_request = draw_slot_request(jax.random.fold_in(keys[21], 71), 0)
    return {"hidden": hidden, "gain_attn": gain_attn, "w_query": w_query, "w_key": w_key, "w_value": w_value, "w_out": w_out, "gain_ffn": gain_ffn, "w_gate": w_gate, "w_up": w_up, "w_down": w_down, "shared_pages": shared_pages, "leaf_pages": leaf_pages, "root_table": root_table, "mid_table": mid_table, "leaf_table": leaf_table, "root_len": root_len, "mid_len": mid_len, "leaf_len": leaf_len, "mid_parent": mid_parent, "leaf_parent": leaf_parent, "slot_request": slot_request}


masked_score = -1e+30
rope_base = 10000.0

def rms_norm(row_data, gain_vector):
    values = row_data.astype(jnp.float32)
    inverse_rms = lax.rsqrt(lax.optimization_barrier(jnp.mean(values * values, -1, keepdims=True)) + 1e-05)
    return (values * inverse_rms * gain_vector.astype(jnp.float32)).astype(jnp.bfloat16)

def rotate(vector, position):
    half_size = vector.shape[-1] // 2
    frequency = rope_base ** (-2.0 * jnp.arange(half_size, dtype=jnp.float32) / vector.shape[-1])
    angles = position.astype(jnp.float32)[..., None] * frequency
    cos_part = jnp.cos(angles)
    sin_part = jnp.sin(angles)
    first_half = vector[..., :half_size]
    second_half = vector[..., half_size:]
    return jnp.concatenate([first_half * cos_part - second_half * sin_part, second_half * cos_part + first_half * sin_part], -1)

def page_columns(pages):
    moved = jnp.moveaxis(pages, -5, -2)
    return moved.reshape(moved.shape[:-2] + (moved.shape[-2] * moved.shape[-1],))

def rounded_copy(values):
    return lax.optimization_barrier(values.astype(jnp.bfloat16)).astype(jnp.float32)

def reference(hidden, gain_attn, w_query, w_key, w_value, w_out, gain_ffn, w_gate, w_up, w_down, shared_pages, leaf_pages, root_table, mid_table, leaf_table, root_len, mid_len, leaf_len, mid_parent, leaf_parent, slot_request):
    new_rows, all_requests, model_width = hidden.shape
    group_size = QH // KVH
    requests = slot_request
    mid_nodes = leaf_parent[requests]
    root_nodes = mid_parent[mid_nodes]
    root_span = root_len[root_nodes]
    mid_span = mid_len[mid_nodes]
    leaf_span = leaf_len[requests]
    context = root_span + mid_span + leaf_span
    new_index = jnp.arange(new_rows, dtype=jnp.int32)
    query_pos = context[None, :] + new_index[:, None]
    normed = rms_norm(hidden, gain_attn).reshape(-1, model_width)
    query_proj = jnp.dot(normed, w_query, preferred_element_type=jnp.float32).reshape(new_rows, all_requests, QH, HD)
    queries = rotate(query_proj, query_pos[:, :, None]).astype(jnp.bfloat16)
    key_proj = jnp.dot(normed, w_key, preferred_element_type=jnp.float32).reshape(new_rows, all_requests, KVH, HD)
    new_keys = rotate(key_proj, query_pos[:, :, None]).astype(jnp.bfloat16)
    new_values = jnp.dot(normed, w_value, preferred_element_type=jnp.float32).astype(jnp.bfloat16).reshape(new_rows, all_requests, KVH, HD)
    root_steps = jnp.arange(R0P * PAGE, dtype=jnp.int32)
    mid_steps = jnp.arange(R1P * PAGE, dtype=jnp.int32)
    leaf_steps = jnp.arange(R2P * PAGE, dtype=jnp.int32)

    def one_slot(slot_index):
        root_pack = page_columns(shared_pages[root_table[root_nodes[slot_index]]])
        mid_pack = page_columns(shared_pages[mid_table[mid_nodes[slot_index]]])
        leaf_pack = page_columns(leaf_pages[leaf_table[requests[slot_index]]])
        fresh_pack = jnp.stack([jnp.transpose(new_keys[:, slot_index], (1, 2, 0)), jnp.transpose(new_values[:, slot_index], (1, 2, 0))], 1)
        key_pack = jnp.concatenate([root_pack, mid_pack, leaf_pack, fresh_pack], -1)
        key_pos = jnp.concatenate([root_steps, root_span[slot_index] + mid_steps, root_span[slot_index] + mid_span[slot_index] + leaf_steps, context[slot_index] + new_index])
        present = jnp.concatenate([root_steps < root_span[slot_index], mid_steps < mid_span[slot_index], leaf_steps < leaf_span[slot_index], new_index >= 0])
        query_rows = queries[:, slot_index].reshape(new_rows, KVH, group_size, HD).astype(jnp.float32)
        scores = jnp.einsum('nkge,ket->nkgt', query_rows, key_pack[:, 0].astype(jnp.float32)) * HD ** (-0.5)
        distance = query_pos[:, slot_index][:, None] - key_pos[None, :]
        allowed = (present[None, :] & (distance >= 0) & (distance < WINDOW))[:, None, None, :]
        scores = jnp.where(allowed, scores, masked_score)
        maximum = lax.optimization_barrier(jnp.max(scores, -1, keepdims=True))
        weights = jnp.where(allowed, jnp.exp(scores - maximum), 0.0)
        totals = lax.optimization_barrier(jnp.sum(weights, -1))
        weighted = jnp.einsum('nkgt,ket->nkge', rounded_copy(weights), key_pack[:, 1].astype(jnp.float32))
        return (weighted / totals[..., None]).reshape(new_rows, QH * HD).astype(jnp.bfloat16)
    attended = lax.map(one_slot, jnp.arange(all_requests, dtype=jnp.int32))
    attended = jnp.transpose(attended, (1, 0, 2)).reshape(-1, QH * HD)
    attn_proj = jnp.dot(attended, w_out, preferred_element_type=jnp.float32)
    resid = hidden.reshape(-1, model_width).astype(jnp.float32) + attn_proj
    normed_ffn = rms_norm(resid, gain_ffn)
    gate_rows = jnp.dot(normed_ffn, w_gate, preferred_element_type=jnp.float32)
    up_rows = jnp.dot(normed_ffn, w_up, preferred_element_type=jnp.float32)
    activated = (jax.nn.silu(gate_rows) * up_rows).astype(jnp.bfloat16)
    ffn_proj = jnp.dot(activated, w_down, preferred_element_type=jnp.float32)
    layer_out = resid + ffn_proj
    return layer_out.reshape(new_rows, all_requests, model_width)
```

```python
import jax
import jax.numpy as jnp
from jax import lax
from jax.sharding import PartitionSpec as P

QH = 32
KVH = 8
HD = 80
WINDOW = 4096


masked_score = -1e30
rope_base = 10000.0


def rms_norm(row_data, gain_vector):
    values = row_data.astype(jnp.float32)
    inverse_rms = lax.rsqrt(jnp.mean(values * values, -1, keepdims=True) + 1e-05)
    return (values * inverse_rms * gain_vector.astype(jnp.float32)).astype(jnp.bfloat16)


def rotate(vector, position):
    half_size = vector.shape[-1] // 2
    frequency = rope_base ** (-2.0 * jnp.arange(half_size, dtype=jnp.float32) / vector.shape[-1])
    angles = position.astype(jnp.float32)[..., None] * frequency
    cos_part = jnp.cos(angles)
    sin_part = jnp.sin(angles)
    first_half = vector[..., :half_size]
    second_half = vector[..., half_size:]
    return jnp.concatenate(
        [
            first_half * cos_part - second_half * sin_part,
            second_half * cos_part + first_half * sin_part,
        ],
        -1,
    )


def page_columns(pages):
    moved = jnp.moveaxis(pages, -5, -2)
    return moved.reshape(moved.shape[:-2] + (moved.shape[-2] * moved.shape[-1],))


def attend(queries, key_pack, key_pos, present, query_pos):
    scores = jnp.einsum(
        "nbkge,bket->nbkgt", queries, key_pack[:, :, 0], preferred_element_type=jnp.float32
    ) * queries.shape[-1] ** (-0.5)
    distance = query_pos[:, :, None] - key_pos[None, :, :]
    allowed = (present[None, :, :] & (distance >= 0) & (distance < WINDOW))[:, :, None, None, :]
    scores = jnp.where(allowed, scores, masked_score)
    maximum = jnp.max(scores, -1)
    weights = jnp.where(allowed, jnp.exp(scores - maximum[..., None]), 0.0)
    totals = jnp.sum(weights, -1)
    weighted = jnp.einsum(
        "nbkgt,bket->nbkge",
        weights.astype(jnp.bfloat16),
        key_pack[:, :, 1],
        preferred_element_type=jnp.float32,
    )
    return (weighted, maximum, totals)


def merge_parts(first, second):
    maximum = jnp.maximum(first[1], second[1])
    first_scale = jnp.exp(first[1] - maximum)
    second_scale = jnp.exp(second[1] - maximum)
    return (
        first[0] * first_scale[..., None] + second[0] * second_scale[..., None],
        maximum,
        first[2] * first_scale + second[2] * second_scale,
    )


def spans(request_ids, root_len, mid_len, leaf_len, mid_parent, leaf_parent):
    mid_nodes = leaf_parent[request_ids]
    root_nodes = mid_parent[mid_nodes]
    return (root_nodes, mid_nodes, root_len[root_nodes], mid_len[mid_nodes], leaf_len[request_ids])


def shards(
    hidden,
    gain_attn,
    w_query,
    w_key,
    w_value,
    w_out,
    gain_ffn,
    w_gate,
    w_up,
    w_down,
    shared_pages,
    leaf_pages,
    root_table,
    mid_table,
    leaf_table,
    root_len,
    mid_len,
    leaf_len,
    mid_parent,
    leaf_parent,
    slot_request,
):
    new_rows, local_reqs, model_width = hidden.shape
    seq_count = lax.axis_size("seq")
    seq_index = lax.axis_index("seq")
    kv_local = leaf_pages.shape[1]
    group_size = QH // KVH
    pages_here = leaf_pages.shape[0]
    slot_ids = seq_index * local_reqs + jnp.arange(local_reqs, dtype=jnp.int32)
    requests = slot_request[slot_ids]
    root_nodes, mid_nodes, root_span, mid_span, leaf_span = spans(
        requests, root_len, mid_len, leaf_len, mid_parent, leaf_parent
    )
    context = root_span + mid_span + leaf_span
    new_index = jnp.arange(new_rows, dtype=jnp.int32)
    query_pos = context[None, :] + new_index[:, None]
    all_slots = slot_request.reshape(seq_count, local_reqs)
    page_store = lax.all_gather(shared_pages, "seq", axis=0, tiled=True)
    root_index = root_table[root_nodes]
    mid_index = mid_table[mid_nodes]
    normed = rms_norm(hidden, gain_attn).reshape(-1, model_width)
    query_proj = jnp.dot(normed, w_query, preferred_element_type=jnp.float32).reshape(
        new_rows, local_reqs, -1, HD
    )
    queries = (
        rotate(query_proj, query_pos[:, :, None])
        .astype(jnp.bfloat16)
        .reshape(new_rows, local_reqs, kv_local, group_size, HD)
    )
    key_proj = jnp.dot(normed, w_key, preferred_element_type=jnp.float32).reshape(
        new_rows, local_reqs, kv_local, HD
    )
    new_keys = rotate(key_proj, query_pos[:, :, None]).astype(jnp.bfloat16)
    new_values = (
        jnp.dot(normed, w_value, preferred_element_type=jnp.float32)
        .astype(jnp.bfloat16)
        .reshape(new_rows, local_reqs, kv_local, HD)
    )
    home_of = leaf_table[:, 0] // pages_here
    own_homes = home_of[requests]
    sender_match = home_of[all_slots] == seq_index
    sender_pick = jnp.argmax(sender_match, 1)
    sender_have = jnp.any(sender_match, 1)
    picked_request = jnp.take_along_axis(all_slots, sender_pick[:, None], 1)[:, 0]
    page_ids = jnp.where(
        sender_have[:, None], leaf_table[picked_request] - seq_index * pages_here, 0
    )
    leaf_steps = jnp.arange(leaf_table.shape[1] * leaf_pages.shape[-1], dtype=jnp.int32)
    fresh_pack = jnp.stack(
        [jnp.transpose(new_keys, (1, 2, 3, 0)), jnp.transpose(new_values, (1, 2, 3, 0))], 2
    )
    fresh_part = attend(
        queries,
        fresh_pack,
        context[:, None] + new_index[None, :],
        jnp.ones((local_reqs, new_rows), bool),
        query_pos,
    )
    outgoing = jnp.where(
        sender_have[:, None, None, None, None, None], jnp.take(leaf_pages, page_ids, axis=0), 0
    )
    arrived = lax.all_to_all(outgoing, "seq", split_axis=0, concat_axis=0, tiled=True)
    leaf_pack = page_columns(jnp.take(arrived, own_homes, axis=0))
    leaf_pos = (root_span + mid_span)[:, None] + leaf_steps[None, :]
    leaf_part = attend(
        queries, leaf_pack, leaf_pos, leaf_steps[None, :] < leaf_span[:, None], query_pos
    )
    root_pack = page_columns(jnp.take(page_store, root_index, axis=0))
    root_steps = jnp.arange(root_pack.shape[-1], dtype=jnp.int32)
    root_part = attend(
        queries,
        root_pack,
        root_steps[None, :] + 0 * root_span[:, None],
        root_steps[None, :] < root_span[:, None],
        query_pos,
    )
    mid_pack = page_columns(jnp.take(page_store, mid_index, axis=0))
    mid_steps = jnp.arange(mid_pack.shape[-1], dtype=jnp.int32)
    mid_part = attend(
        queries,
        mid_pack,
        root_span[:, None] + mid_steps[None, :],
        mid_steps[None, :] < mid_span[:, None],
        query_pos,
    )
    combined = merge_parts(merge_parts(root_part, mid_part), merge_parts(leaf_part, fresh_part))
    attended = (
        (combined[0] / combined[2][..., None])
        .astype(jnp.bfloat16)
        .reshape(new_rows * local_reqs, -1)
    )
    tp_count = lax.axis_size("tp")
    own_count = new_rows // tp_count
    attn_proj = lax.psum_scatter(
        jnp.dot(attended, w_out, preferred_element_type=jnp.float32),
        "tp",
        scatter_dimension=0,
        tiled=True,
    ).reshape(own_count, local_reqs, model_width)
    own_hidden = lax.dynamic_slice_in_dim(hidden, lax.axis_index("tp") * own_count, own_count, 0)
    resid = own_hidden.astype(jnp.float32) + attn_proj
    normed_own = rms_norm(resid, gain_ffn).reshape(-1, model_width)
    normed_ffn = lax.all_gather(normed_own, "tp", axis=0, tiled=True)
    gate_rows = jnp.dot(normed_ffn, w_gate, preferred_element_type=jnp.float32)
    up_rows = jnp.dot(normed_ffn, w_up, preferred_element_type=jnp.float32)
    activated = (jax.nn.silu(gate_rows) * up_rows).astype(jnp.bfloat16)
    ffn_proj = lax.psum_scatter(
        jnp.dot(activated, w_down, preferred_element_type=jnp.float32),
        "tp",
        scatter_dimension=0,
        tiled=True,
    ).reshape(own_count, local_reqs, model_width)
    return resid + ffn_proj


def solution(mesh):
    return jax.shard_map(
        shards,
        mesh=mesh,
        in_specs=(
            P(None, "seq", None),
            P(),
            P(None, "tp"),
            P(None, "tp"),
            P(None, "tp"),
            P("tp", None),
            P(),
            P(None, "tp"),
            P(None, "tp"),
            P("tp", None),
            P("seq", "tp", None, None, None),
            P("seq", "tp", None, None, None),
            P(),
            P(),
            P(),
            P(),
            P(),
            P(),
            P(),
            P(),
            P(),
        ),
        out_specs=P("tp", "seq", None),
        check_vma=False,
    )
```

```python
import jax
import jax.numpy as jnp
from jax import lax
from jax.sharding import PartitionSpec as P
from jax.experimental import pallas as pl
from jax.experimental.pallas import tpu as pltpu

QH = 32
KVH = 8
HD = 80
WINDOW = 4096


masked_score = -1e30
rope_base = 10000.0


def rms_norm(row_data, gain_vector):
    values = row_data.astype(jnp.float32)
    inverse_rms = lax.rsqrt(jnp.mean(values * values, -1, keepdims=True) + 1e-05)
    return (values * inverse_rms * gain_vector.astype(jnp.float32)).astype(jnp.bfloat16)


def rotate(vector, position):
    half_size = vector.shape[-1] // 2
    frequency = rope_base ** (-2.0 * jnp.arange(half_size, dtype=jnp.float32) / vector.shape[-1])
    angles = position.astype(jnp.float32)[..., None] * frequency
    cos_part = jnp.cos(angles)
    sin_part = jnp.sin(angles)
    first_half = vector[..., :half_size]
    second_half = vector[..., half_size:]
    return jnp.concatenate(
        [
            first_half * cos_part - second_half * sin_part,
            second_half * cos_part + first_half * sin_part,
        ],
        -1,
    )


def page_columns(pages):
    moved = jnp.moveaxis(pages, -5, -2)
    return moved.reshape(moved.shape[:-2] + (moved.shape[-2] * moved.shape[-1],))


def attend(queries, key_pack, key_pos, present, query_pos):
    scores = jnp.einsum(
        "nbkge,bket->nbkgt", queries, key_pack[:, :, 0], preferred_element_type=jnp.float32
    ) * queries.shape[-1] ** (-0.5)
    distance = query_pos[:, :, None] - key_pos[None, :, :]
    allowed = (present[None, :, :] & (distance >= 0) & (distance < WINDOW))[:, :, None, None, :]
    scores = jnp.where(allowed, scores, masked_score)
    maximum = jnp.max(scores, -1)
    weights = jnp.where(allowed, jnp.exp(scores - maximum[..., None]), 0.0)
    totals = jnp.sum(weights, -1)
    weighted = jnp.einsum(
        "nbkgt,bket->nbkge",
        weights.astype(jnp.bfloat16),
        key_pack[:, :, 1],
        preferred_element_type=jnp.float32,
    )
    return (weighted, maximum, totals)


def merge_parts(first, second):
    maximum = jnp.maximum(first[1], second[1])
    first_scale = jnp.exp(first[1] - maximum)
    second_scale = jnp.exp(second[1] - maximum)
    return (
        first[0] * first_scale[..., None] + second[0] * second_scale[..., None],
        maximum,
        first[2] * first_scale + second[2] * second_scale,
    )


ROOT_PAGES = 16
MID_PAGES = 16
LEAF_SLOTS = 8


def paged_kernel(tbl, meta, q_ref, fresh_ref, shared_hbm, leaf_hbm, out_ref, kv, sc, sem):
    i = pl.program_id(0)
    steps = pl.num_programs(0)
    slot = i % 2
    shared_count = ROOT_PAGES + MID_PAGES
    page_count = shared_count + LEAF_SLOTS

    def start_request(j, into):
        def shared_body(p, carry):
            pltpu.make_async_copy(shared_hbm.at[tbl[j, p]], kv.at[into, p], sem.at[into]).start()
            return carry

        def leaf_body(p, carry):
            pltpu.make_async_copy(leaf_hbm.at[tbl[j, p]], kv.at[into, p], sem.at[into]).start()
            return carry

        lax.fori_loop(0, shared_count, shared_body, 0)
        lax.fori_loop(shared_count, page_count, leaf_body, 0)

    @pl.when(i == 0)
    def _():
        start_request(0, 0)

    @pl.when(i + 1 < steps)
    def _():
        start_request(i + 1, 1 - slot)

    def wait_body(p, carry):
        pltpu.make_async_copy(shared_hbm.at[0], kv.at[slot, p], sem.at[slot]).wait()
        return carry

    lax.fori_loop(0, page_count, wait_body, 0)

    root_span = meta[i, 0]
    mid_span = meta[i, 1]
    leaf_span = meta[i, 2]
    context = meta[i, 3]
    q = q_ref[0]
    rows, width = q.shape[0], kv.shape[-1]
    query_pos = context + (lax.broadcasted_iota(jnp.int32, (rows, 1), 0) % width)
    lanes = lax.broadcasted_iota(jnp.int32, (1, width), 1)
    scale = HD ** (-0.5)

    def scores_of(keys, key_pos, present):
        s = jnp.dot(q, keys, preferred_element_type=jnp.float32) * scale
        distance = query_pos - key_pos
        allowed = present & (distance >= 0) & (distance < WINDOW)
        return jnp.where(allowed, s, masked_score)

    def geometry(c):
        in_root = c < ROOT_PAGES
        in_mid = c < shared_count
        first = jnp.where(
            in_root, c * width, jnp.where(in_mid, (c - ROOT_PAGES) * width, (c - shared_count) * width)
        )
        base = jnp.where(in_root, 0, jnp.where(in_mid, root_span, root_span + mid_span))
        limit = jnp.where(in_root, root_span, jnp.where(in_mid, mid_span, leaf_span))
        return first, base, limit

    fresh_scores = scores_of(fresh_ref[0, 0], context + lanes, lanes >= 0)
    sc[page_count] = fresh_scores
    maximum = jnp.max(fresh_scores, -1, keepdims=True)

    def max_body(c, running):
        first, base, limit = geometry(c)

        def live():
            steps_in = first + lanes
            s = scores_of(kv[slot, c, 0], base + steps_in, steps_in < limit)
            sc[c] = s
            return jnp.maximum(running, jnp.max(s, -1, keepdims=True))

        return lax.cond(first < limit, live, lambda: running)

    maximum = lax.fori_loop(0, page_count, max_body, maximum)

    def weigh(s, values, totals, acc):
        w = jnp.exp(s - maximum)
        totals = totals + jnp.sum(w, -1, keepdims=True)
        acc = acc + lax.dot_general(
            w.astype(jnp.bfloat16), values, (((1,), (1,)), ((), ())), preferred_element_type=jnp.float32
        )
        return totals, acc

    carry = weigh(
        sc[page_count],
        fresh_ref[0, 1],
        jnp.zeros((rows, 1), jnp.float32),
        jnp.zeros((rows, q.shape[1]), jnp.float32),
    )

    def sum_body(c, carry):
        first, base, limit = geometry(c)
        return lax.cond(
            first < limit, lambda: weigh(sc[c], kv[slot, c, 1], *carry), lambda: carry
        )

    totals, acc = lax.fori_loop(0, page_count, sum_body, carry)
    out_ref[0] = (acc / totals).astype(out_ref.dtype)


def paged_attention(tbl, meta, queries, fresh, shared_store, leaf_store):
    reqs, rows, head = queries.shape
    page_shape = shared_store.shape[1:]
    pages = tbl.shape[1]
    keys_total = (pages + 1) * page_shape[-1]
    grid_spec = pltpu.PrefetchScalarGridSpec(
        num_scalar_prefetch=2,
        grid=(reqs,),
        in_specs=[
            pl.BlockSpec((1, rows, head), lambda i, t, m: (i, 0, 0)),
            pl.BlockSpec((1,) + page_shape, lambda i, t, m: (i, 0, 0, 0)),
            pl.BlockSpec(memory_space=pl.ANY),
            pl.BlockSpec(memory_space=pl.ANY),
        ],
        out_specs=pl.BlockSpec((1, rows, head), lambda i, t, m: (i, 0, 0)),
        scratch_shapes=[
            pltpu.VMEM((2, pages) + page_shape, shared_store.dtype),
            pltpu.VMEM((pages + 1, rows, page_shape[-1]), jnp.float32),
            pltpu.SemaphoreType.DMA((2,)),
        ],
    )
    return pl.pallas_call(
        paged_kernel,
        grid_spec=grid_spec,
        out_shape=jax.ShapeDtypeStruct((reqs, rows, head), jnp.bfloat16),
        compiler_params=pltpu.CompilerParams(dimension_semantics=("arbitrary",)),
        cost_estimate=pl.CostEstimate(
            flops=4 * reqs * rows * keys_total * head,
            transcendentals=reqs * rows * keys_total,
            bytes_accessed=reqs * (pages + 1) * 2 * head * page_shape[-1] * 2,
        ),
    )(tbl, meta, queries, fresh, shared_store, leaf_store)


def spans(request_ids, root_len, mid_len, leaf_len, mid_parent, leaf_parent):
    mid_nodes = leaf_parent[request_ids]
    root_nodes = mid_parent[mid_nodes]
    return (root_nodes, mid_nodes, root_len[root_nodes], mid_len[mid_nodes], leaf_len[request_ids])


def shards(
    hidden,
    gain_attn,
    w_query,
    w_key,
    w_value,
    w_out,
    gain_ffn,
    w_gate,
    w_up,
    w_down,
    shared_pages,
    leaf_pages,
    root_table,
    mid_table,
    leaf_table,
    root_len,
    mid_len,
    leaf_len,
    mid_parent,
    leaf_parent,
    slot_request,
):
    new_rows, local_reqs, model_width = hidden.shape
    seq_count = lax.axis_size("seq")
    seq_index = lax.axis_index("seq")
    kv_local = leaf_pages.shape[1]
    group_size = QH // KVH
    pages_here = leaf_pages.shape[0]
    slot_ids = seq_index * local_reqs + jnp.arange(local_reqs, dtype=jnp.int32)
    requests = slot_request[slot_ids]
    root_nodes, mid_nodes, root_span, mid_span, leaf_span = spans(
        requests, root_len, mid_len, leaf_len, mid_parent, leaf_parent
    )
    context = root_span + mid_span + leaf_span
    new_index = jnp.arange(new_rows, dtype=jnp.int32)
    query_pos = context[None, :] + new_index[:, None]
    all_slots = slot_request.reshape(seq_count, local_reqs)
    page_store = lax.all_gather(shared_pages, "seq", axis=0, tiled=True)
    root_index = root_table[root_nodes]
    mid_index = mid_table[mid_nodes]
    normed = rms_norm(hidden, gain_attn).reshape(-1, model_width)
    query_proj = jnp.dot(normed, w_query, preferred_element_type=jnp.float32).reshape(
        new_rows, local_reqs, -1, HD
    )
    queries = (
        rotate(query_proj, query_pos[:, :, None])
        .astype(jnp.bfloat16)
        .reshape(new_rows, local_reqs, kv_local, group_size, HD)
    )
    key_proj = jnp.dot(normed, w_key, preferred_element_type=jnp.float32).reshape(
        new_rows, local_reqs, kv_local, HD
    )
    new_keys = rotate(key_proj, query_pos[:, :, None]).astype(jnp.bfloat16)
    new_values = (
        jnp.dot(normed, w_value, preferred_element_type=jnp.float32)
        .astype(jnp.bfloat16)
        .reshape(new_rows, local_reqs, kv_local, HD)
    )
    home_of = leaf_table[:, 0] // pages_here
    own_homes = home_of[requests]
    sender_match = home_of[all_slots] == seq_index
    sender_pick = jnp.argmax(sender_match, 1)
    sender_have = jnp.any(sender_match, 1)
    picked_request = jnp.take_along_axis(all_slots, sender_pick[:, None], 1)[:, 0]
    page_ids = jnp.where(
        sender_have[:, None], leaf_table[picked_request] - seq_index * pages_here, 0
    )
    leaf_slots = leaf_table.shape[1]
    outgoing = jnp.where(
        sender_have[:, None, None, None, None, None], jnp.take(leaf_pages, page_ids, axis=0), 0
    )
    arrived = lax.all_to_all(outgoing, "seq", split_axis=0, concat_axis=0, tiled=True)
    page_shape = arrived.shape[-3:]
    leaf_store = arrived.reshape((-1,) + page_shape)
    shared_store = page_store.reshape((-1,) + page_shape)
    tbl = jnp.concatenate(
        [
            root_index,
            mid_index,
            own_homes[:, None] * leaf_slots + jnp.arange(leaf_slots, dtype=jnp.int32)[None, :],
        ],
        1,
    ).astype(jnp.int32)
    meta = jnp.stack([root_span, mid_span, leaf_span, context], 1).astype(jnp.int32)
    fresh_pack = jnp.stack(
        [jnp.transpose(new_keys[:, :, 0], (1, 2, 0)), jnp.transpose(new_values[:, :, 0], (1, 2, 0))], 1
    )
    query_rows = jnp.transpose(queries[:, :, 0], (1, 2, 0, 3)).reshape(local_reqs, -1, HD)
    attended = paged_attention(tbl, meta, query_rows, fresh_pack, shared_store, leaf_store)
    attended = (
        jnp.transpose(attended.reshape(local_reqs, group_size, new_rows, HD), (2, 0, 1, 3))
        .reshape(new_rows * local_reqs, -1)
    )
    tp_count = lax.axis_size("tp")
    own_count = new_rows // tp_count
    attn_proj = lax.psum_scatter(
        jnp.dot(attended, w_out, preferred_element_type=jnp.float32),
        "tp",
        scatter_dimension=0,
        tiled=True,
    ).reshape(own_count, local_reqs, model_width)
    own_hidden = lax.dynamic_slice_in_dim(hidden, lax.axis_index("tp") * own_count, own_count, 0)
    resid = own_hidden.astype(jnp.float32) + attn_proj
    normed_own = rms_norm(resid, gain_ffn).reshape(-1, model_width)
    normed_ffn = lax.all_gather(normed_own, "tp", axis=0, tiled=True)
    gate_rows = jnp.dot(normed_ffn, w_gate, preferred_element_type=jnp.float32)
    up_rows = jnp.dot(normed_ffn, w_up, preferred_element_type=jnp.float32)
    activated = (jax.nn.silu(gate_rows) * up_rows).astype(jnp.bfloat16)
    ffn_proj = lax.psum_scatter(
        jnp.dot(activated, w_down, preferred_element_type=jnp.float32),
        "tp",
        scatter_dimension=0,
        tiled=True,
    ).reshape(own_count, local_reqs, model_width)
    return resid + ffn_proj


def solution(mesh):
    return jax.shard_map(
        shards,
        mesh=mesh,
        in_specs=(
            P(None, "seq", None),
            P(),
            P(None, "tp"),
            P(None, "tp"),
            P(None, "tp"),
            P("tp", None),
            P(),
            P(None, "tp"),
            P(None, "tp"),
            P("tp", None),
            P("seq", "tp", None, None, None),
            P("seq", "tp", None, None, None),
            P(),
            P(),
            P(),
            P(),
            P(),
            P(),
            P(),
            P(),
            P(),
        ),
        out_specs=P("tp", "seq", None),
        check_vma=False,
    )
```

```python
import jax
import jax.numpy as jnp
from jax import lax
from jax.sharding import PartitionSpec as P
from jax.experimental import pallas as pl
from jax.experimental.pallas import tpu as pltpu

QH = 32
KVH = 8
HD = 80
WINDOW = 4096


masked_score = -1e30
rope_base = 10000.0


def rms_norm(row_data, gain_vector):
    values = row_data.astype(jnp.float32)
    inverse_rms = lax.rsqrt(jnp.mean(values * values, -1, keepdims=True) + 1e-05)
    return (values * inverse_rms * gain_vector.astype(jnp.float32)).astype(jnp.bfloat16)


def rotate(vector, position):
    half_size = vector.shape[-1] // 2
    frequency = rope_base ** (-2.0 * jnp.arange(half_size, dtype=jnp.float32) / vector.shape[-1])
    angles = position.astype(jnp.float32)[..., None] * frequency
    cos_part = jnp.cos(angles)
    sin_part = jnp.sin(angles)
    first_half = vector[..., :half_size]
    second_half = vector[..., half_size:]
    return jnp.concatenate(
        [
            first_half * cos_part - second_half * sin_part,
            second_half * cos_part + first_half * sin_part,
        ],
        -1,
    )


def page_columns(pages):
    moved = jnp.moveaxis(pages, -5, -2)
    return moved.reshape(moved.shape[:-2] + (moved.shape[-2] * moved.shape[-1],))


def attend(queries, key_pack, key_pos, present, query_pos):
    scores = jnp.einsum(
        "nbkge,bket->nbkgt", queries, key_pack[:, :, 0], preferred_element_type=jnp.float32
    ) * queries.shape[-1] ** (-0.5)
    distance = query_pos[:, :, None] - key_pos[None, :, :]
    allowed = (present[None, :, :] & (distance >= 0) & (distance < WINDOW))[:, :, None, None, :]
    scores = jnp.where(allowed, scores, masked_score)
    maximum = jnp.max(scores, -1)
    weights = jnp.where(allowed, jnp.exp(scores - maximum[..., None]), 0.0)
    totals = jnp.sum(weights, -1)
    weighted = jnp.einsum(
        "nbkgt,bket->nbkge",
        weights.astype(jnp.bfloat16),
        key_pack[:, :, 1],
        preferred_element_type=jnp.float32,
    )
    return (weighted, maximum, totals)


def merge_parts(first, second):
    maximum = jnp.maximum(first[1], second[1])
    first_scale = jnp.exp(first[1] - maximum)
    second_scale = jnp.exp(second[1] - maximum)
    return (
        first[0] * first_scale[..., None] + second[0] * second_scale[..., None],
        maximum,
        first[2] * first_scale + second[2] * second_scale,
    )


ROOT_PAGES = 16
MID_PAGES = 16
LEAF_SLOTS = 8


def paged_kernel(tbl, meta, q_ref, fresh_ref, shared_hbm, leaf_hbm, out_ref, kv, sc, sem):
    i = pl.program_id(0)
    steps = pl.num_programs(0)
    slot = i % 2
    shared_count = ROOT_PAGES + MID_PAGES
    page_count = shared_count + LEAF_SLOTS

    def start_request(j, into):
        def shared_body(p, carry):
            pltpu.make_async_copy(shared_hbm.at[tbl[j, p]], kv.at[into, p], sem.at[into]).start()
            return carry

        def leaf_body(p, carry):
            pltpu.make_async_copy(leaf_hbm.at[tbl[j, p]], kv.at[into, p], sem.at[into]).start()
            return carry

        lax.fori_loop(0, shared_count, shared_body, 0)
        lax.fori_loop(shared_count, page_count, leaf_body, 0)

    @pl.when(i == 0)
    def _():
        start_request(0, 0)

    @pl.when(i + 1 < steps)
    def _():
        start_request(i + 1, 1 - slot)

    def wait_body(p, carry):
        pltpu.make_async_copy(shared_hbm.at[0], kv.at[slot, p], sem.at[slot]).wait()
        return carry

    lax.fori_loop(0, page_count, wait_body, 0)

    root_span = meta[i, 0]
    mid_span = meta[i, 1]
    leaf_span = meta[i, 2]
    context = meta[i, 3]
    q = q_ref[0]
    rows, width = q.shape[0], kv.shape[-1]
    query_pos = context + (lax.broadcasted_iota(jnp.int32, (rows, 1), 0) % width)
    lanes = lax.broadcasted_iota(jnp.int32, (1, width), 1)
    scale = HD ** (-0.5)

    def scores_of(keys, key_pos, present):
        s = jnp.dot(q, keys, preferred_element_type=jnp.float32) * scale
        distance = query_pos - key_pos
        allowed = present & (distance >= 0) & (distance < WINDOW)
        return jnp.where(allowed, s, masked_score)

    def geometry(c):
        in_root = c < ROOT_PAGES
        in_mid = c < shared_count
        first = jnp.where(
            in_root, c * width, jnp.where(in_mid, (c - ROOT_PAGES) * width, (c - shared_count) * width)
        )
        base = jnp.where(in_root, 0, jnp.where(in_mid, root_span, root_span + mid_span))
        limit = jnp.where(in_root, root_span, jnp.where(in_mid, mid_span, leaf_span))
        return first, base, limit

    fresh_scores = scores_of(fresh_ref[0, 0], context + lanes, lanes >= 0)
    sc[page_count] = fresh_scores
    maximum = jnp.max(fresh_scores, -1, keepdims=True)

    def max_body(c, running):
        first, base, limit = geometry(c)

        def live():
            steps_in = first + lanes
            s = scores_of(kv[slot, c, 0], base + steps_in, steps_in < limit)
            sc[c] = s
            return jnp.maximum(running, jnp.max(s, -1, keepdims=True))

        return lax.cond(first < limit, live, lambda: running)

    maximum = lax.fori_loop(0, page_count, max_body, maximum)

    def weigh(s, values, totals, acc):
        w = jnp.exp(s - maximum)
        totals = totals + jnp.sum(w, -1, keepdims=True)
        acc = acc + lax.dot_general(
            w.astype(jnp.bfloat16), values, (((1,), (1,)), ((), ())), preferred_element_type=jnp.float32
        )
        return totals, acc

    carry = weigh(
        sc[page_count],
        fresh_ref[0, 1],
        jnp.zeros((rows, 1), jnp.float32),
        jnp.zeros((rows, q.shape[1]), jnp.float32),
    )

    def sum_body(c, carry):
        first, base, limit = geometry(c)
        return lax.cond(
            first < limit, lambda: weigh(sc[c], kv[slot, c, 1], *carry), lambda: carry
        )

    totals, acc = lax.fori_loop(0, page_count, sum_body, carry)
    out_ref[0] = (acc / totals).astype(out_ref.dtype)


def paged_attention(tbl, meta, queries, fresh, shared_store, leaf_store):
    reqs, rows, head = queries.shape
    page_shape = shared_store.shape[1:]
    pages = tbl.shape[1]
    keys_total = (pages + 1) * page_shape[-1]
    grid_spec = pltpu.PrefetchScalarGridSpec(
        num_scalar_prefetch=2,
        grid=(reqs,),
        in_specs=[
            pl.BlockSpec((1, rows, head), lambda i, t, m: (i, 0, 0)),
            pl.BlockSpec((1,) + page_shape, lambda i, t, m: (i, 0, 0, 0)),
            pl.BlockSpec(memory_space=pl.ANY),
            pl.BlockSpec(memory_space=pl.ANY),
        ],
        out_specs=pl.BlockSpec((1, rows, head), lambda i, t, m: (i, 0, 0)),
        scratch_shapes=[
            pltpu.VMEM((2, pages) + page_shape, shared_store.dtype),
            pltpu.VMEM((pages + 1, rows, page_shape[-1]), jnp.float32),
            pltpu.SemaphoreType.DMA((2,)),
        ],
    )
    return pl.pallas_call(
        paged_kernel,
        grid_spec=grid_spec,
        out_shape=jax.ShapeDtypeStruct((reqs, rows, head), jnp.bfloat16),
        compiler_params=pltpu.CompilerParams(dimension_semantics=("arbitrary",)),
        cost_estimate=pl.CostEstimate(
            flops=4 * reqs * rows * keys_total * head,
            transcendentals=reqs * rows * keys_total,
            bytes_accessed=reqs * (pages + 1) * 2 * head * page_shape[-1] * 2,
        ),
    )(tbl, meta, queries, fresh, shared_store, leaf_store)


def spans(request_ids, root_len, mid_len, leaf_len, mid_parent, leaf_parent):
    mid_nodes = leaf_parent[request_ids]
    root_nodes = mid_parent[mid_nodes]
    return (root_nodes, mid_nodes, root_len[root_nodes], mid_len[mid_nodes], leaf_len[request_ids])


def shards(
    hidden,
    gain_attn,
    w_query,
    w_key,
    w_value,
    w_out,
    gain_ffn,
    w_gate,
    w_up,
    w_down,
    shared_pages,
    leaf_pages,
    root_table,
    mid_table,
    leaf_table,
    root_len,
    mid_len,
    leaf_len,
    mid_parent,
    leaf_parent,
    slot_request,
):
    new_rows, local_reqs, model_width = hidden.shape
    seq_count = lax.axis_size("seq")
    seq_index = lax.axis_index("seq")
    kv_local = leaf_pages.shape[1]
    group_size = QH // KVH
    pages_here = leaf_pages.shape[0]
    slot_ids = seq_index * local_reqs + jnp.arange(local_reqs, dtype=jnp.int32)
    requests = slot_request[slot_ids]
    root_nodes, mid_nodes, root_span, mid_span, leaf_span = spans(
        requests, root_len, mid_len, leaf_len, mid_parent, leaf_parent
    )
    context = root_span + mid_span + leaf_span
    new_index = jnp.arange(new_rows, dtype=jnp.int32)
    query_pos = context[None, :] + new_index[:, None]
    all_slots = slot_request.reshape(seq_count, local_reqs)
    page_store = lax.all_gather(shared_pages, "seq", axis=0, tiled=True)
    root_index = root_table[root_nodes]
    mid_index = mid_table[mid_nodes]
    normed = rms_norm(hidden, gain_attn).reshape(-1, model_width)
    query_proj = jnp.dot(normed, w_query, preferred_element_type=jnp.float32).reshape(
        new_rows, local_reqs, -1, HD
    )
    queries = (
        rotate(query_proj, query_pos[:, :, None])
        .astype(jnp.bfloat16)
        .reshape(new_rows, local_reqs, kv_local, group_size, HD)
    )
    key_proj = jnp.dot(normed, w_key, preferred_element_type=jnp.float32).reshape(
        new_rows, local_reqs, kv_local, HD
    )
    new_keys = rotate(key_proj, query_pos[:, :, None]).astype(jnp.bfloat16)
    new_values = (
        jnp.dot(normed, w_value, preferred_element_type=jnp.float32)
        .astype(jnp.bfloat16)
        .reshape(new_rows, local_reqs, kv_local, HD)
    )
    home_of = leaf_table[:, 0] // pages_here
    own_homes = home_of[requests]
    sender_match = home_of[all_slots] == seq_index
    sender_pick = jnp.argmax(sender_match, 1)
    sender_have = jnp.any(sender_match, 1)
    picked_request = jnp.take_along_axis(all_slots, sender_pick[:, None], 1)[:, 0]
    page_ids = jnp.where(
        sender_have[:, None], leaf_table[picked_request] - seq_index * pages_here, 0
    )
    leaf_slots = leaf_table.shape[1]
    outgoing = jnp.where(
        sender_have[:, None, None, None, None, None], jnp.take(leaf_pages, page_ids, axis=0), 0
    )
    arrived = lax.all_to_all(outgoing, "seq", split_axis=0, concat_axis=0, tiled=True)
    page_shape = arrived.shape[-3:]
    leaf_store = arrived.reshape((-1,) + page_shape)
    shared_store = page_store.reshape((-1,) + page_shape)
    tbl = jnp.concatenate(
        [
            root_index,
            mid_index,
            own_homes[:, None] * leaf_slots + jnp.arange(leaf_slots, dtype=jnp.int32)[None, :],
        ],
        1,
    ).astype(jnp.int32)
    meta = jnp.stack([root_span, mid_span, leaf_span, context], 1).astype(jnp.int32)
    fresh_pack = jnp.stack(
        [jnp.transpose(new_keys[:, :, 0], (1, 2, 0)), jnp.transpose(new_values[:, :, 0], (1, 2, 0))], 1
    )
    query_rows = jnp.transpose(queries[:, :, 0], (1, 2, 0, 3)).reshape(local_reqs, -1, HD)
    attended = paged_attention(tbl, meta, query_rows, fresh_pack, shared_store, leaf_store)
    attended = (
        jnp.transpose(attended.reshape(local_reqs, group_size, new_rows, HD), (2, 0, 1, 3))
        .reshape(new_rows * local_reqs, -1)
    )
    tp_count = lax.axis_size("tp")
    own_count = new_rows // tp_count
    attn_proj = (
        lax.psum_scatter(
            jnp.dot(attended, w_out, preferred_element_type=jnp.float32).astype(jnp.bfloat16),
            "tp",
            scatter_dimension=0,
            tiled=True,
        )
        .astype(jnp.float32)
        .reshape(own_count, local_reqs, model_width)
    )
    own_hidden = lax.dynamic_slice_in_dim(hidden, lax.axis_index("tp") * own_count, own_count, 0)
    resid = own_hidden.astype(jnp.float32) + attn_proj
    normed_own = rms_norm(resid, gain_ffn).reshape(-1, model_width)
    normed_ffn = lax.all_gather(normed_own, "tp", axis=0, tiled=True)
    gate_rows = jnp.dot(normed_ffn, w_gate, preferred_element_type=jnp.float32)
    up_rows = jnp.dot(normed_ffn, w_up, preferred_element_type=jnp.float32)
    activated = (jax.nn.silu(gate_rows) * up_rows).astype(jnp.bfloat16)
    ffn_proj = (
        lax.psum_scatter(
            jnp.dot(activated, w_down, preferred_element_type=jnp.float32).astype(jnp.bfloat16),
            "tp",
            scatter_dimension=0,
            tiled=True,
        )
        .astype(jnp.float32)
        .reshape(own_count, local_reqs, model_width)
    )
    return resid + ffn_proj


def solution(mesh):
    return jax.shard_map(
        shards,
        mesh=mesh,
        in_specs=(
            P(None, "seq", None),
            P(),
            P(None, "tp"),
            P(None, "tp"),
            P(None, "tp"),
            P("tp", None),
            P(),
            P(None, "tp"),
            P(None, "tp"),
            P("tp", None),
            P("seq", "tp", None, None, None),
            P("seq", "tp", None, None, None),
            P(),
            P(),
            P(),
            P(),
            P(),
            P(),
            P(),
            P(),
            P(),
        ),
        out_specs=P("tp", "seq", None),
        check_vma=False,
    )
```

```python
import jax
import jax.numpy as jnp
from jax import lax
from jax.sharding import PartitionSpec as P
from jax.experimental import pallas as pl
from jax.experimental.pallas import tpu as pltpu

QH = 32
KVH = 8
HD = 80
WINDOW = 4096


masked_score = -1e30
rope_base = 10000.0


def rms_norm(row_data, gain_vector):
    values = row_data.astype(jnp.float32)
    inverse_rms = lax.rsqrt(jnp.mean(values * values, -1, keepdims=True) + 1e-05)
    return (values * inverse_rms * gain_vector.astype(jnp.float32)).astype(jnp.bfloat16)


def rotate(vector, position):
    half_size = vector.shape[-1] // 2
    frequency = rope_base ** (-2.0 * jnp.arange(half_size, dtype=jnp.float32) / vector.shape[-1])
    angles = position.astype(jnp.float32)[..., None] * frequency
    cos_part = jnp.cos(angles)
    sin_part = jnp.sin(angles)
    first_half = vector[..., :half_size]
    second_half = vector[..., half_size:]
    return jnp.concatenate(
        [
            first_half * cos_part - second_half * sin_part,
            second_half * cos_part + first_half * sin_part,
        ],
        -1,
    )


def page_columns(pages):
    moved = jnp.moveaxis(pages, -5, -2)
    return moved.reshape(moved.shape[:-2] + (moved.shape[-2] * moved.shape[-1],))


def attend(queries, key_pack, key_pos, present, query_pos):
    scores = jnp.einsum(
        "nbkge,bket->nbkgt", queries, key_pack[:, :, 0], preferred_element_type=jnp.float32
    ) * queries.shape[-1] ** (-0.5)
    distance = query_pos[:, :, None] - key_pos[None, :, :]
    allowed = (present[None, :, :] & (distance >= 0) & (distance < WINDOW))[:, :, None, None, :]
    scores = jnp.where(allowed, scores, masked_score)
    maximum = jnp.max(scores, -1)
    weights = jnp.where(allowed, jnp.exp(scores - maximum[..., None]), 0.0)
    totals = jnp.sum(weights, -1)
    weighted = jnp.einsum(
        "nbkgt,bket->nbkge",
        weights.astype(jnp.bfloat16),
        key_pack[:, :, 1],
        preferred_element_type=jnp.float32,
    )
    return (weighted, maximum, totals)


def merge_parts(first, second):
    maximum = jnp.maximum(first[1], second[1])
    first_scale = jnp.exp(first[1] - maximum)
    second_scale = jnp.exp(second[1] - maximum)
    return (
        first[0] * first_scale[..., None] + second[0] * second_scale[..., None],
        maximum,
        first[2] * first_scale + second[2] * second_scale,
    )


ROOT_PAGES = 16
MID_PAGES = 16
LEAF_SLOTS = 8


def paged_kernel(tbl, meta, q_ref, fresh_ref, shared_hbm, leaf_hbm, out_ref, kv, sc, fresh_sc, top, mass, acc, sem):
    b = pl.program_id(0)
    h = pl.program_id(1)
    requests = pl.num_programs(0)
    slot = b % 2
    shared_count = ROOT_PAGES + MID_PAGES
    page_count = shared_count + LEAF_SLOTS
    width = kv.shape[-1]
    span = 2 * width

    def start_request(j, into):
        def shared_body(p, carry):
            pltpu.make_async_copy(shared_hbm.at[tbl[j, p]], kv.at[into, p], sem.at[into]).start()
            return carry

        def leaf_body(p, carry):
            pltpu.make_async_copy(leaf_hbm.at[tbl[j, p]], kv.at[into, p], sem.at[into]).start()
            return carry

        lax.fori_loop(0, shared_count, shared_body, 0)
        lax.fori_loop(shared_count, page_count, leaf_body, 0)

    @pl.when((h == 0) & (b == 0))
    def _():
        start_request(0, 0)

    @pl.when((h == 0) & (b + 1 < requests))
    def _():
        start_request(b + 1, 1 - slot)

    @pl.when(h == 0)
    def _():
        def wait_body(p, carry):
            pltpu.make_async_copy(shared_hbm.at[0], kv.at[slot, p], sem.at[slot]).wait()
            return carry

        lax.fori_loop(0, page_count, wait_body, 0)

    root_span = meta[b, 0]
    mid_span = meta[b, 1]
    leaf_span = meta[b, 2]
    context = meta[b, 3]
    q = q_ref[0]
    rows = q.shape[0]
    query_pos = context + lax.broadcasted_iota(jnp.int32, (rows, 1), 0)
    lanes = lax.broadcasted_iota(jnp.int32, (1, span), 1)
    scale = HD ** (-0.5)

    def masked(s, key_pos, present):
        distance = query_pos - key_pos
        allowed = present & (distance >= 0) & (distance < WINDOW)
        return jnp.where(allowed, s, masked_score)

    def geometry(c):
        page = 2 * c
        in_root = page < ROOT_PAGES
        in_mid = page < shared_count
        first = jnp.where(
            in_root, page * width, jnp.where(in_mid, (page - ROOT_PAGES) * width, (page - shared_count) * width)
        )
        base = jnp.where(in_root, 0, jnp.where(in_mid, root_span, root_span + mid_span))
        limit = jnp.where(in_root, root_span, jnp.where(in_mid, mid_span, leaf_span))
        return first, base, limit

    def pair(c, part):
        return jnp.concatenate([kv[slot, 2 * c, part], kv[slot, 2 * c + 1, part]], 1)

    fresh_lanes = lax.broadcasted_iota(jnp.int32, (1, width), 1)
    fresh_scores = masked(
        jnp.dot(q, fresh_ref[0, 0], preferred_element_type=jnp.float32) * scale,
        context + fresh_lanes,
        fresh_lanes >= 0,
    )
    fresh_sc[...] = fresh_scores
    top[...] = fresh_scores

    def keep(c, s):
        sc[c] = s
        top[...] = jnp.maximum(top[...], jnp.maximum(s[:, :width], s[:, width:]))

    def max_body(c, carry):
        first, base, limit = geometry(c)
        live = first < limit
        full = (first + span <= limit) & (context + rows - 1 - (base + first) < WINDOW)

        @pl.when(full)
        def _():
            keep(c, jnp.dot(q, pair(c, 0), preferred_element_type=jnp.float32) * scale)

        @pl.when(live & jnp.logical_not(full))
        def _():
            steps_in = first + lanes
            s = jnp.dot(q, pair(c, 0), preferred_element_type=jnp.float32) * scale
            keep(c, masked(s, base + steps_in, steps_in < limit))

        return carry

    chunks = page_count // 2
    lax.fori_loop(0, chunks, max_body, 0)
    top[...] = jnp.broadcast_to(jnp.max(top[...], -1, keepdims=True), top.shape)
    row_top = top[...]

    fresh_w = jnp.exp(fresh_sc[...] - row_top)
    mass[...] = fresh_w
    acc[...] = lax.dot_general(
        fresh_w.astype(jnp.bfloat16), fresh_ref[0, 1], (((1,), (1,)), ((), ())), preferred_element_type=jnp.float32
    )

    def sum_body(c, carry):
        first, base, limit = geometry(c)

        @pl.when(first < limit)
        def _():
            s = sc[c]
            w0 = jnp.exp(s[:, :width] - row_top)
            w1 = jnp.exp(s[:, width:] - row_top)
            mass[...] = mass[...] + w0 + w1
            w = jnp.concatenate([w0, w1], 1).astype(jnp.bfloat16)
            acc[...] = acc[...] + lax.dot_general(
                w, pair(c, 1), (((1,), (1,)), ((), ())), preferred_element_type=jnp.float32
            )

        return carry

    lax.fori_loop(0, chunks, sum_body, 0)
    totals = jnp.sum(mass[...], -1, keepdims=True)
    out_ref[0] = (acc[...] / totals).astype(out_ref.dtype)


def paged_attention(tbl, meta, queries, fresh, shared_store, leaf_store):
    reqs, rows, head = queries.shape
    page_shape = shared_store.shape[1:]
    width = page_shape[-1]
    groups = rows // width
    pages = tbl.shape[1]
    keys_total = (pages + 1) * width
    grid_spec = pltpu.PrefetchScalarGridSpec(
        num_scalar_prefetch=2,
        grid=(reqs, groups),
        in_specs=[
            pl.BlockSpec((1, width, head), lambda i, g, t, m: (i, g, 0)),
            pl.BlockSpec((1,) + page_shape, lambda i, g, t, m: (i, 0, 0, 0)),
            pl.BlockSpec(memory_space=pl.ANY),
            pl.BlockSpec(memory_space=pl.ANY),
        ],
        out_specs=pl.BlockSpec((1, width, head), lambda i, g, t, m: (i, g, 0)),
        scratch_shapes=[
            pltpu.VMEM((2, pages) + page_shape, shared_store.dtype),
            pltpu.VMEM((pages // 2, width, 2 * width), jnp.float32),
            pltpu.VMEM((width, width), jnp.float32),
            pltpu.VMEM((width, width), jnp.float32),
            pltpu.VMEM((width, width), jnp.float32),
            pltpu.VMEM((width, head), jnp.float32),
            pltpu.SemaphoreType.DMA((2,)),
        ],
    )
    return pl.pallas_call(
        paged_kernel,
        grid_spec=grid_spec,
        out_shape=jax.ShapeDtypeStruct((reqs, rows, head), jnp.bfloat16),
        compiler_params=pltpu.CompilerParams(dimension_semantics=("arbitrary", "arbitrary")),
        cost_estimate=pl.CostEstimate(
            flops=4 * reqs * rows * keys_total * head,
            transcendentals=reqs * rows * keys_total,
            bytes_accessed=reqs * (pages + 1) * 2 * head * width * 2,
        ),
    )(tbl, meta, queries, fresh, shared_store, leaf_store)


def spans(request_ids, root_len, mid_len, leaf_len, mid_parent, leaf_parent):
    mid_nodes = leaf_parent[request_ids]
    root_nodes = mid_parent[mid_nodes]
    return (root_nodes, mid_nodes, root_len[root_nodes], mid_len[mid_nodes], leaf_len[request_ids])


def shards(
    hidden,
    gain_attn,
    w_query,
    w_key,
    w_value,
    w_out,
    gain_ffn,
    w_gate,
    w_up,
    w_down,
    shared_pages,
    leaf_pages,
    root_table,
    mid_table,
    leaf_table,
    root_len,
    mid_len,
    leaf_len,
    mid_parent,
    leaf_parent,
    slot_request,
):
    new_rows, local_reqs, model_width = hidden.shape
    seq_count = lax.axis_size("seq")
    seq_index = lax.axis_index("seq")
    kv_local = leaf_pages.shape[1]
    group_size = QH // KVH
    pages_here = leaf_pages.shape[0]
    slot_ids = seq_index * local_reqs + jnp.arange(local_reqs, dtype=jnp.int32)
    requests = slot_request[slot_ids]
    root_nodes, mid_nodes, root_span, mid_span, leaf_span = spans(
        requests, root_len, mid_len, leaf_len, mid_parent, leaf_parent
    )
    context = root_span + mid_span + leaf_span
    new_index = jnp.arange(new_rows, dtype=jnp.int32)
    query_pos = context[None, :] + new_index[:, None]
    all_slots = slot_request.reshape(seq_count, local_reqs)
    page_store = lax.all_gather(shared_pages, "seq", axis=0, tiled=True)
    root_index = root_table[root_nodes]
    mid_index = mid_table[mid_nodes]
    normed = rms_norm(hidden, gain_attn).reshape(-1, model_width)
    query_proj = jnp.dot(normed, w_query, preferred_element_type=jnp.float32).reshape(
        new_rows, local_reqs, -1, HD
    )
    queries = (
        rotate(query_proj, query_pos[:, :, None])
        .astype(jnp.bfloat16)
        .reshape(new_rows, local_reqs, kv_local, group_size, HD)
    )
    key_proj = jnp.dot(normed, w_key, preferred_element_type=jnp.float32).reshape(
        new_rows, local_reqs, kv_local, HD
    )
    new_keys = rotate(key_proj, query_pos[:, :, None]).astype(jnp.bfloat16)
    new_values = (
        jnp.dot(normed, w_value, preferred_element_type=jnp.float32)
        .astype(jnp.bfloat16)
        .reshape(new_rows, local_reqs, kv_local, HD)
    )
    home_of = leaf_table[:, 0] // pages_here
    own_homes = home_of[requests]
    sender_match = home_of[all_slots] == seq_index
    sender_pick = jnp.argmax(sender_match, 1)
    sender_have = jnp.any(sender_match, 1)
    picked_request = jnp.take_along_axis(all_slots, sender_pick[:, None], 1)[:, 0]
    page_ids = jnp.where(
        sender_have[:, None], leaf_table[picked_request] - seq_index * pages_here, 0
    )
    leaf_slots = leaf_table.shape[1]
    outgoing = jnp.where(
        sender_have[:, None, None, None, None, None], jnp.take(leaf_pages, page_ids, axis=0), 0
    )
    arrived = lax.all_to_all(outgoing, "seq", split_axis=0, concat_axis=0, tiled=True)
    page_shape = arrived.shape[-3:]
    leaf_store = arrived.reshape((-1,) + page_shape)
    shared_store = page_store.reshape((-1,) + page_shape)
    tbl = jnp.concatenate(
        [
            root_index,
            mid_index,
            own_homes[:, None] * leaf_slots + jnp.arange(leaf_slots, dtype=jnp.int32)[None, :],
        ],
        1,
    ).astype(jnp.int32)
    meta = jnp.stack([root_span, mid_span, leaf_span, context], 1).astype(jnp.int32)
    fresh_pack = jnp.stack(
        [jnp.transpose(new_keys[:, :, 0], (1, 2, 0)), jnp.transpose(new_values[:, :, 0], (1, 2, 0))], 1
    )
    query_rows = jnp.transpose(queries[:, :, 0], (1, 2, 0, 3)).reshape(local_reqs, -1, HD)
    attended = paged_attention(tbl, meta, query_rows, fresh_pack, shared_store, leaf_store)
    attended = (
        jnp.transpose(attended.reshape(local_reqs, group_size, new_rows, HD), (2, 0, 1, 3))
        .reshape(new_rows * local_reqs, -1)
    )
    tp_count = lax.axis_size("tp")
    own_count = new_rows // tp_count
    attn_proj = (
        lax.psum_scatter(
            jnp.dot(attended, w_out, preferred_element_type=jnp.float32).astype(jnp.bfloat16),
            "tp",
            scatter_dimension=0,
            tiled=True,
        )
        .astype(jnp.float32)
        .reshape(own_count, local_reqs, model_width)
    )
    own_hidden = lax.dynamic_slice_in_dim(hidden, lax.axis_index("tp") * own_count, own_count, 0)
    resid = own_hidden.astype(jnp.float32) + attn_proj
    normed_own = rms_norm(resid, gain_ffn).reshape(-1, model_width)
    normed_ffn = lax.all_gather(normed_own, "tp", axis=0, tiled=True)
    gate_rows = jnp.dot(normed_ffn, w_gate, preferred_element_type=jnp.float32)
    up_rows = jnp.dot(normed_ffn, w_up, preferred_element_type=jnp.float32)
    activated = (jax.nn.silu(gate_rows) * up_rows).astype(jnp.bfloat16)
    ffn_proj = (
        lax.psum_scatter(
            jnp.dot(activated, w_down, preferred_element_type=jnp.float32).astype(jnp.bfloat16),
            "tp",
            scatter_dimension=0,
            tiled=True,
        )
        .astype(jnp.float32)
        .reshape(own_count, local_reqs, model_width)
    )
    return resid + ffn_proj


def solution(mesh):
    return jax.shard_map(
        shards,
        mesh=mesh,
        in_specs=(
            P(None, "seq", None),
            P(),
            P(None, "tp"),
            P(None, "tp"),
            P(None, "tp"),
            P("tp", None),
            P(),
            P(None, "tp"),
            P(None, "tp"),
            P("tp", None),
            P("seq", "tp", None, None, None),
            P("seq", "tp", None, None, None),
            P(),
            P(),
            P(),
            P(),
            P(),
            P(),
            P(),
            P(),
            P(),
        ),
        out_specs=P("tp", "seq", None),
        check_vma=False,
    )
```

```python
import jax
import jax.numpy as jnp
from jax import lax
from jax.sharding import PartitionSpec as P
from jax.experimental import pallas as pl
from jax.experimental.pallas import tpu as pltpu

QH = 32
KVH = 8
HD = 80
WINDOW = 4096


masked_score = -1e30
rope_base = 10000.0


def rms_norm(row_data, gain_vector):
    values = row_data.astype(jnp.float32)
    inverse_rms = lax.rsqrt(jnp.mean(values * values, -1, keepdims=True) + 1e-05)
    return (values * inverse_rms * gain_vector.astype(jnp.float32)).astype(jnp.bfloat16)


def rotate(vector, position):
    half_size = vector.shape[-1] // 2
    frequency = rope_base ** (-2.0 * jnp.arange(half_size, dtype=jnp.float32) / vector.shape[-1])
    angles = position.astype(jnp.float32)[..., None] * frequency
    cos_part = jnp.cos(angles)
    sin_part = jnp.sin(angles)
    first_half = vector[..., :half_size]
    second_half = vector[..., half_size:]
    return jnp.concatenate(
        [
            first_half * cos_part - second_half * sin_part,
            second_half * cos_part + first_half * sin_part,
        ],
        -1,
    )


def page_columns(pages):
    moved = jnp.moveaxis(pages, -5, -2)
    return moved.reshape(moved.shape[:-2] + (moved.shape[-2] * moved.shape[-1],))


def attend(queries, key_pack, key_pos, present, query_pos):
    scores = jnp.einsum(
        "nbkge,bket->nbkgt", queries, key_pack[:, :, 0], preferred_element_type=jnp.float32
    ) * queries.shape[-1] ** (-0.5)
    distance = query_pos[:, :, None] - key_pos[None, :, :]
    allowed = (present[None, :, :] & (distance >= 0) & (distance < WINDOW))[:, :, None, None, :]
    scores = jnp.where(allowed, scores, masked_score)
    maximum = jnp.max(scores, -1)
    weights = jnp.where(allowed, jnp.exp(scores - maximum[..., None]), 0.0)
    totals = jnp.sum(weights, -1)
    weighted = jnp.einsum(
        "nbkgt,bket->nbkge",
        weights.astype(jnp.bfloat16),
        key_pack[:, :, 1],
        preferred_element_type=jnp.float32,
    )
    return (weighted, maximum, totals)


def merge_parts(first, second):
    maximum = jnp.maximum(first[1], second[1])
    first_scale = jnp.exp(first[1] - maximum)
    second_scale = jnp.exp(second[1] - maximum)
    return (
        first[0] * first_scale[..., None] + second[0] * second_scale[..., None],
        maximum,
        first[2] * first_scale + second[2] * second_scale,
    )


ROOT_PAGES = 16
MID_PAGES = 16
LEAF_SLOTS = 8
CHUNK_PAGES = 4


def paged_kernel(tbl, meta, q_ref, fresh_ref, shared_hbm, leaf_hbm, out_ref, kv, sc, fresh_sc, top, mass, acc, sem):
    b = pl.program_id(0)
    requests = pl.num_programs(0)
    slot = b % 2
    shared_count = ROOT_PAGES + MID_PAGES
    page_count = shared_count + LEAF_SLOTS
    width = kv.shape[-1]
    group = CHUNK_PAGES
    span = group * width

    def start_request(j, into):
        def shared_body(p, carry):
            pltpu.make_async_copy(shared_hbm.at[tbl[j, p]], kv.at[into, p], sem.at[into]).start()
            return carry

        def leaf_body(p, carry):
            pltpu.make_async_copy(leaf_hbm.at[tbl[j, p]], kv.at[into, p], sem.at[into]).start()
            return carry

        lax.fori_loop(0, shared_count, shared_body, 0)
        lax.fori_loop(shared_count, page_count, leaf_body, 0)

    @pl.when(b == 0)
    def _():
        start_request(0, 0)

    @pl.when(b + 1 < requests)
    def _():
        start_request(b + 1, 1 - slot)

    def wait_body(p, carry):
        pltpu.make_async_copy(shared_hbm.at[0], kv.at[slot, p], sem.at[slot]).wait()
        return carry

    lax.fori_loop(0, page_count, wait_body, 0)

    root_span = meta[b, 0]
    mid_span = meta[b, 1]
    leaf_span = meta[b, 2]
    context = meta[b, 3]
    q = q_ref[0]
    rows = q.shape[0]
    query_pos = context + (lax.broadcasted_iota(jnp.int32, (rows, 1), 0) % width)
    lanes = lax.broadcasted_iota(jnp.int32, (1, span), 1)
    scale = HD ** (-0.5)

    def masked(s, key_pos, present):
        distance = query_pos - key_pos
        allowed = present & (distance >= 0) & (distance < WINDOW)
        return jnp.where(allowed, s, masked_score)

    def geometry(c):
        page = group * c
        in_root = page < ROOT_PAGES
        in_mid = page < shared_count
        first = jnp.where(
            in_root, page * width, jnp.where(in_mid, (page - ROOT_PAGES) * width, (page - shared_count) * width)
        )
        base = jnp.where(in_root, 0, jnp.where(in_mid, root_span, root_span + mid_span))
        limit = jnp.where(in_root, root_span, jnp.where(in_mid, mid_span, leaf_span))
        return first, base, limit

    def pages_of(c, part):
        return jnp.concatenate([kv[slot, group * c + k, part] for k in range(group)], 1)

    fresh_lanes = lax.broadcasted_iota(jnp.int32, (1, width), 1)
    fresh_scores = masked(
        jnp.dot(q, fresh_ref[0, 0], preferred_element_type=jnp.float32) * scale,
        context + fresh_lanes,
        fresh_lanes >= 0,
    )
    fresh_sc[...] = fresh_scores
    top[...] = fresh_scores

    def keep(c, s):
        sc[c] = s
        m = top[...]
        for k in range(group):
            m = jnp.maximum(m, s[:, k * width:(k + 1) * width])
        top[...] = m

    def max_body(c, carry):
        first, base, limit = geometry(c)
        live = (first < limit) & (context - (base + first + span - 1) < WINDOW)
        full = (first + span <= limit) & (context + width - 1 - (base + first) < WINDOW)

        @pl.when(full)
        def _():
            keep(c, jnp.dot(q, pages_of(c, 0), preferred_element_type=jnp.float32) * scale)

        @pl.when(live & jnp.logical_not(full))
        def _():
            steps_in = first + lanes
            s = jnp.dot(q, pages_of(c, 0), preferred_element_type=jnp.float32) * scale
            keep(c, masked(s, base + steps_in, steps_in < limit))

        return carry

    chunks = page_count // group
    lax.fori_loop(0, chunks, max_body, 0)
    top[...] = jnp.broadcast_to(jnp.max(top[...], -1, keepdims=True), top.shape)
    row_top = top[...]

    fresh_w = jnp.exp(fresh_sc[...] - row_top)
    mass[...] = fresh_w
    acc[...] = lax.dot_general(
        fresh_w.astype(jnp.bfloat16), fresh_ref[0, 1], (((1,), (1,)), ((), ())), preferred_element_type=jnp.float32
    )

    def sum_body(c, carry):
        first, base, limit = geometry(c)
        live = (first < limit) & (context - (base + first + span - 1) < WINDOW)

        @pl.when(live)
        def _():
            s = sc[c]
            parts = [jnp.exp(s[:, k * width:(k + 1) * width] - row_top) for k in range(group)]
            total = mass[...]
            for part in parts:
                total = total + part
            mass[...] = total
            w = jnp.concatenate(parts, 1).astype(jnp.bfloat16)
            acc[...] = acc[...] + lax.dot_general(
                w, pages_of(c, 1), (((1,), (1,)), ((), ())), preferred_element_type=jnp.float32
            )

        return carry

    lax.fori_loop(0, chunks, sum_body, 0)
    totals = jnp.sum(mass[...], -1, keepdims=True)
    out_ref[0] = (acc[...] / totals).astype(out_ref.dtype)


def paged_attention(tbl, meta, queries, fresh, shared_store, leaf_store):
    reqs, rows, head = queries.shape
    page_shape = shared_store.shape[1:]
    width = page_shape[-1]
    pages = tbl.shape[1]
    keys_total = (pages + 1) * width
    grid_spec = pltpu.PrefetchScalarGridSpec(
        num_scalar_prefetch=2,
        grid=(reqs,),
        in_specs=[
            pl.BlockSpec((1, rows, head), lambda i, t, m: (i, 0, 0)),
            pl.BlockSpec((1,) + page_shape, lambda i, t, m: (i, 0, 0, 0)),
            pl.BlockSpec(memory_space=pl.ANY),
            pl.BlockSpec(memory_space=pl.ANY),
        ],
        out_specs=pl.BlockSpec((1, rows, head), lambda i, t, m: (i, 0, 0)),
        scratch_shapes=[
            pltpu.VMEM((2, pages) + page_shape, shared_store.dtype),
            pltpu.VMEM((pages // CHUNK_PAGES, rows, CHUNK_PAGES * width), jnp.float32),
            pltpu.VMEM((rows, width), jnp.float32),
            pltpu.VMEM((rows, width), jnp.float32),
            pltpu.VMEM((rows, width), jnp.float32),
            pltpu.VMEM((rows, head), jnp.float32),
            pltpu.SemaphoreType.DMA((2,)),
        ],
    )
    return pl.pallas_call(
        paged_kernel,
        grid_spec=grid_spec,
        out_shape=jax.ShapeDtypeStruct((reqs, rows, head), jnp.bfloat16),
        compiler_params=pltpu.CompilerParams(dimension_semantics=("arbitrary",)),
        cost_estimate=pl.CostEstimate(
            flops=4 * reqs * rows * keys_total * head,
            transcendentals=reqs * rows * keys_total,
            bytes_accessed=reqs * (pages + 1) * 2 * head * width * 2,
        ),
    )(tbl, meta, queries, fresh, shared_store, leaf_store)


def spans(request_ids, root_len, mid_len, leaf_len, mid_parent, leaf_parent):
    mid_nodes = leaf_parent[request_ids]
    root_nodes = mid_parent[mid_nodes]
    return (root_nodes, mid_nodes, root_len[root_nodes], mid_len[mid_nodes], leaf_len[request_ids])


def shards(
    hidden,
    gain_attn,
    w_query,
    w_key,
    w_value,
    w_out,
    gain_ffn,
    w_gate,
    w_up,
    w_down,
    shared_pages,
    leaf_pages,
    root_table,
    mid_table,
    leaf_table,
    root_len,
    mid_len,
    leaf_len,
    mid_parent,
    leaf_parent,
    slot_request,
):
    new_rows, local_reqs, model_width = hidden.shape
    seq_count = lax.axis_size("seq")
    seq_index = lax.axis_index("seq")
    kv_local = leaf_pages.shape[1]
    group_size = QH // KVH
    pages_here = leaf_pages.shape[0]
    slot_ids = seq_index * local_reqs + jnp.arange(local_reqs, dtype=jnp.int32)
    requests = slot_request[slot_ids]
    root_nodes, mid_nodes, root_span, mid_span, leaf_span = spans(
        requests, root_len, mid_len, leaf_len, mid_parent, leaf_parent
    )
    context = root_span + mid_span + leaf_span
    new_index = jnp.arange(new_rows, dtype=jnp.int32)
    query_pos = context[None, :] + new_index[:, None]
    all_slots = slot_request.reshape(seq_count, local_reqs)
    page_store = lax.all_gather(shared_pages, "seq", axis=0, tiled=True)
    root_index = root_table[root_nodes]
    mid_index = mid_table[mid_nodes]
    normed = rms_norm(hidden, gain_attn).reshape(-1, model_width)
    query_proj = jnp.dot(normed, w_query, preferred_element_type=jnp.float32).reshape(
        new_rows, local_reqs, -1, HD
    )
    queries = (
        rotate(query_proj, query_pos[:, :, None])
        .astype(jnp.bfloat16)
        .reshape(new_rows, local_reqs, kv_local, group_size, HD)
    )
    key_proj = jnp.dot(normed, w_key, preferred_element_type=jnp.float32).reshape(
        new_rows, local_reqs, kv_local, HD
    )
    new_keys = rotate(key_proj, query_pos[:, :, None]).astype(jnp.bfloat16)
    new_values = (
        jnp.dot(normed, w_value, preferred_element_type=jnp.float32)
        .astype(jnp.bfloat16)
        .reshape(new_rows, local_reqs, kv_local, HD)
    )
    home_of = leaf_table[:, 0] // pages_here
    own_homes = home_of[requests]
    sender_match = home_of[all_slots] == seq_index
    sender_pick = jnp.argmax(sender_match, 1)
    sender_have = jnp.any(sender_match, 1)
    picked_request = jnp.take_along_axis(all_slots, sender_pick[:, None], 1)[:, 0]
    page_ids = jnp.where(
        sender_have[:, None], leaf_table[picked_request] - seq_index * pages_here, 0
    )
    leaf_slots = leaf_table.shape[1]
    outgoing = jnp.where(
        sender_have[:, None, None, None, None, None], jnp.take(leaf_pages, page_ids, axis=0), 0
    )
    arrived = lax.all_to_all(outgoing, "seq", split_axis=0, concat_axis=0, tiled=True)
    page_shape = arrived.shape[-3:]
    leaf_store = arrived.reshape((-1,) + page_shape)
    shared_store = page_store.reshape((-1,) + page_shape)
    tbl = jnp.concatenate(
        [
            root_index,
            mid_index,
            own_homes[:, None] * leaf_slots + jnp.arange(leaf_slots, dtype=jnp.int32)[None, :],
        ],
        1,
    ).astype(jnp.int32)
    meta = jnp.stack([root_span, mid_span, leaf_span, context], 1).astype(jnp.int32)
    fresh_pack = jnp.stack(
        [jnp.transpose(new_keys[:, :, 0], (1, 2, 0)), jnp.transpose(new_values[:, :, 0], (1, 2, 0))], 1
    )
    query_rows = jnp.transpose(queries[:, :, 0], (1, 2, 0, 3)).reshape(local_reqs, -1, HD)
    attended = paged_attention(tbl, meta, query_rows, fresh_pack, shared_store, leaf_store)
    attended = (
        jnp.transpose(attended.reshape(local_reqs, group_size, new_rows, HD), (2, 0, 1, 3))
        .reshape(new_rows * local_reqs, -1)
    )
    tp_count = lax.axis_size("tp")
    own_count = new_rows // tp_count
    attn_proj = (
        lax.psum_scatter(
            jnp.dot(attended, w_out, preferred_element_type=jnp.float32).astype(jnp.bfloat16),
            "tp",
            scatter_dimension=0,
            tiled=True,
        )
        .astype(jnp.float32)
        .reshape(own_count, local_reqs, model_width)
    )
    own_hidden = lax.dynamic_slice_in_dim(hidden, lax.axis_index("tp") * own_count, own_count, 0)
    resid = own_hidden.astype(jnp.float32) + attn_proj
    normed_own = rms_norm(resid, gain_ffn).reshape(-1, model_width)
    normed_ffn = lax.all_gather(normed_own, "tp", axis=0, tiled=True)
    gate_rows = jnp.dot(normed_ffn, w_gate, preferred_element_type=jnp.float32)
    up_rows = jnp.dot(normed_ffn, w_up, preferred_element_type=jnp.float32)
    activated = (jax.nn.silu(gate_rows) * up_rows).astype(jnp.bfloat16)
    ffn_proj = (
        lax.psum_scatter(
            jnp.dot(activated, w_down, preferred_element_type=jnp.float32).astype(jnp.bfloat16),
            "tp",
            scatter_dimension=0,
            tiled=True,
        )
        .astype(jnp.float32)
        .reshape(own_count, local_reqs, model_width)
    )
    return resid + ffn_proj


def solution(mesh):
    return jax.shard_map(
        shards,
        mesh=mesh,
        in_specs=(
            P(None, "seq", None),
            P(),
            P(None, "tp"),
            P(None, "tp"),
            P(None, "tp"),
            P("tp", None),
            P(),
            P(None, "tp"),
            P(None, "tp"),
            P("tp", None),
            P("seq", "tp", None, None, None),
            P("seq", "tp", None, None, None),
            P(),
            P(),
            P(),
            P(),
            P(),
            P(),
            P(),
            P(),
            P(),
        ),
        out_specs=P("tp", "seq", None),
        check_vma=False,
    )
```

```python
import jax
import jax.numpy as jnp
from jax import lax
from jax.sharding import PartitionSpec as P
from jax.experimental import pallas as pl
from jax.experimental.pallas import tpu as pltpu

QH = 32
KVH = 8
HD = 80
WINDOW = 4096


masked_score = -1e30
rope_base = 10000.0


def rms_norm(row_data, gain_vector):
    values = row_data.astype(jnp.float32)
    inverse_rms = lax.rsqrt(jnp.mean(values * values, -1, keepdims=True) + 1e-05)
    return (values * inverse_rms * gain_vector.astype(jnp.float32)).astype(jnp.bfloat16)


def rotate(vector, position):
    half_size = vector.shape[-1] // 2
    frequency = rope_base ** (-2.0 * jnp.arange(half_size, dtype=jnp.float32) / vector.shape[-1])
    angles = position.astype(jnp.float32)[..., None] * frequency
    cos_part = jnp.cos(angles)
    sin_part = jnp.sin(angles)
    first_half = vector[..., :half_size]
    second_half = vector[..., half_size:]
    return jnp.concatenate(
        [
            first_half * cos_part - second_half * sin_part,
            second_half * cos_part + first_half * sin_part,
        ],
        -1,
    )


def page_columns(pages):
    moved = jnp.moveaxis(pages, -5, -2)
    return moved.reshape(moved.shape[:-2] + (moved.shape[-2] * moved.shape[-1],))


def attend(queries, key_pack, key_pos, present, query_pos):
    scores = jnp.einsum(
        "nbkge,bket->nbkgt", queries, key_pack[:, :, 0], preferred_element_type=jnp.float32
    ) * queries.shape[-1] ** (-0.5)
    distance = query_pos[:, :, None] - key_pos[None, :, :]
    allowed = (present[None, :, :] & (distance >= 0) & (distance < WINDOW))[:, :, None, None, :]
    scores = jnp.where(allowed, scores, masked_score)
    maximum = jnp.max(scores, -1)
    weights = jnp.where(allowed, jnp.exp(scores - maximum[..., None]), 0.0)
    totals = jnp.sum(weights, -1)
    weighted = jnp.einsum(
        "nbkgt,bket->nbkge",
        weights.astype(jnp.bfloat16),
        key_pack[:, :, 1],
        preferred_element_type=jnp.float32,
    )
    return (weighted, maximum, totals)


def merge_parts(first, second):
    maximum = jnp.maximum(first[1], second[1])
    first_scale = jnp.exp(first[1] - maximum)
    second_scale = jnp.exp(second[1] - maximum)
    return (
        first[0] * first_scale[..., None] + second[0] * second_scale[..., None],
        maximum,
        first[2] * first_scale + second[2] * second_scale,
    )


ROOT_PAGES = 16
MID_PAGES = 16
LEAF_SLOTS = 8
CHUNK_PAGES = 4


def paged_kernel(tbl, meta, q_ref, fresh_ref, shared_hbm, leaf_hbm, out_ref, kv, sc, fresh_sc, top, mass, acc, sem):
    b = pl.program_id(0)
    requests = pl.num_programs(0)
    slot = b % 2
    shared_count = ROOT_PAGES + MID_PAGES
    page_count = shared_count + LEAF_SLOTS
    width = kv.shape[-1]
    group = CHUNK_PAGES
    span = group * width

    def start_request(j, into):
        def shared_body(p, carry):
            pltpu.make_async_copy(shared_hbm.at[tbl[j, p]], kv.at[into, p], sem.at[into]).start()
            return carry

        def leaf_body(p, carry):
            pltpu.make_async_copy(leaf_hbm.at[tbl[j, p]], kv.at[into, p], sem.at[into]).start()
            return carry

        lax.fori_loop(0, ROOT_PAGES, shared_body, 0)
        lax.fori_loop(ROOT_PAGES, page_count, leaf_body, 0)

    @pl.when(b == 0)
    def _():
        start_request(0, 0)

    @pl.when(b + 1 < requests)
    def _():
        start_request(b + 1, 1 - slot)

    def wait_body(p, carry):
        pltpu.make_async_copy(shared_hbm.at[0], kv.at[slot, p], sem.at[slot]).wait()
        return carry

    lax.fori_loop(0, page_count, wait_body, 0)

    root_span = meta[b, 0]
    mid_span = meta[b, 1]
    leaf_span = meta[b, 2]
    context = meta[b, 3]
    q = q_ref[0]
    rows = q.shape[0]
    query_pos = context + (lax.broadcasted_iota(jnp.int32, (rows, 1), 0) % width)
    lanes = lax.broadcasted_iota(jnp.int32, (1, span), 1)
    scale = HD ** (-0.5)

    def masked(s, key_pos, present):
        distance = query_pos - key_pos
        allowed = present & (distance >= 0) & (distance < WINDOW)
        return jnp.where(allowed, s, masked_score)

    def geometry(c):
        page = group * c
        in_root = page < ROOT_PAGES
        in_mid = page < shared_count
        first = jnp.where(
            in_root, page * width, jnp.where(in_mid, (page - ROOT_PAGES) * width, (page - shared_count) * width)
        )
        base = jnp.where(in_root, 0, jnp.where(in_mid, root_span, root_span + mid_span))
        limit = jnp.where(in_root, root_span, jnp.where(in_mid, mid_span, leaf_span))
        return first, base, limit

    def pages_of(c, part):
        return jnp.concatenate([kv[slot, group * c + k, part] for k in range(group)], 1)

    fresh_lanes = lax.broadcasted_iota(jnp.int32, (1, width), 1)
    fresh_scores = masked(
        jnp.dot(q, fresh_ref[0, 0], preferred_element_type=jnp.float32) * scale,
        context + fresh_lanes,
        fresh_lanes >= 0,
    )
    fresh_sc[...] = fresh_scores
    top[...] = fresh_scores

    def keep(c, s):
        sc[c] = s
        m = top[...]
        for k in range(group):
            m = jnp.maximum(m, s[:, k * width:(k + 1) * width])
        top[...] = m

    def max_body(c, carry):
        first, base, limit = geometry(c)
        live = (first < limit) & (context - (base + first + span - 1) < WINDOW)
        full = (first + span <= limit) & (context + width - 1 - (base + first) < WINDOW)

        @pl.when(full)
        def _():
            keep(c, jnp.dot(q, pages_of(c, 0), preferred_element_type=jnp.float32) * scale)

        @pl.when(live & jnp.logical_not(full))
        def _():
            steps_in = first + lanes
            s = jnp.dot(q, pages_of(c, 0), preferred_element_type=jnp.float32) * scale
            keep(c, masked(s, base + steps_in, steps_in < limit))

        return carry

    chunks = page_count // group
    lax.fori_loop(0, chunks, max_body, 0)
    top[...] = jnp.broadcast_to(jnp.max(top[...], -1, keepdims=True), top.shape)
    row_top = top[...]

    fresh_w = jnp.exp(fresh_sc[...] - row_top)
    mass[...] = fresh_w
    acc[...] = lax.dot_general(
        fresh_w.astype(jnp.bfloat16), fresh_ref[0, 1], (((1,), (1,)), ((), ())), preferred_element_type=jnp.float32
    )

    def sum_body(c, carry):
        first, base, limit = geometry(c)
        live = (first < limit) & (context - (base + first + span - 1) < WINDOW)

        @pl.when(live)
        def _():
            s = sc[c]
            parts = [jnp.exp(s[:, k * width:(k + 1) * width] - row_top) for k in range(group)]
            total = mass[...]
            for part in parts:
                total = total + part
            mass[...] = total
            w = jnp.concatenate(parts, 1).astype(jnp.bfloat16)
            acc[...] = acc[...] + lax.dot_general(
                w, pages_of(c, 1), (((1,), (1,)), ((), ())), preferred_element_type=jnp.float32
            )

        return carry

    lax.fori_loop(0, chunks, sum_body, 0)
    totals = jnp.sum(mass[...], -1, keepdims=True)
    out_ref[0] = (acc[...] / totals).astype(out_ref.dtype)


def paged_attention(tbl, meta, queries, fresh, shared_store, leaf_store):
    reqs, rows, head = queries.shape
    page_shape = shared_store.shape[1:]
    width = page_shape[-1]
    pages = tbl.shape[1]
    keys_total = (pages + 1) * width
    grid_spec = pltpu.PrefetchScalarGridSpec(
        num_scalar_prefetch=2,
        grid=(reqs,),
        in_specs=[
            pl.BlockSpec((1, rows, head), lambda i, t, m: (i, 0, 0)),
            pl.BlockSpec((1,) + page_shape, lambda i, t, m: (i, 0, 0, 0)),
            pl.BlockSpec(memory_space=pl.ANY),
            pl.BlockSpec(memory_space=pl.ANY),
        ],
        out_specs=pl.BlockSpec((1, rows, head), lambda i, t, m: (i, 0, 0)),
        scratch_shapes=[
            pltpu.VMEM((2, pages) + page_shape, shared_store.dtype),
            pltpu.VMEM((pages // CHUNK_PAGES, rows, CHUNK_PAGES * width), jnp.float32),
            pltpu.VMEM((rows, width), jnp.float32),
            pltpu.VMEM((rows, width), jnp.float32),
            pltpu.VMEM((rows, width), jnp.float32),
            pltpu.VMEM((rows, head), jnp.float32),
            pltpu.SemaphoreType.DMA((2,)),
        ],
    )
    return pl.pallas_call(
        paged_kernel,
        grid_spec=grid_spec,
        out_shape=jax.ShapeDtypeStruct((reqs, rows, head), jnp.bfloat16),
        compiler_params=pltpu.CompilerParams(dimension_semantics=("arbitrary",)),
        cost_estimate=pl.CostEstimate(
            flops=4 * reqs * rows * keys_total * head,
            transcendentals=reqs * rows * keys_total,
            bytes_accessed=reqs * (pages + 1) * 2 * head * width * 2,
        ),
    )(tbl, meta, queries, fresh, shared_store, leaf_store)


def spans(request_ids, root_len, mid_len, leaf_len, mid_parent, leaf_parent):
    mid_nodes = leaf_parent[request_ids]
    root_nodes = mid_parent[mid_nodes]
    return (root_nodes, mid_nodes, root_len[root_nodes], mid_len[mid_nodes], leaf_len[request_ids])


def shards(
    hidden,
    gain_attn,
    w_query,
    w_key,
    w_value,
    w_out,
    gain_ffn,
    w_gate,
    w_up,
    w_down,
    shared_pages,
    leaf_pages,
    root_table,
    mid_table,
    leaf_table,
    root_len,
    mid_len,
    leaf_len,
    mid_parent,
    leaf_parent,
    slot_request,
):
    new_rows, local_reqs, model_width = hidden.shape
    seq_count = lax.axis_size("seq")
    seq_index = lax.axis_index("seq")
    kv_local = leaf_pages.shape[1]
    group_size = QH // KVH
    pages_here = leaf_pages.shape[0]
    slot_ids = seq_index * local_reqs + jnp.arange(local_reqs, dtype=jnp.int32)
    requests = slot_request[slot_ids]
    root_nodes, mid_nodes, root_span, mid_span, leaf_span = spans(
        requests, root_len, mid_len, leaf_len, mid_parent, leaf_parent
    )
    context = root_span + mid_span + leaf_span
    new_index = jnp.arange(new_rows, dtype=jnp.int32)
    query_pos = context[None, :] + new_index[:, None]
    all_slots = slot_request.reshape(seq_count, local_reqs)
    per_index = shared_pages.shape[0]
    root_home = root_table // per_index
    root_local = jnp.take_along_axis(
        root_table, jnp.argmax(root_home == seq_index, 1)[:, None], 1
    )[:, 0] - seq_index * per_index
    mid_home = mid_table // per_index
    mid_local = jnp.take_along_axis(
        mid_table, jnp.argmax(mid_home == seq_index, 1)[:, None], 1
    )[:, 0] - seq_index * per_index
    root_store = lax.all_gather(jnp.take(shared_pages, root_local, axis=0), "seq", axis=0, tiled=True)
    root_count = root_table.shape[0]
    normed = rms_norm(hidden, gain_attn).reshape(-1, model_width)
    query_proj = jnp.dot(normed, w_query, preferred_element_type=jnp.float32).reshape(
        new_rows, local_reqs, -1, HD
    )
    queries = (
        rotate(query_proj, query_pos[:, :, None])
        .astype(jnp.bfloat16)
        .reshape(new_rows, local_reqs, kv_local, group_size, HD)
    )
    key_proj = jnp.dot(normed, w_key, preferred_element_type=jnp.float32).reshape(
        new_rows, local_reqs, kv_local, HD
    )
    new_keys = rotate(key_proj, query_pos[:, :, None]).astype(jnp.bfloat16)
    new_values = (
        jnp.dot(normed, w_value, preferred_element_type=jnp.float32)
        .astype(jnp.bfloat16)
        .reshape(new_rows, local_reqs, kv_local, HD)
    )
    home_of = leaf_table[:, 0] // pages_here
    own_homes = home_of[requests]
    sender_match = home_of[all_slots] == seq_index
    sender_pick = jnp.argmax(sender_match, 1)
    sender_have = jnp.any(sender_match, 1)
    picked_request = jnp.take_along_axis(all_slots, sender_pick[:, None], 1)[:, 0]
    page_ids = jnp.where(
        sender_have[:, None], leaf_table[picked_request] - seq_index * pages_here, 0
    )
    leaf_slots = leaf_table.shape[1]
    mid_out = jnp.take(shared_pages, mid_local[leaf_parent[all_slots]], axis=0)
    outgoing = jnp.concatenate([jnp.take(leaf_pages, page_ids, axis=0), mid_out], 1)
    arrived = lax.all_to_all(outgoing, "seq", split_axis=0, concat_axis=0, tiled=True)
    per_source = arrived.shape[1]
    page_shape = arrived.shape[-3:]
    rest_store = arrived.reshape((-1,) + page_shape)
    root_pages = root_store.reshape((-1,) + page_shape)
    slot_ids_local = jnp.arange(local_reqs, dtype=jnp.int32)
    tbl = jnp.concatenate(
        [
            root_home[root_nodes] * root_count + root_nodes[:, None],
            mid_home[mid_nodes] * per_source + leaf_slots + slot_ids_local[:, None],
            own_homes[:, None] * per_source + jnp.arange(leaf_slots, dtype=jnp.int32)[None, :],
        ],
        1,
    ).astype(jnp.int32)
    meta = jnp.stack([root_span, mid_span, leaf_span, context], 1).astype(jnp.int32)
    fresh_pack = jnp.stack(
        [jnp.transpose(new_keys[:, :, 0], (1, 2, 0)), jnp.transpose(new_values[:, :, 0], (1, 2, 0))], 1
    )
    query_rows = jnp.transpose(queries[:, :, 0], (1, 2, 0, 3)).reshape(local_reqs, -1, HD)
    attended = paged_attention(tbl, meta, query_rows, fresh_pack, root_pages, rest_store)
    attended = (
        jnp.transpose(attended.reshape(local_reqs, group_size, new_rows, HD), (2, 0, 1, 3))
        .reshape(new_rows * local_reqs, -1)
    )
    tp_count = lax.axis_size("tp")
    own_count = new_rows // tp_count
    attn_proj = (
        lax.psum_scatter(
            jnp.dot(attended, w_out, preferred_element_type=jnp.float32).astype(jnp.bfloat16),
            "tp",
            scatter_dimension=0,
            tiled=True,
        )
        .astype(jnp.float32)
        .reshape(own_count, local_reqs, model_width)
    )
    own_hidden = lax.dynamic_slice_in_dim(hidden, lax.axis_index("tp") * own_count, own_count, 0)
    resid = own_hidden.astype(jnp.float32) + attn_proj
    normed_own = rms_norm(resid, gain_ffn).reshape(-1, model_width)
    normed_ffn = lax.all_gather(normed_own, "tp", axis=0, tiled=True)
    gate_rows = jnp.dot(normed_ffn, w_gate, preferred_element_type=jnp.float32)
    up_rows = jnp.dot(normed_ffn, w_up, preferred_element_type=jnp.float32)
    activated = (jax.nn.silu(gate_rows) * up_rows).astype(jnp.bfloat16)
    ffn_proj = (
        lax.psum_scatter(
            jnp.dot(activated, w_down, preferred_element_type=jnp.float32).astype(jnp.bfloat16),
            "tp",
            scatter_dimension=0,
            tiled=True,
        )
        .astype(jnp.float32)
        .reshape(own_count, local_reqs, model_width)
    )
    return resid + ffn_proj


def solution(mesh):
    return jax.shard_map(
        shards,
        mesh=mesh,
        in_specs=(
            P(None, "seq", None),
            P(),
            P(None, "tp"),
            P(None, "tp"),
            P(None, "tp"),
            P("tp", None),
            P(),
            P(None, "tp"),
            P(None, "tp"),
            P("tp", None),
            P("seq", "tp", None, None, None),
            P("seq", "tp", None, None, None),
            P(),
            P(),
            P(),
            P(),
            P(),
            P(),
            P(),
            P(),
            P(),
        ),
        out_specs=P("tp", "seq", None),
        check_vma=False,
    )
```

```python
import jax
import jax.numpy as jnp
from jax import lax
from jax.sharding import PartitionSpec as P
from jax.experimental import pallas as pl
from jax.experimental.pallas import tpu as pltpu

QH = 32
KVH = 8
HD = 80
WINDOW = 4096


masked_score = -1e30
rope_base = 10000.0


def rms_norm(row_data, gain_vector):
    values = row_data.astype(jnp.float32)
    inverse_rms = lax.rsqrt(jnp.mean(values * values, -1, keepdims=True) + 1e-05)
    return (values * inverse_rms * gain_vector.astype(jnp.float32)).astype(jnp.bfloat16)


def rotate(vector, position):
    half_size = vector.shape[-1] // 2
    frequency = rope_base ** (-2.0 * jnp.arange(half_size, dtype=jnp.float32) / vector.shape[-1])
    angles = position.astype(jnp.float32)[..., None] * frequency
    cos_part = jnp.cos(angles)
    sin_part = jnp.sin(angles)
    first_half = vector[..., :half_size]
    second_half = vector[..., half_size:]
    return jnp.concatenate(
        [
            first_half * cos_part - second_half * sin_part,
            second_half * cos_part + first_half * sin_part,
        ],
        -1,
    )


def page_columns(pages):
    moved = jnp.moveaxis(pages, -5, -2)
    return moved.reshape(moved.shape[:-2] + (moved.shape[-2] * moved.shape[-1],))


def attend(queries, key_pack, key_pos, present, query_pos):
    scores = jnp.einsum(
        "nbkge,bket->nbkgt", queries, key_pack[:, :, 0], preferred_element_type=jnp.float32
    ) * queries.shape[-1] ** (-0.5)
    distance = query_pos[:, :, None] - key_pos[None, :, :]
    allowed = (present[None, :, :] & (distance >= 0) & (distance < WINDOW))[:, :, None, None, :]
    scores = jnp.where(allowed, scores, masked_score)
    maximum = jnp.max(scores, -1)
    weights = jnp.where(allowed, jnp.exp(scores - maximum[..., None]), 0.0)
    totals = jnp.sum(weights, -1)
    weighted = jnp.einsum(
        "nbkgt,bket->nbkge",
        weights.astype(jnp.bfloat16),
        key_pack[:, :, 1],
        preferred_element_type=jnp.float32,
    )
    return (weighted, maximum, totals)


def merge_parts(first, second):
    maximum = jnp.maximum(first[1], second[1])
    first_scale = jnp.exp(first[1] - maximum)
    second_scale = jnp.exp(second[1] - maximum)
    return (
        first[0] * first_scale[..., None] + second[0] * second_scale[..., None],
        maximum,
        first[2] * first_scale + second[2] * second_scale,
    )


ROOT_PAGES = 16
MID_PAGES = 16
LEAF_SLOTS = 8
CHUNK_PAGES = 4


def paged_kernel(tbl, meta, q_ref, fresh_ref, shared_hbm, leaf_hbm, out_ref, kv, sc, fresh_sc, top, mass, acc, sem):
    b = pl.program_id(0)
    requests = pl.num_programs(0)
    slot = b % 2
    shared_count = ROOT_PAGES + MID_PAGES
    page_count = shared_count + LEAF_SLOTS
    width = kv.shape[-1]
    group = CHUNK_PAGES
    span = group * width

    def start_request(j, into):
        def shared_body(p, carry):
            pltpu.make_async_copy(shared_hbm.at[tbl[j, p]], kv.at[into, p], sem.at[into]).start()
            return carry

        def leaf_body(p, carry):
            pltpu.make_async_copy(leaf_hbm.at[tbl[j, p]], kv.at[into, p], sem.at[into]).start()
            return carry

        lax.fori_loop(0, shared_count, shared_body, 0)
        lax.fori_loop(shared_count, page_count, leaf_body, 0)

    @pl.when(b == 0)
    def _():
        start_request(0, 0)

    @pl.when(b + 1 < requests)
    def _():
        start_request(b + 1, 1 - slot)

    def wait_body(p, carry):
        pltpu.make_async_copy(shared_hbm.at[0], kv.at[slot, p], sem.at[slot]).wait()
        return carry

    lax.fori_loop(0, page_count, wait_body, 0)

    root_span = meta[b, 0]
    mid_span = meta[b, 1]
    leaf_span = meta[b, 2]
    context = meta[b, 3]
    q = q_ref[0]
    rows = q.shape[0]
    query_pos = context + (lax.broadcasted_iota(jnp.int32, (rows, 1), 0) % width)
    lanes = lax.broadcasted_iota(jnp.int32, (1, span), 1)
    scale = HD ** (-0.5)

    def masked(s, key_pos, present):
        distance = query_pos - key_pos
        allowed = present & (distance >= 0) & (distance < WINDOW)
        return jnp.where(allowed, s, masked_score)

    def geometry(c):
        page = group * c
        in_root = page < ROOT_PAGES
        in_mid = page < shared_count
        first = jnp.where(
            in_root, page * width, jnp.where(in_mid, (page - ROOT_PAGES) * width, (page - shared_count) * width)
        )
        base = jnp.where(in_root, 0, jnp.where(in_mid, root_span, root_span + mid_span))
        limit = jnp.where(in_root, root_span, jnp.where(in_mid, mid_span, leaf_span))
        return first, base, limit

    def pages_of(c, part):
        return jnp.concatenate([kv[slot, group * c + k, part] for k in range(group)], 1)

    fresh_lanes = lax.broadcasted_iota(jnp.int32, (1, width), 1)
    fresh_scores = masked(
        jnp.dot(q, fresh_ref[0, 0], preferred_element_type=jnp.float32) * scale,
        context + fresh_lanes,
        fresh_lanes >= 0,
    )
    fresh_sc[...] = fresh_scores
    top[...] = fresh_scores

    def keep(c, s):
        sc[c] = s
        m = top[...]
        for k in range(group):
            m = jnp.maximum(m, s[:, k * width:(k + 1) * width])
        top[...] = m

    def max_body(c, carry):
        first, base, limit = geometry(c)
        live = (first < limit) & (context - (base + first + span - 1) < WINDOW)
        full = (first + span <= limit) & (context + width - 1 - (base + first) < WINDOW)

        @pl.when(full)
        def _():
            keep(c, jnp.dot(q, pages_of(c, 0), preferred_element_type=jnp.float32) * scale)

        @pl.when(live & jnp.logical_not(full))
        def _():
            steps_in = first + lanes
            s = jnp.dot(q, pages_of(c, 0), preferred_element_type=jnp.float32) * scale
            keep(c, masked(s, base + steps_in, steps_in < limit))

        return carry

    chunks = page_count // group
    lax.fori_loop(0, chunks, max_body, 0)
    top[...] = jnp.broadcast_to(jnp.max(top[...], -1, keepdims=True), top.shape)
    row_top = top[...]

    fresh_w = jnp.exp(fresh_sc[...] - row_top)
    mass[...] = fresh_w
    acc[...] = lax.dot_general(
        fresh_w.astype(jnp.bfloat16), fresh_ref[0, 1], (((1,), (1,)), ((), ())), preferred_element_type=jnp.float32
    )

    def sum_body(c, carry):
        first, base, limit = geometry(c)
        live = (first < limit) & (context - (base + first + span - 1) < WINDOW)

        @pl.when(live)
        def _():
            s = sc[c]
            parts = [jnp.exp(s[:, k * width:(k + 1) * width] - row_top) for k in range(group)]
            total = mass[...]
            for part in parts:
                total = total + part
            mass[...] = total
            w = jnp.concatenate(parts, 1).astype(jnp.bfloat16)
            acc[...] = acc[...] + lax.dot_general(
                w, pages_of(c, 1), (((1,), (1,)), ((), ())), preferred_element_type=jnp.float32
            )

        return carry

    lax.fori_loop(0, chunks, sum_body, 0)
    totals = jnp.sum(mass[...], -1, keepdims=True)
    out_ref[0] = (acc[...] / totals).astype(out_ref.dtype)


def paged_attention(tbl, meta, queries, fresh, shared_store, leaf_store):
    reqs, rows, head = queries.shape
    page_shape = shared_store.shape[1:]
    width = page_shape[-1]
    pages = tbl.shape[1]
    keys_total = (pages + 1) * width
    grid_spec = pltpu.PrefetchScalarGridSpec(
        num_scalar_prefetch=2,
        grid=(reqs,),
        in_specs=[
            pl.BlockSpec((1, rows, head), lambda i, t, m: (i, 0, 0)),
            pl.BlockSpec((1,) + page_shape, lambda i, t, m: (i, 0, 0, 0)),
            pl.BlockSpec(memory_space=pl.ANY),
            pl.BlockSpec(memory_space=pl.ANY),
        ],
        out_specs=pl.BlockSpec((1, rows, head), lambda i, t, m: (i, 0, 0)),
        scratch_shapes=[
            pltpu.VMEM((2, pages) + page_shape, shared_store.dtype),
            pltpu.VMEM((pages // CHUNK_PAGES, rows, CHUNK_PAGES * width), jnp.float32),
            pltpu.VMEM((rows, width), jnp.float32),
            pltpu.VMEM((rows, width), jnp.float32),
            pltpu.VMEM((rows, width), jnp.float32),
            pltpu.VMEM((rows, head), jnp.float32),
            pltpu.SemaphoreType.DMA((2,)),
        ],
    )
    return pl.pallas_call(
        paged_kernel,
        grid_spec=grid_spec,
        out_shape=jax.ShapeDtypeStruct((reqs, rows, head), jnp.bfloat16),
        compiler_params=pltpu.CompilerParams(dimension_semantics=("arbitrary",)),
        cost_estimate=pl.CostEstimate(
            flops=4 * reqs * rows * keys_total * head,
            transcendentals=reqs * rows * keys_total,
            bytes_accessed=reqs * (pages + 1) * 2 * head * width * 2,
        ),
    )(tbl, meta, queries, fresh, shared_store, leaf_store)


def spans(request_ids, root_len, mid_len, leaf_len, mid_parent, leaf_parent):
    mid_nodes = leaf_parent[request_ids]
    root_nodes = mid_parent[mid_nodes]
    return (root_nodes, mid_nodes, root_len[root_nodes], mid_len[mid_nodes], leaf_len[request_ids])


def shards(
    hidden,
    gain_attn,
    w_query,
    w_key,
    w_value,
    w_out,
    gain_ffn,
    w_gate,
    w_up,
    w_down,
    shared_pages,
    leaf_pages,
    root_table,
    mid_table,
    leaf_table,
    root_len,
    mid_len,
    leaf_len,
    mid_parent,
    leaf_parent,
    slot_request,
):
    new_rows, local_reqs, model_width = hidden.shape
    seq_count = lax.axis_size("seq")
    seq_index = lax.axis_index("seq")
    kv_local = leaf_pages.shape[1]
    group_size = QH // KVH
    pages_here = leaf_pages.shape[0]
    slot_ids = seq_index * local_reqs + jnp.arange(local_reqs, dtype=jnp.int32)
    requests = slot_request[slot_ids]
    root_nodes, mid_nodes, root_span, mid_span, leaf_span = spans(
        requests, root_len, mid_len, leaf_len, mid_parent, leaf_parent
    )
    context = root_span + mid_span + leaf_span
    new_index = jnp.arange(new_rows, dtype=jnp.int32)
    query_pos = context[None, :] + new_index[:, None]
    all_slots = slot_request.reshape(seq_count, local_reqs)
    page_store = lax.all_gather(shared_pages, "seq", axis=0, tiled=True)
    root_index = root_table[root_nodes]
    mid_index = mid_table[mid_nodes]
    normed = rms_norm(hidden, gain_attn).reshape(-1, model_width)
    query_proj = jnp.dot(normed, w_query, preferred_element_type=jnp.float32).reshape(
        new_rows, local_reqs, -1, HD
    )
    queries = (
        rotate(query_proj, query_pos[:, :, None])
        .astype(jnp.bfloat16)
        .reshape(new_rows, local_reqs, kv_local, group_size, HD)
    )
    key_proj = jnp.dot(normed, w_key, preferred_element_type=jnp.float32).reshape(
        new_rows, local_reqs, kv_local, HD
    )
    new_keys = rotate(key_proj, query_pos[:, :, None]).astype(jnp.bfloat16)
    new_values = (
        jnp.dot(normed, w_value, preferred_element_type=jnp.float32)
        .astype(jnp.bfloat16)
        .reshape(new_rows, local_reqs, kv_local, HD)
    )
    home_of = leaf_table[:, 0] // pages_here
    own_homes = home_of[requests]
    sender_match = home_of[all_slots] == seq_index
    sender_pick = jnp.argmax(sender_match, 1)
    sender_have = jnp.any(sender_match, 1)
    picked_request = jnp.take_along_axis(all_slots, sender_pick[:, None], 1)[:, 0]
    page_ids = jnp.where(
        sender_have[:, None], leaf_table[picked_request] - seq_index * pages_here, 0
    )
    leaf_slots = leaf_table.shape[1]
    outgoing = jnp.take(leaf_pages, page_ids, axis=0)
    arrived = lax.all_to_all(outgoing, "seq", split_axis=0, concat_axis=0, tiled=True)
    page_shape = arrived.shape[-3:]
    leaf_store = arrived.reshape((-1,) + page_shape)
    shared_store = page_store.reshape((-1,) + page_shape)
    tbl = jnp.concatenate(
        [
            root_index,
            mid_index,
            own_homes[:, None] * leaf_slots + jnp.arange(leaf_slots, dtype=jnp.int32)[None, :],
        ],
        1,
    ).astype(jnp.int32)
    meta = jnp.stack([root_span, mid_span, leaf_span, context], 1).astype(jnp.int32)
    fresh_pack = jnp.stack(
        [jnp.transpose(new_keys[:, :, 0], (1, 2, 0)), jnp.transpose(new_values[:, :, 0], (1, 2, 0))], 1
    )
    query_rows = jnp.transpose(queries[:, :, 0], (1, 2, 0, 3)).reshape(local_reqs, -1, HD)
    attended = paged_attention(tbl, meta, query_rows, fresh_pack, shared_store, leaf_store)
    attended = (
        jnp.transpose(attended.reshape(local_reqs, group_size, new_rows, HD), (2, 0, 1, 3))
        .reshape(new_rows * local_reqs, -1)
    )
    tp_count = lax.axis_size("tp")
    own_count = new_rows // tp_count
    attn_proj = (
        lax.psum_scatter(
            jnp.dot(attended, w_out, preferred_element_type=jnp.float32).astype(jnp.bfloat16),
            "tp",
            scatter_dimension=0,
            tiled=True,
        )
        .astype(jnp.float32)
        .reshape(own_count, local_reqs, model_width)
    )
    own_hidden = lax.dynamic_slice_in_dim(hidden, lax.axis_index("tp") * own_count, own_count, 0)
    resid = own_hidden.astype(jnp.float32) + attn_proj
    normed_own = rms_norm(resid, gain_ffn).reshape(-1, model_width)
    normed_ffn = lax.all_gather(normed_own, "tp", axis=0, tiled=True)
    gate_rows = jnp.dot(normed_ffn, w_gate, preferred_element_type=jnp.float32)
    up_rows = jnp.dot(normed_ffn, w_up, preferred_element_type=jnp.float32)
    activated = (jax.nn.silu(gate_rows) * up_rows).astype(jnp.bfloat16)
    ffn_proj = (
        lax.psum_scatter(
            jnp.dot(activated, w_down, preferred_element_type=jnp.float32).astype(jnp.bfloat16),
            "tp",
            scatter_dimension=0,
            tiled=True,
        )
        .astype(jnp.float32)
        .reshape(own_count, local_reqs, model_width)
    )
    return resid + ffn_proj


def solution(mesh):
    return jax.shard_map(
        shards,
        mesh=mesh,
        in_specs=(
            P(None, "seq", None),
            P(),
            P(None, "tp"),
            P(None, "tp"),
            P(None, "tp"),
            P("tp", None),
            P(),
            P(None, "tp"),
            P(None, "tp"),
            P("tp", None),
            P("seq", "tp", None, None, None),
            P("seq", "tp", None, None, None),
            P(),
            P(),
            P(),
            P(),
            P(),
            P(),
            P(),
            P(),
            P(),
        ),
        out_specs=P("tp", "seq", None),
        check_vma=False,
    )
```

```python
import jax
import jax.numpy as jnp
from jax import lax
from jax.sharding import PartitionSpec as P
from jax.experimental import pallas as pl
from jax.experimental.pallas import tpu as pltpu

QH = 32
KVH = 8
HD = 80
WINDOW = 4096


masked_score = -1e30
rope_base = 10000.0


def rms_norm(row_data, gain_vector):
    values = row_data.astype(jnp.float32)
    inverse_rms = lax.rsqrt(jnp.mean(values * values, -1, keepdims=True) + 1e-05)
    return (values * inverse_rms * gain_vector.astype(jnp.float32)).astype(jnp.bfloat16)


def rotate(vector, position):
    half_size = vector.shape[-1] // 2
    frequency = rope_base ** (-2.0 * jnp.arange(half_size, dtype=jnp.float32) / vector.shape[-1])
    angles = position.astype(jnp.float32)[..., None] * frequency
    cos_part = jnp.cos(angles)
    sin_part = jnp.sin(angles)
    first_half = vector[..., :half_size]
    second_half = vector[..., half_size:]
    return jnp.concatenate(
        [
            first_half * cos_part - second_half * sin_part,
            second_half * cos_part + first_half * sin_part,
        ],
        -1,
    )


def page_columns(pages):
    moved = jnp.moveaxis(pages, -5, -2)
    return moved.reshape(moved.shape[:-2] + (moved.shape[-2] * moved.shape[-1],))


def attend(queries, key_pack, key_pos, present, query_pos):
    scores = jnp.einsum(
        "nbkge,bket->nbkgt", queries, key_pack[:, :, 0], preferred_element_type=jnp.float32
    ) * queries.shape[-1] ** (-0.5)
    distance = query_pos[:, :, None] - key_pos[None, :, :]
    allowed = (present[None, :, :] & (distance >= 0) & (distance < WINDOW))[:, :, None, None, :]
    scores = jnp.where(allowed, scores, masked_score)
    maximum = jnp.max(scores, -1)
    weights = jnp.where(allowed, jnp.exp(scores - maximum[..., None]), 0.0)
    totals = jnp.sum(weights, -1)
    weighted = jnp.einsum(
        "nbkgt,bket->nbkge",
        weights.astype(jnp.bfloat16),
        key_pack[:, :, 1],
        preferred_element_type=jnp.float32,
    )
    return (weighted, maximum, totals)


def merge_parts(first, second):
    maximum = jnp.maximum(first[1], second[1])
    first_scale = jnp.exp(first[1] - maximum)
    second_scale = jnp.exp(second[1] - maximum)
    return (
        first[0] * first_scale[..., None] + second[0] * second_scale[..., None],
        maximum,
        first[2] * first_scale + second[2] * second_scale,
    )


ROOT_PAGES = 16
MID_PAGES = 16
LEAF_SLOTS = 8
CHUNK_PAGES = 4


def part_body(chunk0, with_fresh, tbl, meta, q_ref, store_hbm, kv, sc, top, mass, acc, sem, begin, finish):
    b = pl.program_id(0)
    requests = pl.num_programs(0)
    slot = b % 2
    shared_count = ROOT_PAGES + MID_PAGES
    page_count = kv.shape[1]
    width = kv.shape[-1]
    group = CHUNK_PAGES
    span = group * width

    def start_request(j, into):
        def page_body(p, carry):
            pltpu.make_async_copy(store_hbm.at[tbl[j, p]], kv.at[into, p], sem.at[into]).start()
            return carry

        lax.fori_loop(0, page_count, page_body, 0)

    @pl.when(b == 0)
    def _():
        start_request(0, 0)

    @pl.when(b + 1 < requests)
    def _():
        start_request(b + 1, 1 - slot)

    def wait_body(p, carry):
        pltpu.make_async_copy(store_hbm.at[0], kv.at[slot, p], sem.at[slot]).wait()
        return carry

    lax.fori_loop(0, page_count, wait_body, 0)

    root_span = meta[b, 0]
    mid_span = meta[b, 1]
    leaf_span = meta[b, 2]
    context = meta[b, 3]
    q = q_ref[0]
    rows = q.shape[0]
    query_pos = context + (lax.broadcasted_iota(jnp.int32, (rows, 1), 0) % width)
    lanes = lax.broadcasted_iota(jnp.int32, (1, span), 1)
    scale = HD ** (-0.5)

    def masked(s, key_pos, present):
        distance = query_pos - key_pos
        allowed = present & (distance >= 0) & (distance < WINDOW)
        return jnp.where(allowed, s, masked_score)

    def geometry(c):
        page = group * (chunk0 + c)
        in_root = page < ROOT_PAGES
        in_mid = page < shared_count
        first = jnp.where(
            in_root, page * width, jnp.where(in_mid, (page - ROOT_PAGES) * width, (page - shared_count) * width)
        )
        base = jnp.where(in_root, 0, jnp.where(in_mid, root_span, root_span + mid_span))
        limit = jnp.where(in_root, root_span, jnp.where(in_mid, mid_span, leaf_span))
        live = (first < limit) & (context - (base + first + span - 1) < WINDOW)
        return first, base, limit, live

    def pages_of(c, part):
        return jnp.concatenate([kv[slot, group * c + k, part] for k in range(group)], 1)

    begin(q, query_pos, masked, scale)

    def keep(c, s):
        sc[c] = s
        m = top[...]
        for k in range(group):
            m = jnp.maximum(m, s[:, k * width:(k + 1) * width])
        top[...] = m

    def max_body(c, carry):
        first, base, limit, live = geometry(c)
        full = (first + span <= limit) & (context + width - 1 - (base + first) < WINDOW)

        @pl.when(full)
        def _():
            keep(c, jnp.dot(q, pages_of(c, 0), preferred_element_type=jnp.float32) * scale)

        @pl.when(live & jnp.logical_not(full))
        def _():
            steps_in = first + lanes
            s = jnp.dot(q, pages_of(c, 0), preferred_element_type=jnp.float32) * scale
            keep(c, masked(s, base + steps_in, steps_in < limit))

        return carry

    chunks = page_count // group
    lax.fori_loop(0, chunks, max_body, 0)
    earlier = top[...]
    top[...] = jnp.broadcast_to(jnp.max(earlier, -1, keepdims=True), top.shape)
    row_top = top[...]
    finish(row_top)

    def sum_body(c, carry):
        first, base, limit, live = geometry(c)

        @pl.when(live)
        def _():
            s = sc[c]
            parts = [jnp.exp(s[:, k * width:(k + 1) * width] - row_top) for k in range(group)]
            total = mass[...]
            for part in parts:
                total = total + part
            mass[...] = total
            w = jnp.concatenate(parts, 1).astype(jnp.bfloat16)
            acc[...] = acc[...] + lax.dot_general(
                w, pages_of(c, 1), (((1,), (1,)), ((), ())), preferred_element_type=jnp.float32
            )

        return carry

    lax.fori_loop(0, chunks, sum_body, 0)


def leaf_kernel(tbl, meta, q_ref, fresh_ref, store_hbm, acc_out, top_out, mass_out, kv, sc, fresh_sc, top, mass, acc, sem):
    def begin(q, query_pos, masked, scale):
        width = fresh_sc.shape[-1]
        fresh_lanes = lax.broadcasted_iota(jnp.int32, (1, width), 1)
        fresh_scores = masked(
            jnp.dot(q, fresh_ref[0, 0], preferred_element_type=jnp.float32) * scale,
            meta[pl.program_id(0), 3] + fresh_lanes,
            fresh_lanes >= 0,
        )
        fresh_sc[...] = fresh_scores
        top[...] = fresh_scores

    def finish(row_top):
        fresh_w = jnp.exp(fresh_sc[...] - row_top)
        mass[...] = fresh_w
        acc[...] = lax.dot_general(
            fresh_w.astype(jnp.bfloat16), fresh_ref[0, 1], (((1,), (1,)), ((), ())),
            preferred_element_type=jnp.float32,
        )

    part_body(
        (ROOT_PAGES + MID_PAGES) // CHUNK_PAGES, True, tbl, meta, q_ref, store_hbm, kv, sc, top, mass, acc, sem,
        begin, finish,
    )
    acc_out[0] = acc[...]
    top_out[0] = top[...]
    mass_out[0] = mass[...]


def shared_kernel(tbl, meta, q_ref, acc_in, top_in, mass_in, store_hbm, out_ref, kv, sc, top, mass, acc, sem):
    def begin(q, query_pos, masked, scale):
        top[...] = top_in[0]

    def finish(row_top):
        factor = jnp.exp(top_in[0] - row_top)
        mass[...] = mass_in[0] * factor
        acc[...] = acc_in[0] * factor[:, :1]

    part_body(0, False, tbl, meta, q_ref, store_hbm, kv, sc, top, mass, acc, sem, begin, finish)
    totals = jnp.sum(mass[...], -1, keepdims=True)
    out_ref[0] = (acc[...] / totals).astype(out_ref.dtype)


def part_call(kernel, tbl, meta, inputs, in_blocks, store, out_shapes):
    reqs, rows, head = inputs[0].shape
    page_shape = store.shape[1:]
    width = page_shape[-1]
    pages = tbl.shape[1]

    def block(shape):
        return pl.BlockSpec((1,) + shape[1:], lambda i, t, m: (i,) + (0,) * (len(shape) - 1))

    scratch = [
        pltpu.VMEM((2, pages) + page_shape, store.dtype),
        pltpu.VMEM((pages // CHUNK_PAGES, rows, CHUNK_PAGES * width), jnp.float32),
    ]
    if kernel is leaf_kernel:
        scratch.append(pltpu.VMEM((rows, width), jnp.float32))
    scratch += [
        pltpu.VMEM((rows, width), jnp.float32),
        pltpu.VMEM((rows, width), jnp.float32),
        pltpu.VMEM((rows, head), jnp.float32),
        pltpu.SemaphoreType.DMA((2,)),
    ]
    grid_spec = pltpu.PrefetchScalarGridSpec(
        num_scalar_prefetch=2,
        grid=(reqs,),
        in_specs=[block(x.shape) for x in inputs] + [pl.BlockSpec(memory_space=pl.ANY)],
        out_specs=[block(s.shape) for s in out_shapes],
        scratch_shapes=scratch,
    )
    keys_total = pages * width
    return pl.pallas_call(
        kernel,
        grid_spec=grid_spec,
        out_shape=out_shapes,
        compiler_params=pltpu.CompilerParams(dimension_semantics=("arbitrary",)),
        cost_estimate=pl.CostEstimate(
            flops=4 * reqs * rows * keys_total * head,
            transcendentals=reqs * rows * keys_total,
            bytes_accessed=reqs * pages * 2 * head * width * 2,
        ),
    )(tbl, meta, *inputs, store)


def paged_attention(tbl, meta, queries, fresh, shared_store, leaf_store):
    reqs, rows, head = queries.shape
    width = shared_store.shape[-1]
    shared_count = ROOT_PAGES + MID_PAGES
    state = part_call(
        leaf_kernel, tbl[:, shared_count:], meta, [queries, fresh], None, leaf_store,
        [
            jax.ShapeDtypeStruct((reqs, rows, head), jnp.float32),
            jax.ShapeDtypeStruct((reqs, rows, width), jnp.float32),
            jax.ShapeDtypeStruct((reqs, rows, width), jnp.float32),
        ],
    )
    (out,) = part_call(
        shared_kernel, tbl[:, :shared_count], meta, [queries] + list(state), None, shared_store,
        [jax.ShapeDtypeStruct((reqs, rows, head), jnp.bfloat16)],
    )
    return out


def spans(request_ids, root_len, mid_len, leaf_len, mid_parent, leaf_parent):
    mid_nodes = leaf_parent[request_ids]
    root_nodes = mid_parent[mid_nodes]
    return (root_nodes, mid_nodes, root_len[root_nodes], mid_len[mid_nodes], leaf_len[request_ids])


def shards(
    hidden,
    gain_attn,
    w_query,
    w_key,
    w_value,
    w_out,
    gain_ffn,
    w_gate,
    w_up,
    w_down,
    shared_pages,
    leaf_pages,
    root_table,
    mid_table,
    leaf_table,
    root_len,
    mid_len,
    leaf_len,
    mid_parent,
    leaf_parent,
    slot_request,
):
    new_rows, local_reqs, model_width = hidden.shape
    seq_count = lax.axis_size("seq")
    seq_index = lax.axis_index("seq")
    kv_local = leaf_pages.shape[1]
    group_size = QH // KVH
    pages_here = leaf_pages.shape[0]
    slot_ids = seq_index * local_reqs + jnp.arange(local_reqs, dtype=jnp.int32)
    requests = slot_request[slot_ids]
    root_nodes, mid_nodes, root_span, mid_span, leaf_span = spans(
        requests, root_len, mid_len, leaf_len, mid_parent, leaf_parent
    )
    context = root_span + mid_span + leaf_span
    new_index = jnp.arange(new_rows, dtype=jnp.int32)
    query_pos = context[None, :] + new_index[:, None]
    all_slots = slot_request.reshape(seq_count, local_reqs)
    page_store = lax.all_gather(shared_pages, "seq", axis=0, tiled=True)
    root_index = root_table[root_nodes]
    mid_index = mid_table[mid_nodes]
    normed = rms_norm(hidden, gain_attn).reshape(-1, model_width)
    query_proj = jnp.dot(normed, w_query, preferred_element_type=jnp.float32).reshape(
        new_rows, local_reqs, -1, HD
    )
    queries = (
        rotate(query_proj, query_pos[:, :, None])
        .astype(jnp.bfloat16)
        .reshape(new_rows, local_reqs, kv_local, group_size, HD)
    )
    key_proj = jnp.dot(normed, w_key, preferred_element_type=jnp.float32).reshape(
        new_rows, local_reqs, kv_local, HD
    )
    new_keys = rotate(key_proj, query_pos[:, :, None]).astype(jnp.bfloat16)
    new_values = (
        jnp.dot(normed, w_value, preferred_element_type=jnp.float32)
        .astype(jnp.bfloat16)
        .reshape(new_rows, local_reqs, kv_local, HD)
    )
    home_of = leaf_table[:, 0] // pages_here
    own_homes = home_of[requests]
    sender_match = home_of[all_slots] == seq_index
    sender_pick = jnp.argmax(sender_match, 1)
    sender_have = jnp.any(sender_match, 1)
    picked_request = jnp.take_along_axis(all_slots, sender_pick[:, None], 1)[:, 0]
    page_ids = jnp.where(
        sender_have[:, None], leaf_table[picked_request] - seq_index * pages_here, 0
    )
    leaf_slots = leaf_table.shape[1]
    outgoing = jnp.where(
        sender_have[:, None, None, None, None, None], jnp.take(leaf_pages, page_ids, axis=0), 0
    )
    arrived = lax.all_to_all(outgoing, "seq", split_axis=0, concat_axis=0, tiled=True)
    page_shape = arrived.shape[-3:]
    leaf_store = arrived.reshape((-1,) + page_shape)
    shared_store = page_store.reshape((-1,) + page_shape)
    tbl = jnp.concatenate(
        [
            root_index,
            mid_index,
            own_homes[:, None] * leaf_slots + jnp.arange(leaf_slots, dtype=jnp.int32)[None, :],
        ],
        1,
    ).astype(jnp.int32)
    meta = jnp.stack([root_span, mid_span, leaf_span, context], 1).astype(jnp.int32)
    fresh_pack = jnp.stack(
        [jnp.transpose(new_keys[:, :, 0], (1, 2, 0)), jnp.transpose(new_values[:, :, 0], (1, 2, 0))], 1
    )
    query_rows = jnp.transpose(queries[:, :, 0], (1, 2, 0, 3)).reshape(local_reqs, -1, HD)
    attended = paged_attention(tbl, meta, query_rows, fresh_pack, shared_store, leaf_store)
    attended = (
        jnp.transpose(attended.reshape(local_reqs, group_size, new_rows, HD), (2, 0, 1, 3))
        .reshape(new_rows * local_reqs, -1)
    )
    tp_count = lax.axis_size("tp")
    own_count = new_rows // tp_count
    attn_proj = (
        lax.psum_scatter(
            jnp.dot(attended, w_out, preferred_element_type=jnp.float32).astype(jnp.bfloat16),
            "tp",
            scatter_dimension=0,
            tiled=True,
        )
        .astype(jnp.float32)
        .reshape(own_count, local_reqs, model_width)
    )
    own_hidden = lax.dynamic_slice_in_dim(hidden, lax.axis_index("tp") * own_count, own_count, 0)
    resid = own_hidden.astype(jnp.float32) + attn_proj
    normed_own = rms_norm(resid, gain_ffn).reshape(-1, model_width)
    normed_ffn = lax.all_gather(normed_own, "tp", axis=0, tiled=True)
    gate_rows = jnp.dot(normed_ffn, w_gate, preferred_element_type=jnp.float32)
    up_rows = jnp.dot(normed_ffn, w_up, preferred_element_type=jnp.float32)
    activated = (jax.nn.silu(gate_rows) * up_rows).astype(jnp.bfloat16)
    ffn_proj = (
        lax.psum_scatter(
            jnp.dot(activated, w_down, preferred_element_type=jnp.float32).astype(jnp.bfloat16),
            "tp",
            scatter_dimension=0,
            tiled=True,
        )
        .astype(jnp.float32)
        .reshape(own_count, local_reqs, model_width)
    )
    return resid + ffn_proj


def solution(mesh):
    return jax.shard_map(
        shards,
        mesh=mesh,
        in_specs=(
            P(None, "seq", None),
            P(),
            P(None, "tp"),
            P(None, "tp"),
            P(None, "tp"),
            P("tp", None),
            P(),
            P(None, "tp"),
            P(None, "tp"),
            P("tp", None),
            P("seq", "tp", None, None, None),
            P("seq", "tp", None, None, None),
            P(),
            P(),
            P(),
            P(),
            P(),
            P(),
            P(),
            P(),
            P(),
        ),
        out_specs=P("tp", "seq", None),
        check_vma=False,
    )
```

```python
import jax
import jax.numpy as jnp
from jax import lax
from jax.sharding import PartitionSpec as P
from jax.experimental import pallas as pl
from jax.experimental.pallas import tpu as pltpu

QH = 32
KVH = 8
HD = 80
WINDOW = 4096


masked_score = -1e30
rope_base = 10000.0


def rms_norm(row_data, gain_vector):
    values = row_data.astype(jnp.float32)
    inverse_rms = lax.rsqrt(jnp.mean(values * values, -1, keepdims=True) + 1e-05)
    return (values * inverse_rms * gain_vector.astype(jnp.float32)).astype(jnp.bfloat16)


def rotate(vector, position):
    half_size = vector.shape[-1] // 2
    frequency = rope_base ** (-2.0 * jnp.arange(half_size, dtype=jnp.float32) / vector.shape[-1])
    angles = position.astype(jnp.float32)[..., None] * frequency
    cos_part = jnp.cos(angles)
    sin_part = jnp.sin(angles)
    first_half = vector[..., :half_size]
    second_half = vector[..., half_size:]
    return jnp.concatenate(
        [
            first_half * cos_part - second_half * sin_part,
            second_half * cos_part + first_half * sin_part,
        ],
        -1,
    )


def page_columns(pages):
    moved = jnp.moveaxis(pages, -5, -2)
    return moved.reshape(moved.shape[:-2] + (moved.shape[-2] * moved.shape[-1],))


def attend(queries, key_pack, key_pos, present, query_pos):
    scores = jnp.einsum(
        "nbkge,bket->nbkgt", queries, key_pack[:, :, 0], preferred_element_type=jnp.float32
    ) * queries.shape[-1] ** (-0.5)
    distance = query_pos[:, :, None] - key_pos[None, :, :]
    allowed = (present[None, :, :] & (distance >= 0) & (distance < WINDOW))[:, :, None, None, :]
    scores = jnp.where(allowed, scores, masked_score)
    maximum = jnp.max(scores, -1)
    weights = jnp.where(allowed, jnp.exp(scores - maximum[..., None]), 0.0)
    totals = jnp.sum(weights, -1)
    weighted = jnp.einsum(
        "nbkgt,bket->nbkge",
        weights.astype(jnp.bfloat16),
        key_pack[:, :, 1],
        preferred_element_type=jnp.float32,
    )
    return (weighted, maximum, totals)


def merge_parts(first, second):
    maximum = jnp.maximum(first[1], second[1])
    first_scale = jnp.exp(first[1] - maximum)
    second_scale = jnp.exp(second[1] - maximum)
    return (
        first[0] * first_scale[..., None] + second[0] * second_scale[..., None],
        maximum,
        first[2] * first_scale + second[2] * second_scale,
    )


ROOT_PAGES = 16
MID_PAGES = 16
LEAF_SLOTS = 8
CHUNK_PAGES = 4


def part_body(chunk0, with_fresh, tbl, meta, q_ref, store_hbm, kv, sc, top, mass, acc, sem, begin, finish):
    b = pl.program_id(0)
    requests = pl.num_programs(0)
    slot = b % 2
    shared_count = ROOT_PAGES + MID_PAGES
    page_count = kv.shape[1]
    width = kv.shape[-1]
    group = CHUNK_PAGES
    span = group * width

    def start_request(j, into):
        def page_body(p, carry):
            pltpu.make_async_copy(store_hbm.at[tbl[j, p]], kv.at[into, p], sem.at[into]).start()
            return carry

        lax.fori_loop(0, page_count, page_body, 0)

    @pl.when(b == 0)
    def _():
        start_request(0, 0)

    @pl.when(b + 1 < requests)
    def _():
        start_request(b + 1, 1 - slot)

    def wait_body(p, carry):
        pltpu.make_async_copy(store_hbm.at[0], kv.at[slot, p], sem.at[slot]).wait()
        return carry

    lax.fori_loop(0, page_count, wait_body, 0)

    root_span = meta[b, 0]
    mid_span = meta[b, 1]
    leaf_span = meta[b, 2]
    context = meta[b, 3]
    q = q_ref[0]
    rows = q.shape[0]
    query_pos = context + (lax.broadcasted_iota(jnp.int32, (rows, 1), 0) % width)
    lanes = lax.broadcasted_iota(jnp.int32, (1, span), 1)
    scale = HD ** (-0.5)

    def masked(s, key_pos, present):
        distance = query_pos - key_pos
        allowed = present & (distance >= 0) & (distance < WINDOW)
        return jnp.where(allowed, s, masked_score)

    def geometry(c):
        page = group * (chunk0 + c)
        in_root = page < ROOT_PAGES
        in_mid = page < shared_count
        first = jnp.where(
            in_root, page * width, jnp.where(in_mid, (page - ROOT_PAGES) * width, (page - shared_count) * width)
        )
        base = jnp.where(in_root, 0, jnp.where(in_mid, root_span, root_span + mid_span))
        limit = jnp.where(in_root, root_span, jnp.where(in_mid, mid_span, leaf_span))
        live = (first < limit) & (context - (base + first + span - 1) < WINDOW)
        return first, base, limit, live

    def pages_of(c, part):
        return jnp.concatenate([kv[slot, group * c + k, part] for k in range(group)], 1)

    begin(q, query_pos, masked, scale)

    def keep(c, s):
        sc[c] = s
        m = top[...]
        for k in range(group):
            m = jnp.maximum(m, s[:, k * width:(k + 1) * width])
        top[...] = m

    def max_body(c, carry):
        first, base, limit, live = geometry(c)
        full = (first + span <= limit) & (context + width - 1 - (base + first) < WINDOW)

        @pl.when(full)
        def _():
            keep(c, jnp.dot(q, pages_of(c, 0), preferred_element_type=jnp.float32) * scale)

        @pl.when(live & jnp.logical_not(full))
        def _():
            steps_in = first + lanes
            s = jnp.dot(q, pages_of(c, 0), preferred_element_type=jnp.float32) * scale
            keep(c, masked(s, base + steps_in, steps_in < limit))

        return carry

    chunks = page_count // group
    lax.fori_loop(0, chunks, max_body, 0)
    earlier = top[...]
    top[...] = jnp.broadcast_to(jnp.max(earlier, -1, keepdims=True), top.shape)
    row_top = top[...]
    finish(row_top)

    def sum_body(c, carry):
        first, base, limit, live = geometry(c)

        @pl.when(live)
        def _():
            s = sc[c]
            parts = [jnp.exp(s[:, k * width:(k + 1) * width] - row_top) for k in range(group)]
            total = mass[...]
            for part in parts:
                total = total + part
            mass[...] = total
            w = jnp.concatenate(parts, 1).astype(jnp.bfloat16)
            acc[...] = acc[...] + lax.dot_general(
                w, pages_of(c, 1), (((1,), (1,)), ((), ())), preferred_element_type=jnp.float32
            )

        return carry

    lax.fori_loop(0, chunks, sum_body, 0)


def leaf_kernel(tbl, meta, q_ref, fresh_ref, store_hbm, acc_out, top_out, mass_out, kv, sc, fresh_sc, top, mass, acc, sem):
    def begin(q, query_pos, masked, scale):
        width = fresh_sc.shape[-1]
        fresh_lanes = lax.broadcasted_iota(jnp.int32, (1, width), 1)
        fresh_scores = masked(
            jnp.dot(q, fresh_ref[0, 0], preferred_element_type=jnp.float32) * scale,
            meta[pl.program_id(0), 3] + fresh_lanes,
            fresh_lanes >= 0,
        )
        fresh_sc[...] = fresh_scores
        top[...] = fresh_scores

    def finish(row_top):
        fresh_w = jnp.exp(fresh_sc[...] - row_top)
        mass[...] = fresh_w
        acc[...] = lax.dot_general(
            fresh_w.astype(jnp.bfloat16), fresh_ref[0, 1], (((1,), (1,)), ((), ())),
            preferred_element_type=jnp.float32,
        )

    part_body(
        (ROOT_PAGES + MID_PAGES) // CHUNK_PAGES, True, tbl, meta, q_ref, store_hbm, kv, sc, top, mass, acc, sem,
        begin, finish,
    )
    acc_out[0] = acc[...]
    top_out[0] = top[...]
    mass_out[0] = mass[...]


def shared_kernel(tbl, meta, q_ref, acc_in, top_in, mass_in, store_hbm, out_ref, kv, sc, top, mass, acc, sem):
    def begin(q, query_pos, masked, scale):
        top[...] = top_in[0]

    def finish(row_top):
        factor = jnp.exp(top_in[0] - row_top)
        mass[...] = mass_in[0] * factor
        acc[...] = acc_in[0] * factor[:, :1]

    part_body(0, False, tbl, meta, q_ref, store_hbm, kv, sc, top, mass, acc, sem, begin, finish)
    totals = jnp.sum(mass[...], -1, keepdims=True)
    out_ref[0] = (acc[...] / totals).astype(out_ref.dtype)


def part_call(kernel, tbl, meta, inputs, in_blocks, store, out_shapes):
    reqs, rows, head = inputs[0].shape
    page_shape = store.shape[1:]
    width = page_shape[-1]
    pages = tbl.shape[1]

    def block(shape):
        return pl.BlockSpec((1,) + shape[1:], lambda i, t, m: (i,) + (0,) * (len(shape) - 1))

    scratch = [
        pltpu.VMEM((2, pages) + page_shape, store.dtype),
        pltpu.VMEM((pages // CHUNK_PAGES, rows, CHUNK_PAGES * width), jnp.float32),
    ]
    if kernel is leaf_kernel:
        scratch.append(pltpu.VMEM((rows, width), jnp.float32))
    scratch += [
        pltpu.VMEM((rows, width), jnp.float32),
        pltpu.VMEM((rows, width), jnp.float32),
        pltpu.VMEM((rows, head), jnp.float32),
        pltpu.SemaphoreType.DMA((2,)),
    ]
    grid_spec = pltpu.PrefetchScalarGridSpec(
        num_scalar_prefetch=2,
        grid=(reqs,),
        in_specs=[block(x.shape) for x in inputs] + [pl.BlockSpec(memory_space=pl.ANY)],
        out_specs=[block(s.shape) for s in out_shapes],
        scratch_shapes=scratch,
    )
    keys_total = pages * width
    return pl.pallas_call(
        kernel,
        grid_spec=grid_spec,
        out_shape=out_shapes,
        compiler_params=pltpu.CompilerParams(dimension_semantics=("arbitrary",)),
        cost_estimate=pl.CostEstimate(
            flops=4 * reqs * rows * keys_total * head,
            transcendentals=reqs * rows * keys_total,
            bytes_accessed=reqs * pages * 2 * head * width * 2,
        ),
    )(tbl, meta, *inputs, store)


def paged_attention(tbl, meta, queries, fresh, shared_store, leaf_store):
    reqs, rows, head = queries.shape
    width = shared_store.shape[-1]
    shared_count = ROOT_PAGES + MID_PAGES
    state = part_call(
        leaf_kernel, tbl[:, shared_count:], meta, [queries, fresh], None, leaf_store,
        [
            jax.ShapeDtypeStruct((reqs, rows, head), jnp.float32),
            jax.ShapeDtypeStruct((reqs, rows, width), jnp.float32),
            jax.ShapeDtypeStruct((reqs, rows, width), jnp.float32),
        ],
    )
    (out,) = part_call(
        shared_kernel, tbl[:, :shared_count], meta, [queries] + list(state), None, shared_store,
        [jax.ShapeDtypeStruct((reqs, rows, head), jnp.bfloat16)],
    )
    return out


def tp_row_sum(partial):
    count = lax.axis_size("tp")
    blocks = partial.astype(jnp.bfloat16).reshape((count, -1) + partial.shape[1:])
    arrived = lax.all_to_all(blocks, "tp", 0, 0, tiled=True)
    return jnp.sum(arrived.astype(jnp.float32), 0)


def spans(request_ids, root_len, mid_len, leaf_len, mid_parent, leaf_parent):
    mid_nodes = leaf_parent[request_ids]
    root_nodes = mid_parent[mid_nodes]
    return (root_nodes, mid_nodes, root_len[root_nodes], mid_len[mid_nodes], leaf_len[request_ids])


def shards(
    hidden,
    gain_attn,
    w_query,
    w_key,
    w_value,
    w_out,
    gain_ffn,
    w_gate,
    w_up,
    w_down,
    shared_pages,
    leaf_pages,
    root_table,
    mid_table,
    leaf_table,
    root_len,
    mid_len,
    leaf_len,
    mid_parent,
    leaf_parent,
    slot_request,
):
    new_rows, local_reqs, model_width = hidden.shape
    seq_count = lax.axis_size("seq")
    seq_index = lax.axis_index("seq")
    kv_local = leaf_pages.shape[1]
    group_size = QH // KVH
    pages_here = leaf_pages.shape[0]
    slot_ids = seq_index * local_reqs + jnp.arange(local_reqs, dtype=jnp.int32)
    requests = slot_request[slot_ids]
    root_nodes, mid_nodes, root_span, mid_span, leaf_span = spans(
        requests, root_len, mid_len, leaf_len, mid_parent, leaf_parent
    )
    context = root_span + mid_span + leaf_span
    new_index = jnp.arange(new_rows, dtype=jnp.int32)
    query_pos = context[None, :] + new_index[:, None]
    all_slots = slot_request.reshape(seq_count, local_reqs)
    page_store = lax.all_gather(shared_pages, "seq", axis=0, tiled=True)
    root_index = root_table[root_nodes]
    mid_index = mid_table[mid_nodes]
    normed = rms_norm(hidden, gain_attn).reshape(-1, model_width)
    query_proj = jnp.dot(normed, w_query, preferred_element_type=jnp.float32).reshape(
        new_rows, local_reqs, -1, HD
    )
    queries = (
        rotate(query_proj, query_pos[:, :, None])
        .astype(jnp.bfloat16)
        .reshape(new_rows, local_reqs, kv_local, group_size, HD)
    )
    key_proj = jnp.dot(normed, w_key, preferred_element_type=jnp.float32).reshape(
        new_rows, local_reqs, kv_local, HD
    )
    new_keys = rotate(key_proj, query_pos[:, :, None]).astype(jnp.bfloat16)
    new_values = (
        jnp.dot(normed, w_value, preferred_element_type=jnp.float32)
        .astype(jnp.bfloat16)
        .reshape(new_rows, local_reqs, kv_local, HD)
    )
    home_of = leaf_table[:, 0] // pages_here
    own_homes = home_of[requests]
    sender_match = home_of[all_slots] == seq_index
    sender_pick = jnp.argmax(sender_match, 1)
    sender_have = jnp.any(sender_match, 1)
    picked_request = jnp.take_along_axis(all_slots, sender_pick[:, None], 1)[:, 0]
    page_ids = jnp.where(
        sender_have[:, None], leaf_table[picked_request] - seq_index * pages_here, 0
    )
    leaf_slots = leaf_table.shape[1]
    outgoing = jnp.where(
        sender_have[:, None, None, None, None, None], jnp.take(leaf_pages, page_ids, axis=0), 0
    )
    arrived = lax.all_to_all(outgoing, "seq", split_axis=0, concat_axis=0, tiled=True)
    page_shape = arrived.shape[-3:]
    leaf_store = arrived.reshape((-1,) + page_shape)
    shared_store = page_store.reshape((-1,) + page_shape)
    tbl = jnp.concatenate(
        [
            root_index,
            mid_index,
            own_homes[:, None] * leaf_slots + jnp.arange(leaf_slots, dtype=jnp.int32)[None, :],
        ],
        1,
    ).astype(jnp.int32)
    meta = jnp.stack([root_span, mid_span, leaf_span, context], 1).astype(jnp.int32)
    fresh_pack = jnp.stack(
        [jnp.transpose(new_keys[:, :, 0], (1, 2, 0)), jnp.transpose(new_values[:, :, 0], (1, 2, 0))], 1
    )
    query_rows = jnp.transpose(queries[:, :, 0], (1, 2, 0, 3)).reshape(local_reqs, -1, HD)
    attended = paged_attention(tbl, meta, query_rows, fresh_pack, shared_store, leaf_store)
    attended = (
        jnp.transpose(attended.reshape(local_reqs, group_size, new_rows, HD), (2, 0, 1, 3))
        .reshape(new_rows * local_reqs, -1)
    )
    tp_count = lax.axis_size("tp")
    own_count = new_rows // tp_count
    attn_proj = tp_row_sum(jnp.dot(attended, w_out, preferred_element_type=jnp.float32)).reshape(
        own_count, local_reqs, model_width
    )
    own_hidden = lax.dynamic_slice_in_dim(hidden, lax.axis_index("tp") * own_count, own_count, 0)
    resid = own_hidden.astype(jnp.float32) + attn_proj
    normed_own = rms_norm(resid, gain_ffn).reshape(-1, model_width)
    normed_ffn = lax.all_gather(normed_own, "tp", axis=0, tiled=True)
    gate_rows = jnp.dot(normed_ffn, w_gate, preferred_element_type=jnp.float32)
    up_rows = jnp.dot(normed_ffn, w_up, preferred_element_type=jnp.float32)
    activated = (jax.nn.silu(gate_rows) * up_rows).astype(jnp.bfloat16)
    ffn_proj = tp_row_sum(jnp.dot(activated, w_down, preferred_element_type=jnp.float32)).reshape(
        own_count, local_reqs, model_width
    )
    return resid + ffn_proj


def solution(mesh):
    return jax.shard_map(
        shards,
        mesh=mesh,
        in_specs=(
            P(None, "seq", None),
            P(),
            P(None, "tp"),
            P(None, "tp"),
            P(None, "tp"),
            P("tp", None),
            P(),
            P(None, "tp"),
            P(None, "tp"),
            P("tp", None),
            P("seq", "tp", None, None, None),
            P("seq", "tp", None, None, None),
            P(),
            P(),
            P(),
            P(),
            P(),
            P(),
            P(),
            P(),
            P(),
        ),
        out_specs=P("tp", "seq", None),
        check_vma=False,
    )
```

```python
import jax
import jax.numpy as jnp
from jax import lax
from jax.sharding import PartitionSpec as P
from jax.experimental import pallas as pl
from jax.experimental.pallas import tpu as pltpu

QH = 32
KVH = 8
HD = 80
WINDOW = 4096


masked_score = -1e30
rope_base = 10000.0


def rms_norm(row_data, gain_vector):
    values = row_data.astype(jnp.float32)
    inverse_rms = lax.rsqrt(jnp.mean(values * values, -1, keepdims=True) + 1e-05)
    return (values * inverse_rms * gain_vector.astype(jnp.float32)).astype(jnp.bfloat16)


def rotate(vector, position):
    half_size = vector.shape[-1] // 2
    frequency = rope_base ** (-2.0 * jnp.arange(half_size, dtype=jnp.float32) / vector.shape[-1])
    angles = position.astype(jnp.float32)[..., None] * frequency
    cos_part = jnp.cos(angles)
    sin_part = jnp.sin(angles)
    first_half = vector[..., :half_size]
    second_half = vector[..., half_size:]
    return jnp.concatenate(
        [
            first_half * cos_part - second_half * sin_part,
            second_half * cos_part + first_half * sin_part,
        ],
        -1,
    )


def page_columns(pages):
    moved = jnp.moveaxis(pages, -5, -2)
    return moved.reshape(moved.shape[:-2] + (moved.shape[-2] * moved.shape[-1],))


def attend(queries, key_pack, key_pos, present, query_pos):
    scores = jnp.einsum(
        "nbkge,bket->nbkgt", queries, key_pack[:, :, 0], preferred_element_type=jnp.float32
    ) * queries.shape[-1] ** (-0.5)
    distance = query_pos[:, :, None] - key_pos[None, :, :]
    allowed = (present[None, :, :] & (distance >= 0) & (distance < WINDOW))[:, :, None, None, :]
    scores = jnp.where(allowed, scores, masked_score)
    maximum = jnp.max(scores, -1)
    weights = jnp.where(allowed, jnp.exp(scores - maximum[..., None]), 0.0)
    totals = jnp.sum(weights, -1)
    weighted = jnp.einsum(
        "nbkgt,bket->nbkge",
        weights.astype(jnp.bfloat16),
        key_pack[:, :, 1],
        preferred_element_type=jnp.float32,
    )
    return (weighted, maximum, totals)


def merge_parts(first, second):
    maximum = jnp.maximum(first[1], second[1])
    first_scale = jnp.exp(first[1] - maximum)
    second_scale = jnp.exp(second[1] - maximum)
    return (
        first[0] * first_scale[..., None] + second[0] * second_scale[..., None],
        maximum,
        first[2] * first_scale + second[2] * second_scale,
    )


ROOT_PAGES = 16
MID_PAGES = 16
LEAF_SLOTS = 8
CHUNK_PAGES = 4


def part_body(chunk0, with_fresh, tbl, meta, q_ref, store_hbm, kv, sc, top, mass, acc, sem, begin, finish):
    b = pl.program_id(0)
    requests = pl.num_programs(0)
    slot = b % 2
    shared_count = ROOT_PAGES + MID_PAGES
    page_count = kv.shape[1]
    width = kv.shape[-1]
    group = CHUNK_PAGES
    span = group * width

    def start_request(j, into):
        def page_body(p, carry):
            pltpu.make_async_copy(store_hbm.at[tbl[j, p]], kv.at[into, p], sem.at[into]).start()
            return carry

        lax.fori_loop(0, page_count, page_body, 0)

    @pl.when(b == 0)
    def _():
        start_request(0, 0)

    @pl.when(b + 1 < requests)
    def _():
        start_request(b + 1, 1 - slot)

    def wait_body(p, carry):
        pltpu.make_async_copy(store_hbm.at[0], kv.at[slot, p], sem.at[slot]).wait()
        return carry

    lax.fori_loop(0, page_count, wait_body, 0)

    root_span = meta[b, 0]
    mid_span = meta[b, 1]
    leaf_span = meta[b, 2]
    context = meta[b, 3]
    q = q_ref[0]
    rows = q.shape[0]
    query_pos = context + (lax.broadcasted_iota(jnp.int32, (rows, 1), 0) % width)
    lanes = lax.broadcasted_iota(jnp.int32, (1, span), 1)
    scale = HD ** (-0.5)

    def masked(s, key_pos, present):
        distance = query_pos - key_pos
        allowed = present & (distance >= 0) & (distance < WINDOW)
        return jnp.where(allowed, s, masked_score)

    def geometry(c):
        page = group * (chunk0 + c)
        in_root = page < ROOT_PAGES
        in_mid = page < shared_count
        first = jnp.where(
            in_root, page * width, jnp.where(in_mid, (page - ROOT_PAGES) * width, (page - shared_count) * width)
        )
        base = jnp.where(in_root, 0, jnp.where(in_mid, root_span, root_span + mid_span))
        limit = jnp.where(in_root, root_span, jnp.where(in_mid, mid_span, leaf_span))
        live = (first < limit) & (context - (base + first + span - 1) < WINDOW)
        return first, base, limit, live

    def pages_of(c, part):
        return jnp.concatenate([kv[slot, group * c + k, part] for k in range(group)], 1)

    begin(q, query_pos, masked, scale)

    def keep(c, s):
        sc[c] = s
        m = top[...]
        for k in range(group):
            m = jnp.maximum(m, s[:, k * width:(k + 1) * width])
        top[...] = m

    def max_body(c, carry):
        first, base, limit, live = geometry(c)
        full = (first + span <= limit) & (context + width - 1 - (base + first) < WINDOW)

        @pl.when(full)
        def _():
            keep(c, jnp.dot(q, pages_of(c, 0), preferred_element_type=jnp.float32) * scale)

        @pl.when(live & jnp.logical_not(full))
        def _():
            steps_in = first + lanes
            s = jnp.dot(q, pages_of(c, 0), preferred_element_type=jnp.float32) * scale
            keep(c, masked(s, base + steps_in, steps_in < limit))

        return carry

    chunks = page_count // group
    lax.fori_loop(0, chunks, max_body, 0)
    earlier = top[...]
    top[...] = jnp.broadcast_to(jnp.max(earlier, -1, keepdims=True), top.shape)
    row_top = top[...]
    finish(row_top)

    def sum_body(c, carry):
        first, base, limit, live = geometry(c)

        @pl.when(live)
        def _():
            s = sc[c]
            parts = [jnp.exp(s[:, k * width:(k + 1) * width] - row_top) for k in range(group)]
            total = mass[...]
            for part in parts:
                total = total + part
            mass[...] = total
            w = jnp.concatenate(parts, 1).astype(jnp.bfloat16)
            acc[...] = acc[...] + lax.dot_general(
                w, pages_of(c, 1), (((1,), (1,)), ((), ())), preferred_element_type=jnp.float32
            )

        return carry

    lax.fori_loop(0, chunks, sum_body, 0)


def leaf_kernel(tbl, meta, q_ref, fresh_ref, store_hbm, acc_out, top_out, mass_out, kv, sc, fresh_sc, top, mass, acc, sem):
    def begin(q, query_pos, masked, scale):
        width = fresh_sc.shape[-1]
        fresh_lanes = lax.broadcasted_iota(jnp.int32, (1, width), 1)
        fresh_scores = masked(
            jnp.dot(q, fresh_ref[0, 0], preferred_element_type=jnp.float32) * scale,
            meta[pl.program_id(0), 3] + fresh_lanes,
            fresh_lanes >= 0,
        )
        fresh_sc[...] = fresh_scores
        top[...] = fresh_scores

    def finish(row_top):
        fresh_w = jnp.exp(fresh_sc[...] - row_top)
        mass[...] = fresh_w
        acc[...] = lax.dot_general(
            fresh_w.astype(jnp.bfloat16), fresh_ref[0, 1], (((1,), (1,)), ((), ())),
            preferred_element_type=jnp.float32,
        )

    part_body(
        (ROOT_PAGES + MID_PAGES) // CHUNK_PAGES, True, tbl, meta, q_ref, store_hbm, kv, sc, top, mass, acc, sem,
        begin, finish,
    )
    acc_out[0] = acc[...]
    top_out[0] = top[...]
    mass_out[0] = mass[...]


def shared_kernel(tbl, meta, q_ref, acc_in, top_in, mass_in, store_hbm, out_ref, kv, sc, top, mass, acc, sem):
    def begin(q, query_pos, masked, scale):
        top[...] = top_in[0]

    def finish(row_top):
        factor = jnp.exp(top_in[0] - row_top)
        mass[...] = mass_in[0] * factor
        acc[...] = acc_in[0] * factor[:, :1]

    part_body(0, False, tbl, meta, q_ref, store_hbm, kv, sc, top, mass, acc, sem, begin, finish)
    totals = jnp.sum(mass[...], -1, keepdims=True)
    out_ref[0] = (acc[...] / totals).astype(out_ref.dtype)


def part_call(kernel, tbl, meta, inputs, in_blocks, store, out_shapes):
    reqs, rows, head = inputs[0].shape
    page_shape = store.shape[1:]
    width = page_shape[-1]
    pages = tbl.shape[1]

    def block(shape):
        return pl.BlockSpec((1,) + shape[1:], lambda i, t, m: (i,) + (0,) * (len(shape) - 1))

    scratch = [
        pltpu.VMEM((2, pages) + page_shape, store.dtype),
        pltpu.VMEM((pages // CHUNK_PAGES, rows, CHUNK_PAGES * width), jnp.float32),
    ]
    if kernel is leaf_kernel:
        scratch.append(pltpu.VMEM((rows, width), jnp.float32))
    scratch += [
        pltpu.VMEM((rows, width), jnp.float32),
        pltpu.VMEM((rows, width), jnp.float32),
        pltpu.VMEM((rows, head), jnp.float32),
        pltpu.SemaphoreType.DMA((2,)),
    ]
    grid_spec = pltpu.PrefetchScalarGridSpec(
        num_scalar_prefetch=2,
        grid=(reqs,),
        in_specs=[block(x.shape) for x in inputs] + [pl.BlockSpec(memory_space=pl.ANY)],
        out_specs=[block(s.shape) for s in out_shapes],
        scratch_shapes=scratch,
    )
    keys_total = pages * width
    return pl.pallas_call(
        kernel,
        grid_spec=grid_spec,
        out_shape=out_shapes,
        compiler_params=pltpu.CompilerParams(dimension_semantics=("arbitrary",)),
        cost_estimate=pl.CostEstimate(
            flops=4 * reqs * rows * keys_total * head,
            transcendentals=reqs * rows * keys_total,
            bytes_accessed=reqs * pages * 2 * head * width * 2,
        ),
    )(tbl, meta, *inputs, store)


def paged_attention(tbl, meta, queries, fresh, shared_store, leaf_store):
    reqs, rows, head = queries.shape
    width = shared_store.shape[-1]
    shared_count = ROOT_PAGES + MID_PAGES
    state = part_call(
        leaf_kernel, tbl[:, shared_count:], meta, [queries, fresh], None, leaf_store,
        [
            jax.ShapeDtypeStruct((reqs, rows, head), jnp.float32),
            jax.ShapeDtypeStruct((reqs, rows, width), jnp.float32),
            jax.ShapeDtypeStruct((reqs, rows, width), jnp.float32),
        ],
    )
    (out,) = part_call(
        shared_kernel, tbl[:, :shared_count], meta, [queries] + list(state), None, shared_store,
        [jax.ShapeDtypeStruct((reqs, rows, head), jnp.bfloat16)],
    )
    return out


def tp_row_sum(partial):
    count = lax.axis_size("tp")
    blocks = partial.astype(jnp.bfloat16).reshape((count, -1) + partial.shape[1:])
    arrived = lax.all_to_all(blocks, "tp", 0, 0, tiled=True)
    return jnp.sum(arrived.astype(jnp.float32), 0)


def tp_streamed_sum(rows, weight):
    count = lax.axis_size("tp")
    me = lax.axis_index("tp")
    block = rows.shape[0] // count
    total = None
    for k in range(count):
        target = (me + k) % count
        part = jnp.dot(
            lax.dynamic_slice_in_dim(rows, target * block, block, 0), weight, preferred_element_type=jnp.float32
        ).astype(jnp.bfloat16)
        if k:
            part = lax.ppermute(part, "tp", [(d, (d + k) % count) for d in range(count)])
        part = part.astype(jnp.float32)
        total = part if total is None else total + part
    return total


def spans(request_ids, root_len, mid_len, leaf_len, mid_parent, leaf_parent):
    mid_nodes = leaf_parent[request_ids]
    root_nodes = mid_parent[mid_nodes]
    return (root_nodes, mid_nodes, root_len[root_nodes], mid_len[mid_nodes], leaf_len[request_ids])


def shards(
    hidden,
    gain_attn,
    w_query,
    w_key,
    w_value,
    w_out,
    gain_ffn,
    w_gate,
    w_up,
    w_down,
    shared_pages,
    leaf_pages,
    root_table,
    mid_table,
    leaf_table,
    root_len,
    mid_len,
    leaf_len,
    mid_parent,
    leaf_parent,
    slot_request,
):
    new_rows, local_reqs, model_width = hidden.shape
    seq_count = lax.axis_size("seq")
    seq_index = lax.axis_index("seq")
    kv_local = leaf_pages.shape[1]
    group_size = QH // KVH
    pages_here = leaf_pages.shape[0]
    slot_ids = seq_index * local_reqs + jnp.arange(local_reqs, dtype=jnp.int32)
    requests = slot_request[slot_ids]
    root_nodes, mid_nodes, root_span, mid_span, leaf_span = spans(
        requests, root_len, mid_len, leaf_len, mid_parent, leaf_parent
    )
    context = root_span + mid_span + leaf_span
    new_index = jnp.arange(new_rows, dtype=jnp.int32)
    query_pos = context[None, :] + new_index[:, None]
    all_slots = slot_request.reshape(seq_count, local_reqs)
    page_store = lax.all_gather(shared_pages, "seq", axis=0, tiled=True)
    root_index = root_table[root_nodes]
    mid_index = mid_table[mid_nodes]
    normed = rms_norm(hidden, gain_attn).reshape(-1, model_width)
    query_proj = jnp.dot(normed, w_query, preferred_element_type=jnp.float32).reshape(
        new_rows, local_reqs, -1, HD
    )
    queries = (
        rotate(query_proj, query_pos[:, :, None])
        .astype(jnp.bfloat16)
        .reshape(new_rows, local_reqs, kv_local, group_size, HD)
    )
    key_proj = jnp.dot(normed, w_key, preferred_element_type=jnp.float32).reshape(
        new_rows, local_reqs, kv_local, HD
    )
    new_keys = rotate(key_proj, query_pos[:, :, None]).astype(jnp.bfloat16)
    new_values = (
        jnp.dot(normed, w_value, preferred_element_type=jnp.float32)
        .astype(jnp.bfloat16)
        .reshape(new_rows, local_reqs, kv_local, HD)
    )
    home_of = leaf_table[:, 0] // pages_here
    own_homes = home_of[requests]
    sender_match = home_of[all_slots] == seq_index
    sender_pick = jnp.argmax(sender_match, 1)
    sender_have = jnp.any(sender_match, 1)
    picked_request = jnp.take_along_axis(all_slots, sender_pick[:, None], 1)[:, 0]
    page_ids = jnp.where(
        sender_have[:, None], leaf_table[picked_request] - seq_index * pages_here, 0
    )
    leaf_slots = leaf_table.shape[1]
    outgoing = jnp.where(
        sender_have[:, None, None, None, None, None], jnp.take(leaf_pages, page_ids, axis=0), 0
    )
    arrived = lax.all_to_all(outgoing, "seq", split_axis=0, concat_axis=0, tiled=True)
    page_shape = arrived.shape[-3:]
    leaf_store = arrived.reshape((-1,) + page_shape)
    shared_store = page_store.reshape((-1,) + page_shape)
    tbl = jnp.concatenate(
        [
            root_index,
            mid_index,
            own_homes[:, None] * leaf_slots + jnp.arange(leaf_slots, dtype=jnp.int32)[None, :],
        ],
        1,
    ).astype(jnp.int32)
    meta = jnp.stack([root_span, mid_span, leaf_span, context], 1).astype(jnp.int32)
    fresh_pack = jnp.stack(
        [jnp.transpose(new_keys[:, :, 0], (1, 2, 0)), jnp.transpose(new_values[:, :, 0], (1, 2, 0))], 1
    )
    query_rows = jnp.transpose(queries[:, :, 0], (1, 2, 0, 3)).reshape(local_reqs, -1, HD)
    attended = paged_attention(tbl, meta, query_rows, fresh_pack, shared_store, leaf_store)
    attended = (
        jnp.transpose(attended.reshape(local_reqs, group_size, new_rows, HD), (2, 0, 1, 3))
        .reshape(new_rows * local_reqs, -1)
    )
    tp_count = lax.axis_size("tp")
    own_count = new_rows // tp_count
    attn_proj = tp_row_sum(jnp.dot(attended, w_out, preferred_element_type=jnp.float32)).reshape(
        own_count, local_reqs, model_width
    )
    own_hidden = lax.dynamic_slice_in_dim(hidden, lax.axis_index("tp") * own_count, own_count, 0)
    resid = own_hidden.astype(jnp.float32) + attn_proj
    normed_own = rms_norm(resid, gain_ffn).reshape(-1, model_width)
    normed_ffn = lax.all_gather(normed_own, "tp", axis=0, tiled=True)
    gate_rows = jnp.dot(normed_ffn, w_gate, preferred_element_type=jnp.float32)
    up_rows = jnp.dot(normed_ffn, w_up, preferred_element_type=jnp.float32)
    activated = (jax.nn.silu(gate_rows) * up_rows).astype(jnp.bfloat16)
    ffn_proj = tp_streamed_sum(activated, w_down).reshape(own_count, local_reqs, model_width)
    return resid + ffn_proj


def solution(mesh):
    return jax.shard_map(
        shards,
        mesh=mesh,
        in_specs=(
            P(None, "seq", None),
            P(),
            P(None, "tp"),
            P(None, "tp"),
            P(None, "tp"),
            P("tp", None),
            P(),
            P(None, "tp"),
            P(None, "tp"),
            P("tp", None),
            P("seq", "tp", None, None, None),
            P("seq", "tp", None, None, None),
            P(),
            P(),
            P(),
            P(),
            P(),
            P(),
            P(),
            P(),
            P(),
        ),
        out_specs=P("tp", "seq", None),
        check_vma=False,
    )
```

```python
import jax
import jax.numpy as jnp
from jax import lax
from jax.sharding import PartitionSpec as P
from jax.experimental import pallas as pl
from jax.experimental.pallas import tpu as pltpu

QH = 32
KVH = 8
HD = 80
WINDOW = 4096


masked_score = -1e30
rope_base = 10000.0


def rms_norm(row_data, gain_vector):
    values = row_data.astype(jnp.float32)
    inverse_rms = lax.rsqrt(jnp.mean(values * values, -1, keepdims=True) + 1e-05)
    return (values * inverse_rms * gain_vector.astype(jnp.float32)).astype(jnp.bfloat16)


def rotate(vector, position):
    half_size = vector.shape[-1] // 2
    frequency = rope_base ** (-2.0 * jnp.arange(half_size, dtype=jnp.float32) / vector.shape[-1])
    angles = position.astype(jnp.float32)[..., None] * frequency
    cos_part = jnp.cos(angles)
    sin_part = jnp.sin(angles)
    first_half = vector[..., :half_size]
    second_half = vector[..., half_size:]
    return jnp.concatenate(
        [
            first_half * cos_part - second_half * sin_part,
            second_half * cos_part + first_half * sin_part,
        ],
        -1,
    )


def page_columns(pages):
    moved = jnp.moveaxis(pages, -5, -2)
    return moved.reshape(moved.shape[:-2] + (moved.shape[-2] * moved.shape[-1],))


def attend(queries, key_pack, key_pos, present, query_pos):
    scores = jnp.einsum(
        "nbkge,bket->nbkgt", queries, key_pack[:, :, 0], preferred_element_type=jnp.float32
    ) * queries.shape[-1] ** (-0.5)
    distance = query_pos[:, :, None] - key_pos[None, :, :]
    allowed = (present[None, :, :] & (distance >= 0) & (distance < WINDOW))[:, :, None, None, :]
    scores = jnp.where(allowed, scores, masked_score)
    maximum = jnp.max(scores, -1)
    weights = jnp.where(allowed, jnp.exp(scores - maximum[..., None]), 0.0)
    totals = jnp.sum(weights, -1)
    weighted = jnp.einsum(
        "nbkgt,bket->nbkge",
        weights.astype(jnp.bfloat16),
        key_pack[:, :, 1],
        preferred_element_type=jnp.float32,
    )
    return (weighted, maximum, totals)


def merge_parts(first, second):
    maximum = jnp.maximum(first[1], second[1])
    first_scale = jnp.exp(first[1] - maximum)
    second_scale = jnp.exp(second[1] - maximum)
    return (
        first[0] * first_scale[..., None] + second[0] * second_scale[..., None],
        maximum,
        first[2] * first_scale + second[2] * second_scale,
    )


ROOT_PAGES = 16
MID_PAGES = 16
LEAF_SLOTS = 8
CHUNK_PAGES = 4


def part_body(chunk0, with_fresh, tbl, meta, q_ref, store_hbm, kv, sc, top, mass, acc, sem, begin, finish):
    b = pl.program_id(0)
    requests = pl.num_programs(0)
    slot = b % 2
    shared_count = ROOT_PAGES + MID_PAGES
    page_count = kv.shape[1]
    width = kv.shape[-1]
    group = CHUNK_PAGES
    span = group * width

    def start_request(j, into):
        def page_body(p, carry):
            pltpu.make_async_copy(store_hbm.at[tbl[j, p]], kv.at[into, p], sem.at[into]).start()
            return carry

        lax.fori_loop(0, page_count, page_body, 0)

    @pl.when(b == 0)
    def _():
        start_request(0, 0)

    @pl.when(b + 1 < requests)
    def _():
        start_request(b + 1, 1 - slot)

    def wait_body(p, carry):
        pltpu.make_async_copy(store_hbm.at[0], kv.at[slot, p], sem.at[slot]).wait()
        return carry

    lax.fori_loop(0, page_count, wait_body, 0)

    root_span = meta[b, 0]
    mid_span = meta[b, 1]
    leaf_span = meta[b, 2]
    context = meta[b, 3]
    q = q_ref[0]
    rows = q.shape[0]
    query_pos = context + (lax.broadcasted_iota(jnp.int32, (rows, 1), 0) % width)
    lanes = lax.broadcasted_iota(jnp.int32, (1, span), 1)
    scale = HD ** (-0.5)

    def masked(s, key_pos, present):
        distance = query_pos - key_pos
        allowed = present & (distance >= 0) & (distance < WINDOW)
        return jnp.where(allowed, s, masked_score)

    def geometry(c):
        page = group * (chunk0 + c)
        in_root = page < ROOT_PAGES
        in_mid = page < shared_count
        first = jnp.where(
            in_root, page * width, jnp.where(in_mid, (page - ROOT_PAGES) * width, (page - shared_count) * width)
        )
        base = jnp.where(in_root, 0, jnp.where(in_mid, root_span, root_span + mid_span))
        limit = jnp.where(in_root, root_span, jnp.where(in_mid, mid_span, leaf_span))
        live = (first < limit) & (context - (base + first + span - 1) < WINDOW)
        return first, base, limit, live

    def pages_of(c, part):
        return jnp.concatenate([kv[slot, group * c + k, part] for k in range(group)], 1)

    begin(q, query_pos, masked, scale)

    def keep(c, s):
        sc[c] = s
        m = top[...]
        for k in range(group):
            m = jnp.maximum(m, s[:, k * width:(k + 1) * width])
        top[...] = m

    def max_body(c, carry):
        first, base, limit, live = geometry(c)
        full = (first + span <= limit) & (context + width - 1 - (base + first) < WINDOW)

        @pl.when(full)
        def _():
            keep(c, jnp.dot(q, pages_of(c, 0), preferred_element_type=jnp.float32) * scale)

        @pl.when(live & jnp.logical_not(full))
        def _():
            steps_in = first + lanes
            s = jnp.dot(q, pages_of(c, 0), preferred_element_type=jnp.float32) * scale
            keep(c, masked(s, base + steps_in, steps_in < limit))

        return carry

    chunks = page_count // group
    lax.fori_loop(0, chunks, max_body, 0)
    earlier = top[...]
    top[...] = jnp.broadcast_to(jnp.max(earlier, -1, keepdims=True), top.shape)
    row_top = top[...]
    finish(row_top)

    def sum_body(c, carry):
        first, base, limit, live = geometry(c)

        @pl.when(live)
        def _():
            s = sc[c]
            parts = [jnp.exp(s[:, k * width:(k + 1) * width] - row_top) for k in range(group)]
            total = mass[...]
            for part in parts:
                total = total + part
            mass[...] = total
            w = jnp.concatenate(parts, 1).astype(jnp.bfloat16)
            acc[...] = acc[...] + lax.dot_general(
                w, pages_of(c, 1), (((1,), (1,)), ((), ())), preferred_element_type=jnp.float32
            )

        return carry

    lax.fori_loop(0, chunks, sum_body, 0)


def leaf_kernel(tbl, meta, q_ref, fresh_ref, store_hbm, acc_out, top_out, mass_out, kv, sc, fresh_sc, top, mass, acc, sem):
    def begin(q, query_pos, masked, scale):
        width = fresh_sc.shape[-1]
        fresh_lanes = lax.broadcasted_iota(jnp.int32, (1, width), 1)
        fresh_scores = masked(
            jnp.dot(q, fresh_ref[0, 0], preferred_element_type=jnp.float32) * scale,
            meta[pl.program_id(0), 3] + fresh_lanes,
            fresh_lanes >= 0,
        )
        fresh_sc[...] = fresh_scores
        top[...] = fresh_scores

    def finish(row_top):
        fresh_w = jnp.exp(fresh_sc[...] - row_top)
        mass[...] = fresh_w
        acc[...] = lax.dot_general(
            fresh_w.astype(jnp.bfloat16), fresh_ref[0, 1], (((1,), (1,)), ((), ())),
            preferred_element_type=jnp.float32,
        )

    part_body(
        (ROOT_PAGES + MID_PAGES) // CHUNK_PAGES, True, tbl, meta, q_ref, store_hbm, kv, sc, top, mass, acc, sem,
        begin, finish,
    )
    acc_out[0] = acc[...]
    top_out[0] = top[...]
    mass_out[0] = mass[...]


def carry_kernel(tbl, meta, q_ref, acc_in, top_in, mass_in, store_hbm, acc_out, top_out, mass_out, kv, sc, top, mass, acc, sem):
    def begin(q, query_pos, masked, scale):
        top[...] = top_in[0]

    def finish(row_top):
        factor = jnp.exp(top_in[0] - row_top)
        mass[...] = mass_in[0] * factor
        acc[...] = acc_in[0] * factor[:, :1]

    part_body(0, False, tbl, meta, q_ref, store_hbm, kv, sc, top, mass, acc, sem, begin, finish)
    acc_out[0] = acc[...]
    top_out[0] = top[...]
    mass_out[0] = mass[...]


def shared_kernel(tbl, meta, q_ref, acc_in, top_in, mass_in, store_hbm, out_ref, kv, sc, top, mass, acc, sem):
    def begin(q, query_pos, masked, scale):
        top[...] = top_in[0]

    def finish(row_top):
        factor = jnp.exp(top_in[0] - row_top)
        mass[...] = mass_in[0] * factor
        acc[...] = acc_in[0] * factor[:, :1]

    part_body(
        ROOT_PAGES // CHUNK_PAGES, False, tbl, meta, q_ref, store_hbm, kv, sc, top, mass, acc, sem, begin, finish
    )
    totals = jnp.sum(mass[...], -1, keepdims=True)
    out_ref[0] = (acc[...] / totals).astype(out_ref.dtype)


def part_call(kernel, tbl, meta, inputs, in_blocks, store, out_shapes):
    reqs, rows, head = inputs[0].shape
    page_shape = store.shape[1:]
    width = page_shape[-1]
    pages = tbl.shape[1]

    def block(shape):
        return pl.BlockSpec((1,) + shape[1:], lambda i, t, m: (i,) + (0,) * (len(shape) - 1))

    scratch = [
        pltpu.VMEM((2, pages) + page_shape, store.dtype),
        pltpu.VMEM((pages // CHUNK_PAGES, rows, CHUNK_PAGES * width), jnp.float32),
    ]
    if kernel is leaf_kernel:
        scratch.append(pltpu.VMEM((rows, width), jnp.float32))
    scratch += [
        pltpu.VMEM((rows, width), jnp.float32),
        pltpu.VMEM((rows, width), jnp.float32),
        pltpu.VMEM((rows, head), jnp.float32),
        pltpu.SemaphoreType.DMA((2,)),
    ]
    grid_spec = pltpu.PrefetchScalarGridSpec(
        num_scalar_prefetch=2,
        grid=(reqs,),
        in_specs=[block(x.shape) for x in inputs] + [pl.BlockSpec(memory_space=pl.ANY)],
        out_specs=[block(s.shape) for s in out_shapes],
        scratch_shapes=scratch,
    )
    keys_total = pages * width
    return pl.pallas_call(
        kernel,
        grid_spec=grid_spec,
        out_shape=out_shapes,
        compiler_params=pltpu.CompilerParams(dimension_semantics=("arbitrary",)),
        cost_estimate=pl.CostEstimate(
            flops=4 * reqs * rows * keys_total * head,
            transcendentals=reqs * rows * keys_total,
            bytes_accessed=reqs * pages * 2 * head * width * 2,
        ),
    )(tbl, meta, *inputs, store)


def paged_attention(tbl, meta, queries, fresh, root_store, mid_store, leaf_store):
    reqs, rows, head = queries.shape
    width = leaf_store.shape[-1]
    shared_count = ROOT_PAGES + MID_PAGES
    state_shapes = [
        jax.ShapeDtypeStruct((reqs, rows, head), jnp.float32),
        jax.ShapeDtypeStruct((reqs, rows, width), jnp.float32),
        jax.ShapeDtypeStruct((reqs, rows, width), jnp.float32),
    ]
    state = part_call(leaf_kernel, tbl[:, shared_count:], meta, [queries, fresh], None, leaf_store, state_shapes)
    state = part_call(
        carry_kernel, tbl[:, :ROOT_PAGES], meta, [queries] + list(state), None, root_store, state_shapes
    )
    (out,) = part_call(
        shared_kernel, tbl[:, ROOT_PAGES:shared_count], meta, [queries] + list(state), None, mid_store,
        [jax.ShapeDtypeStruct((reqs, rows, head), jnp.bfloat16)],
    )
    return out


def spans(request_ids, root_len, mid_len, leaf_len, mid_parent, leaf_parent):
    mid_nodes = leaf_parent[request_ids]
    root_nodes = mid_parent[mid_nodes]
    return (root_nodes, mid_nodes, root_len[root_nodes], mid_len[mid_nodes], leaf_len[request_ids])


def shards(
    hidden,
    gain_attn,
    w_query,
    w_key,
    w_value,
    w_out,
    gain_ffn,
    w_gate,
    w_up,
    w_down,
    shared_pages,
    leaf_pages,
    root_table,
    mid_table,
    leaf_table,
    root_len,
    mid_len,
    leaf_len,
    mid_parent,
    leaf_parent,
    slot_request,
):
    new_rows, local_reqs, model_width = hidden.shape
    seq_count = lax.axis_size("seq")
    seq_index = lax.axis_index("seq")
    kv_local = leaf_pages.shape[1]
    group_size = QH // KVH
    pages_here = leaf_pages.shape[0]
    slot_ids = seq_index * local_reqs + jnp.arange(local_reqs, dtype=jnp.int32)
    requests = slot_request[slot_ids]
    root_nodes, mid_nodes, root_span, mid_span, leaf_span = spans(
        requests, root_len, mid_len, leaf_len, mid_parent, leaf_parent
    )
    context = root_span + mid_span + leaf_span
    new_index = jnp.arange(new_rows, dtype=jnp.int32)
    query_pos = context[None, :] + new_index[:, None]
    all_slots = slot_request.reshape(seq_count, local_reqs)
    per_index = shared_pages.shape[0]
    root_home = root_table // per_index
    root_local = jnp.take_along_axis(
        root_table, jnp.argmax(root_home == seq_index, 1)[:, None], 1
    )[:, 0] - seq_index * per_index
    mid_home = mid_table // per_index
    mid_local = jnp.take_along_axis(
        mid_table, jnp.argmax(mid_home == seq_index, 1)[:, None], 1
    )[:, 0] - seq_index * per_index
    root_gathered = lax.all_gather(jnp.take(shared_pages, root_local, axis=0), "seq", axis=0, tiled=True)
    mid_gathered = lax.all_gather(jnp.take(shared_pages, mid_local, axis=0), "seq", axis=0, tiled=True)
    root_count = root_table.shape[0]
    mid_count = mid_table.shape[0]
    normed = rms_norm(hidden, gain_attn).reshape(-1, model_width)
    query_proj = jnp.dot(normed, w_query, preferred_element_type=jnp.float32).reshape(
        new_rows, local_reqs, -1, HD
    )
    queries = (
        rotate(query_proj, query_pos[:, :, None])
        .astype(jnp.bfloat16)
        .reshape(new_rows, local_reqs, kv_local, group_size, HD)
    )
    key_proj = jnp.dot(normed, w_key, preferred_element_type=jnp.float32).reshape(
        new_rows, local_reqs, kv_local, HD
    )
    new_keys = rotate(key_proj, query_pos[:, :, None]).astype(jnp.bfloat16)
    new_values = (
        jnp.dot(normed, w_value, preferred_element_type=jnp.float32)
        .astype(jnp.bfloat16)
        .reshape(new_rows, local_reqs, kv_local, HD)
    )
    home_of = leaf_table[:, 0] // pages_here
    own_homes = home_of[requests]
    sender_match = home_of[all_slots] == seq_index
    sender_pick = jnp.argmax(sender_match, 1)
    sender_have = jnp.any(sender_match, 1)
    picked_request = jnp.take_along_axis(all_slots, sender_pick[:, None], 1)[:, 0]
    page_ids = jnp.where(
        sender_have[:, None], leaf_table[picked_request] - seq_index * pages_here, 0
    )
    leaf_slots = leaf_table.shape[1]
    outgoing = jnp.where(
        sender_have[:, None, None, None, None, None], jnp.take(leaf_pages, page_ids, axis=0), 0
    )
    arrived = lax.all_to_all(outgoing, "seq", split_axis=0, concat_axis=0, tiled=True)
    page_shape = arrived.shape[-3:]
    leaf_store = arrived.reshape((-1,) + page_shape)
    root_store = root_gathered.reshape((-1,) + page_shape)
    mid_store = mid_gathered.reshape((-1,) + page_shape)
    tbl = jnp.concatenate(
        [
            root_home[root_nodes] * root_count + root_nodes[:, None],
            mid_home[mid_nodes] * mid_count + mid_nodes[:, None],
            own_homes[:, None] * leaf_slots + jnp.arange(leaf_slots, dtype=jnp.int32)[None, :],
        ],
        1,
    ).astype(jnp.int32)
    meta = jnp.stack([root_span, mid_span, leaf_span, context], 1).astype(jnp.int32)
    fresh_pack = jnp.stack(
        [jnp.transpose(new_keys[:, :, 0], (1, 2, 0)), jnp.transpose(new_values[:, :, 0], (1, 2, 0))], 1
    )
    query_rows = jnp.transpose(queries[:, :, 0], (1, 2, 0, 3)).reshape(local_reqs, -1, HD)
    attended = paged_attention(tbl, meta, query_rows, fresh_pack, root_store, mid_store, leaf_store)
    attended = (
        jnp.transpose(attended.reshape(local_reqs, group_size, new_rows, HD), (2, 0, 1, 3))
        .reshape(new_rows * local_reqs, -1)
    )
    tp_count = lax.axis_size("tp")
    own_count = new_rows // tp_count
    attn_proj = (
        lax.psum_scatter(
            jnp.dot(attended, w_out, preferred_element_type=jnp.float32).astype(jnp.bfloat16),
            "tp",
            scatter_dimension=0,
            tiled=True,
        )
        .astype(jnp.float32)
        .reshape(own_count, local_reqs, model_width)
    )
    own_hidden = lax.dynamic_slice_in_dim(hidden, lax.axis_index("tp") * own_count, own_count, 0)
    resid = own_hidden.astype(jnp.float32) + attn_proj
    normed_own = rms_norm(resid, gain_ffn).reshape(-1, model_width)
    normed_ffn = lax.all_gather(normed_own, "tp", axis=0, tiled=True)
    gate_rows = jnp.dot(normed_ffn, w_gate, preferred_element_type=jnp.float32)
    up_rows = jnp.dot(normed_ffn, w_up, preferred_element_type=jnp.float32)
    activated = (jax.nn.silu(gate_rows) * up_rows).astype(jnp.bfloat16)
    ffn_proj = (
        lax.psum_scatter(
            jnp.dot(activated, w_down, preferred_element_type=jnp.float32).astype(jnp.bfloat16),
            "tp",
            scatter_dimension=0,
            tiled=True,
        )
        .astype(jnp.float32)
        .reshape(own_count, local_reqs, model_width)
    )
    return resid + ffn_proj


def solution(mesh):
    return jax.shard_map(
        shards,
        mesh=mesh,
        in_specs=(
            P(None, "seq", None),
            P(),
            P(None, "tp"),
            P(None, "tp"),
            P(None, "tp"),
            P("tp", None),
            P(),
            P(None, "tp"),
            P(None, "tp"),
            P("tp", None),
            P("seq", "tp", None, None, None),
            P("seq", "tp", None, None, None),
            P(),
            P(),
            P(),
            P(),
            P(),
            P(),
            P(),
            P(),
            P(),
        ),
        out_specs=P("tp", "seq", None),
        check_vma=False,
    )
```

```python
import functools

import jax
import jax.numpy as jnp
from jax import lax
from jax.sharding import PartitionSpec as P
from jax.experimental import pallas as pl
from jax.experimental.pallas import tpu as pltpu

QH = 32
KVH = 8
HD = 80
WINDOW = 4096


masked_score = -1e30
rope_base = 10000.0


def rms_norm(row_data, gain_vector):
    values = row_data.astype(jnp.float32)
    inverse_rms = lax.rsqrt(jnp.mean(values * values, -1, keepdims=True) + 1e-05)
    return (values * inverse_rms * gain_vector.astype(jnp.float32)).astype(jnp.bfloat16)


def rotate(vector, position):
    half_size = vector.shape[-1] // 2
    frequency = rope_base ** (-2.0 * jnp.arange(half_size, dtype=jnp.float32) / vector.shape[-1])
    angles = position.astype(jnp.float32)[..., None] * frequency
    cos_part = jnp.cos(angles)
    sin_part = jnp.sin(angles)
    first_half = vector[..., :half_size]
    second_half = vector[..., half_size:]
    return jnp.concatenate(
        [
            first_half * cos_part - second_half * sin_part,
            second_half * cos_part + first_half * sin_part,
        ],
        -1,
    )


def page_columns(pages):
    moved = jnp.moveaxis(pages, -5, -2)
    return moved.reshape(moved.shape[:-2] + (moved.shape[-2] * moved.shape[-1],))


def attend(queries, key_pack, key_pos, present, query_pos):
    scores = jnp.einsum(
        "nbkge,bket->nbkgt", queries, key_pack[:, :, 0], preferred_element_type=jnp.float32
    ) * queries.shape[-1] ** (-0.5)
    distance = query_pos[:, :, None] - key_pos[None, :, :]
    allowed = (present[None, :, :] & (distance >= 0) & (distance < WINDOW))[:, :, None, None, :]
    scores = jnp.where(allowed, scores, masked_score)
    maximum = jnp.max(scores, -1)
    weights = jnp.where(allowed, jnp.exp(scores - maximum[..., None]), 0.0)
    totals = jnp.sum(weights, -1)
    weighted = jnp.einsum(
        "nbkgt,bket->nbkge",
        weights.astype(jnp.bfloat16),
        key_pack[:, :, 1],
        preferred_element_type=jnp.float32,
    )
    return (weighted, maximum, totals)


def merge_parts(first, second):
    maximum = jnp.maximum(first[1], second[1])
    first_scale = jnp.exp(first[1] - maximum)
    second_scale = jnp.exp(second[1] - maximum)
    return (
        first[0] * first_scale[..., None] + second[0] * second_scale[..., None],
        maximum,
        first[2] * first_scale + second[2] * second_scale,
    )


ROOT_PAGES = 16
MID_PAGES = 16
LEAF_SLOTS = 8
CHUNK_PAGES = 4


def part_body(chunk0, with_fresh, tbl, meta, q_ref, store_hbm, kv, sc, top, mass, acc, sem, begin, finish):
    b = pl.program_id(0)
    requests = pl.num_programs(0)
    slot = b % 2
    shared_count = ROOT_PAGES + MID_PAGES
    page_count = kv.shape[1]
    width = kv.shape[-1]
    group = CHUNK_PAGES
    span = group * width

    def start_request(j, into):
        def page_body(p, carry):
            pltpu.make_async_copy(store_hbm.at[tbl[j, p]], kv.at[into, p], sem.at[into]).start()
            return carry

        lax.fori_loop(0, page_count, page_body, 0)

    @pl.when(b == 0)
    def _():
        start_request(0, 0)

    @pl.when(b + 1 < requests)
    def _():
        start_request(b + 1, 1 - slot)

    def wait_body(p, carry):
        pltpu.make_async_copy(store_hbm.at[0], kv.at[slot, p], sem.at[slot]).wait()
        return carry

    lax.fori_loop(0, page_count, wait_body, 0)

    root_span = meta[b, 0]
    mid_span = meta[b, 1]
    leaf_span = meta[b, 2]
    context = meta[b, 3]
    q = q_ref[0]
    rows = q.shape[0]
    query_pos = context + (lax.broadcasted_iota(jnp.int32, (rows, 1), 0) % width)
    lanes = lax.broadcasted_iota(jnp.int32, (1, span), 1)
    scale = HD ** (-0.5)

    def masked(s, key_pos, present):
        distance = query_pos - key_pos
        allowed = present & (distance >= 0) & (distance < WINDOW)
        return jnp.where(allowed, s, masked_score)

    def geometry(c):
        page = group * (chunk0 + c)
        in_root = page < ROOT_PAGES
        in_mid = page < shared_count
        first = jnp.where(
            in_root, page * width, jnp.where(in_mid, (page - ROOT_PAGES) * width, (page - shared_count) * width)
        )
        base = jnp.where(in_root, 0, jnp.where(in_mid, root_span, root_span + mid_span))
        limit = jnp.where(in_root, root_span, jnp.where(in_mid, mid_span, leaf_span))
        live = (first < limit) & (context - (base + first + span - 1) < WINDOW)
        return first, base, limit, live

    def pages_of(c, part):
        return jnp.concatenate([kv[slot, group * c + k, part] for k in range(group)], 1)

    begin(q, query_pos, masked, scale)

    def keep(c, s):
        sc[c] = s
        m = top[...]
        for k in range(group):
            m = jnp.maximum(m, s[:, k * width:(k + 1) * width])
        top[...] = m

    def max_body(c, carry):
        first, base, limit, live = geometry(c)
        full = (first + span <= limit) & (context + width - 1 - (base + first) < WINDOW)

        @pl.when(full)
        def _():
            keep(c, jnp.dot(q, pages_of(c, 0), preferred_element_type=jnp.float32) * scale)

        @pl.when(live & jnp.logical_not(full))
        def _():
            steps_in = first + lanes
            s = jnp.dot(q, pages_of(c, 0), preferred_element_type=jnp.float32) * scale
            keep(c, masked(s, base + steps_in, steps_in < limit))

        return carry

    chunks = page_count // group
    lax.fori_loop(0, chunks, max_body, 0)
    earlier = top[...]
    top[...] = jnp.broadcast_to(jnp.max(earlier, -1, keepdims=True), top.shape)
    row_top = top[...]
    finish(row_top)

    def sum_body(c, carry):
        first, base, limit, live = geometry(c)

        @pl.when(live)
        def _():
            s = sc[c]
            parts = [jnp.exp(s[:, k * width:(k + 1) * width] - row_top) for k in range(group)]
            total = mass[...]
            for part in parts:
                total = total + part
            mass[...] = total
            w = jnp.concatenate(parts, 1).astype(jnp.bfloat16)
            acc[...] = acc[...] + lax.dot_general(
                w, pages_of(c, 1), (((1,), (1,)), ((), ())), preferred_element_type=jnp.float32
            )

        return carry

    lax.fori_loop(0, chunks, sum_body, 0)


def leaf_kernel(chunk0, tbl, meta, q_ref, fresh_ref, store_hbm, acc_out, top_out, mass_out, kv, sc, fresh_sc, top, mass, acc, sem):
    def begin(q, query_pos, masked, scale):
        width = fresh_sc.shape[-1]
        fresh_lanes = lax.broadcasted_iota(jnp.int32, (1, width), 1)
        fresh_scores = masked(
            jnp.dot(q, fresh_ref[0, 0], preferred_element_type=jnp.float32) * scale,
            meta[pl.program_id(0), 3] + fresh_lanes,
            fresh_lanes >= 0,
        )
        fresh_sc[...] = fresh_scores
        top[...] = fresh_scores

    def finish(row_top):
        fresh_w = jnp.exp(fresh_sc[...] - row_top)
        mass[...] = fresh_w
        acc[...] = lax.dot_general(
            fresh_w.astype(jnp.bfloat16), fresh_ref[0, 1], (((1,), (1,)), ((), ())),
            preferred_element_type=jnp.float32,
        )

    part_body(
        chunk0, True, tbl, meta, q_ref, store_hbm, kv, sc, top, mass, acc, sem,
        begin, finish,
    )
    acc_out[0] = acc[...]
    top_out[0] = top[...]
    mass_out[0] = mass[...]


def shared_kernel(chunk0, tbl, meta, q_ref, acc_in, top_in, mass_in, store_hbm, out_ref, kv, sc, top, mass, acc, sem):
    def begin(q, query_pos, masked, scale):
        top[...] = top_in[0]

    def finish(row_top):
        factor = jnp.exp(top_in[0] - row_top)
        mass[...] = mass_in[0] * factor
        acc[...] = acc_in[0] * factor[:, :1]

    part_body(chunk0, False, tbl, meta, q_ref, store_hbm, kv, sc, top, mass, acc, sem, begin, finish)
    totals = jnp.sum(mass[...], -1, keepdims=True)
    out_ref[0] = (acc[...] / totals).astype(out_ref.dtype)


def part_call(kernel, tbl, meta, inputs, in_blocks, store, out_shapes):
    reqs, rows, head = inputs[0].shape
    page_shape = store.shape[1:]
    width = page_shape[-1]
    pages = tbl.shape[1]

    def block(shape):
        return pl.BlockSpec((1,) + shape[1:], lambda i, t, m: (i,) + (0,) * (len(shape) - 1))

    scratch = [
        pltpu.VMEM((2, pages) + page_shape, store.dtype),
        pltpu.VMEM((pages // CHUNK_PAGES, rows, CHUNK_PAGES * width), jnp.float32),
    ]
    if kernel.func is leaf_kernel:
        scratch.append(pltpu.VMEM((rows, width), jnp.float32))
    scratch += [
        pltpu.VMEM((rows, width), jnp.float32),
        pltpu.VMEM((rows, width), jnp.float32),
        pltpu.VMEM((rows, head), jnp.float32),
        pltpu.SemaphoreType.DMA((2,)),
    ]
    grid_spec = pltpu.PrefetchScalarGridSpec(
        num_scalar_prefetch=2,
        grid=(reqs,),
        in_specs=[block(x.shape) for x in inputs] + [pl.BlockSpec(memory_space=pl.ANY)],
        out_specs=[block(s.shape) for s in out_shapes],
        scratch_shapes=scratch,
    )
    keys_total = pages * width
    return pl.pallas_call(
        kernel,
        grid_spec=grid_spec,
        out_shape=out_shapes,
        compiler_params=pltpu.CompilerParams(dimension_semantics=("arbitrary",)),
        cost_estimate=pl.CostEstimate(
            flops=4 * reqs * rows * keys_total * head,
            transcendentals=reqs * rows * keys_total,
            bytes_accessed=reqs * pages * 2 * head * width * 2,
        ),
    )(tbl, meta, *inputs, store)


def paged_attention(tbl, meta, queries, fresh, shared_store, leaf_store):
    reqs, rows, head = queries.shape
    width = shared_store.shape[-1]
    shared_count = ROOT_PAGES + MID_PAGES
    state = part_call(
        functools.partial(leaf_kernel, 0), tbl[:, :shared_count], meta, [queries, fresh], None, shared_store,
        [
            jax.ShapeDtypeStruct((reqs, rows, head), jnp.float32),
            jax.ShapeDtypeStruct((reqs, rows, width), jnp.float32),
            jax.ShapeDtypeStruct((reqs, rows, width), jnp.float32),
        ],
    )
    (out,) = part_call(
        functools.partial(shared_kernel, shared_count // CHUNK_PAGES), tbl[:, shared_count:], meta,
        [queries] + list(state), None, leaf_store,
        [jax.ShapeDtypeStruct((reqs, rows, head), jnp.bfloat16)],
    )
    return out


def spans(request_ids, root_len, mid_len, leaf_len, mid_parent, leaf_parent):
    mid_nodes = leaf_parent[request_ids]
    root_nodes = mid_parent[mid_nodes]
    return (root_nodes, mid_nodes, root_len[root_nodes], mid_len[mid_nodes], leaf_len[request_ids])


def shards(
    hidden,
    gain_attn,
    w_query,
    w_key,
    w_value,
    w_out,
    gain_ffn,
    w_gate,
    w_up,
    w_down,
    shared_pages,
    leaf_pages,
    root_table,
    mid_table,
    leaf_table,
    root_len,
    mid_len,
    leaf_len,
    mid_parent,
    leaf_parent,
    slot_request,
):
    new_rows, local_reqs, model_width = hidden.shape
    seq_count = lax.axis_size("seq")
    seq_index = lax.axis_index("seq")
    kv_local = leaf_pages.shape[1]
    group_size = QH // KVH
    pages_here = leaf_pages.shape[0]
    slot_ids = seq_index * local_reqs + jnp.arange(local_reqs, dtype=jnp.int32)
    requests = slot_request[slot_ids]
    root_nodes, mid_nodes, root_span, mid_span, leaf_span = spans(
        requests, root_len, mid_len, leaf_len, mid_parent, leaf_parent
    )
    context = root_span + mid_span + leaf_span
    new_index = jnp.arange(new_rows, dtype=jnp.int32)
    query_pos = context[None, :] + new_index[:, None]
    all_slots = slot_request.reshape(seq_count, local_reqs)
    page_store = lax.all_gather(shared_pages, "seq", axis=0, tiled=True)
    root_index = root_table[root_nodes]
    mid_index = mid_table[mid_nodes]
    normed = rms_norm(hidden, gain_attn).reshape(-1, model_width)
    query_proj = jnp.dot(normed, w_query, preferred_element_type=jnp.float32).reshape(
        new_rows, local_reqs, -1, HD
    )
    queries = (
        rotate(query_proj, query_pos[:, :, None])
        .astype(jnp.bfloat16)
        .reshape(new_rows, local_reqs, kv_local, group_size, HD)
    )
    key_proj = jnp.dot(normed, w_key, preferred_element_type=jnp.float32).reshape(
        new_rows, local_reqs, kv_local, HD
    )
    new_keys = rotate(key_proj, query_pos[:, :, None]).astype(jnp.bfloat16)
    new_values = (
        jnp.dot(normed, w_value, preferred_element_type=jnp.float32)
        .astype(jnp.bfloat16)
        .reshape(new_rows, local_reqs, kv_local, HD)
    )
    home_of = leaf_table[:, 0] // pages_here
    own_homes = home_of[requests]
    sender_match = home_of[all_slots] == seq_index
    sender_pick = jnp.argmax(sender_match, 1)
    sender_have = jnp.any(sender_match, 1)
    picked_request = jnp.take_along_axis(all_slots, sender_pick[:, None], 1)[:, 0]
    page_ids = jnp.where(
        sender_have[:, None], leaf_table[picked_request] - seq_index * pages_here, 0
    )
    leaf_slots = leaf_table.shape[1]
    outgoing = jnp.where(
        sender_have[:, None, None, None, None, None], jnp.take(leaf_pages, page_ids, axis=0), 0
    )
    outgoing, page_store = lax.optimization_barrier((outgoing, page_store))
    arrived = lax.all_to_all(outgoing, "seq", split_axis=0, concat_axis=0, tiled=True)
    page_shape = arrived.shape[-3:]
    leaf_store = arrived.reshape((-1,) + page_shape)
    shared_store = page_store.reshape((-1,) + page_shape)
    tbl = jnp.concatenate(
        [
            root_index,
            mid_index,
            own_homes[:, None] * leaf_slots + jnp.arange(leaf_slots, dtype=jnp.int32)[None, :],
        ],
        1,
    ).astype(jnp.int32)
    meta = jnp.stack([root_span, mid_span, leaf_span, context], 1).astype(jnp.int32)
    fresh_pack = jnp.stack(
        [jnp.transpose(new_keys[:, :, 0], (1, 2, 0)), jnp.transpose(new_values[:, :, 0], (1, 2, 0))], 1
    )
    query_rows = jnp.transpose(queries[:, :, 0], (1, 2, 0, 3)).reshape(local_reqs, -1, HD)
    attended = paged_attention(tbl, meta, query_rows, fresh_pack, shared_store, leaf_store)
    attended = (
        jnp.transpose(attended.reshape(local_reqs, group_size, new_rows, HD), (2, 0, 1, 3))
        .reshape(new_rows * local_reqs, -1)
    )
    tp_count = lax.axis_size("tp")
    own_count = new_rows // tp_count
    attn_proj = (
        lax.psum_scatter(
            jnp.dot(attended, w_out, preferred_element_type=jnp.float32).astype(jnp.bfloat16),
            "tp",
            scatter_dimension=0,
            tiled=True,
        )
        .astype(jnp.float32)
        .reshape(own_count, local_reqs, model_width)
    )
    own_hidden = lax.dynamic_slice_in_dim(hidden, lax.axis_index("tp") * own_count, own_count, 0)
    resid = own_hidden.astype(jnp.float32) + attn_proj
    normed_own = rms_norm(resid, gain_ffn).reshape(-1, model_width)
    normed_ffn = lax.all_gather(normed_own, "tp", axis=0, tiled=True)
    gate_rows = jnp.dot(normed_ffn, w_gate, preferred_element_type=jnp.float32)
    up_rows = jnp.dot(normed_ffn, w_up, preferred_element_type=jnp.float32)
    activated = (jax.nn.silu(gate_rows) * up_rows).astype(jnp.bfloat16)
    ffn_proj = (
        lax.psum_scatter(
            jnp.dot(activated, w_down, preferred_element_type=jnp.float32).astype(jnp.bfloat16),
            "tp",
            scatter_dimension=0,
            tiled=True,
        )
        .astype(jnp.float32)
        .reshape(own_count, local_reqs, model_width)
    )
    return resid + ffn_proj


def solution(mesh):
    return jax.shard_map(
        shards,
        mesh=mesh,
        in_specs=(
            P(None, "seq", None),
            P(),
            P(None, "tp"),
            P(None, "tp"),
            P(None, "tp"),
            P("tp", None),
            P(),
            P(None, "tp"),
            P(None, "tp"),
            P("tp", None),
            P("seq", "tp", None, None, None),
            P("seq", "tp", None, None, None),
            P(),
            P(),
            P(),
            P(),
            P(),
            P(),
            P(),
            P(),
            P(),
        ),
        out_specs=P("tp", "seq", None),
        check_vma=False,
    )
```

```python
import jax
import jax.numpy as jnp
from jax import lax
from jax.sharding import PartitionSpec as P
from jax.experimental import pallas as pl
from jax.experimental.pallas import tpu as pltpu

QH = 32
KVH = 8
HD = 80
WINDOW = 4096


masked_score = -1e30
rope_base = 10000.0


def rms_norm(row_data, gain_vector):
    values = row_data.astype(jnp.float32)
    inverse_rms = lax.rsqrt(jnp.mean(values * values, -1, keepdims=True) + 1e-05)
    return (values * inverse_rms * gain_vector.astype(jnp.float32)).astype(jnp.bfloat16)


def rotate(vector, position):
    half_size = vector.shape[-1] // 2
    frequency = rope_base ** (-2.0 * jnp.arange(half_size, dtype=jnp.float32) / vector.shape[-1])
    angles = position.astype(jnp.float32)[..., None] * frequency
    cos_part = jnp.cos(angles)
    sin_part = jnp.sin(angles)
    first_half = vector[..., :half_size]
    second_half = vector[..., half_size:]
    return jnp.concatenate(
        [
            first_half * cos_part - second_half * sin_part,
            second_half * cos_part + first_half * sin_part,
        ],
        -1,
    )


def page_columns(pages):
    moved = jnp.moveaxis(pages, -5, -2)
    return moved.reshape(moved.shape[:-2] + (moved.shape[-2] * moved.shape[-1],))


def attend(queries, key_pack, key_pos, present, query_pos):
    scores = jnp.einsum(
        "nbkge,bket->nbkgt", queries, key_pack[:, :, 0], preferred_element_type=jnp.float32
    ) * queries.shape[-1] ** (-0.5)
    distance = query_pos[:, :, None] - key_pos[None, :, :]
    allowed = (present[None, :, :] & (distance >= 0) & (distance < WINDOW))[:, :, None, None, :]
    scores = jnp.where(allowed, scores, masked_score)
    maximum = jnp.max(scores, -1)
    weights = jnp.where(allowed, jnp.exp(scores - maximum[..., None]), 0.0)
    totals = jnp.sum(weights, -1)
    weighted = jnp.einsum(
        "nbkgt,bket->nbkge",
        weights.astype(jnp.bfloat16),
        key_pack[:, :, 1],
        preferred_element_type=jnp.float32,
    )
    return (weighted, maximum, totals)


def merge_parts(first, second):
    maximum = jnp.maximum(first[1], second[1])
    first_scale = jnp.exp(first[1] - maximum)
    second_scale = jnp.exp(second[1] - maximum)
    return (
        first[0] * first_scale[..., None] + second[0] * second_scale[..., None],
        maximum,
        first[2] * first_scale + second[2] * second_scale,
    )


ROOT_PAGES = 16
MID_PAGES = 16
LEAF_SLOTS = 8
CHUNK_PAGES = 8


def part_body(chunk0, with_fresh, tbl, meta, q_ref, store_hbm, kv, sc, top, mass, acc, sem, begin, finish):
    b = pl.program_id(0)
    requests = pl.num_programs(0)
    slot = b % 2
    shared_count = ROOT_PAGES + MID_PAGES
    page_count = kv.shape[1]
    width = kv.shape[-1]
    group = CHUNK_PAGES
    span = group * width

    def start_request(j, into):
        def page_body(p, carry):
            pltpu.make_async_copy(store_hbm.at[tbl[j, p]], kv.at[into, p], sem.at[into]).start()
            return carry

        lax.fori_loop(0, page_count, page_body, 0)

    @pl.when(b == 0)
    def _():
        start_request(0, 0)

    @pl.when(b + 1 < requests)
    def _():
        start_request(b + 1, 1 - slot)

    def wait_body(p, carry):
        pltpu.make_async_copy(store_hbm.at[0], kv.at[slot, p], sem.at[slot]).wait()
        return carry

    lax.fori_loop(0, page_count, wait_body, 0)

    root_span = meta[b, 0]
    mid_span = meta[b, 1]
    leaf_span = meta[b, 2]
    context = meta[b, 3]
    q = q_ref[0]
    rows = q.shape[0]
    query_pos = context + (lax.broadcasted_iota(jnp.int32, (rows, 1), 0) % width)
    lanes = lax.broadcasted_iota(jnp.int32, (1, span), 1)
    scale = HD ** (-0.5)

    def masked(s, key_pos, present):
        distance = query_pos - key_pos
        allowed = present & (distance >= 0) & (distance < WINDOW)
        return jnp.where(allowed, s, masked_score)

    def geometry(c):
        page = group * (chunk0 + c)
        in_root = page < ROOT_PAGES
        in_mid = page < shared_count
        first = jnp.where(
            in_root, page * width, jnp.where(in_mid, (page - ROOT_PAGES) * width, (page - shared_count) * width)
        )
        base = jnp.where(in_root, 0, jnp.where(in_mid, root_span, root_span + mid_span))
        limit = jnp.where(in_root, root_span, jnp.where(in_mid, mid_span, leaf_span))
        live = (first < limit) & (context - (base + first + span - 1) < WINDOW)
        return first, base, limit, live

    def pages_of(c, part):
        return jnp.concatenate([kv[slot, group * c + k, part] for k in range(group)], 1)

    begin(q, query_pos, masked, scale)

    def keep(c, s):
        sc[c] = s
        m = top[...]
        for k in range(group):
            m = jnp.maximum(m, s[:, k * width:(k + 1) * width])
        top[...] = m

    def max_body(c, carry):
        first, base, limit, live = geometry(c)
        full = (first + span <= limit) & (context + width - 1 - (base + first) < WINDOW)

        @pl.when(full)
        def _():
            keep(c, jnp.dot(q, pages_of(c, 0), preferred_element_type=jnp.float32) * scale)

        @pl.when(live & jnp.logical_not(full))
        def _():
            steps_in = first + lanes
            s = jnp.dot(q, pages_of(c, 0), preferred_element_type=jnp.float32) * scale
            keep(c, masked(s, base + steps_in, steps_in < limit))

        return carry

    chunks = page_count // group
    lax.fori_loop(0, chunks, max_body, 0)
    earlier = top[...]
    top[...] = jnp.broadcast_to(jnp.max(earlier, -1, keepdims=True), top.shape)
    row_top = top[...]
    finish(row_top)

    def sum_body(c, carry):
        first, base, limit, live = geometry(c)

        @pl.when(live)
        def _():
            s = sc[c]
            parts = [jnp.exp(s[:, k * width:(k + 1) * width] - row_top) for k in range(group)]
            total = mass[...]
            for part in parts:
                total = total + part
            mass[...] = total
            w = jnp.concatenate(parts, 1).astype(jnp.bfloat16)
            acc[...] = acc[...] + lax.dot_general(
                w, pages_of(c, 1), (((1,), (1,)), ((), ())), preferred_element_type=jnp.float32
            )

        return carry

    lax.fori_loop(0, chunks, sum_body, 0)


def leaf_kernel(tbl, meta, q_ref, fresh_ref, store_hbm, acc_out, top_out, mass_out, kv, sc, fresh_sc, top, mass, acc, sem):
    def begin(q, query_pos, masked, scale):
        width = fresh_sc.shape[-1]
        fresh_lanes = lax.broadcasted_iota(jnp.int32, (1, width), 1)
        fresh_scores = masked(
            jnp.dot(q, fresh_ref[0, 0], preferred_element_type=jnp.float32) * scale,
            meta[pl.program_id(0), 3] + fresh_lanes,
            fresh_lanes >= 0,
        )
        fresh_sc[...] = fresh_scores
        top[...] = fresh_scores

    def finish(row_top):
        fresh_w = jnp.exp(fresh_sc[...] - row_top)
        mass[...] = fresh_w
        acc[...] = lax.dot_general(
            fresh_w.astype(jnp.bfloat16), fresh_ref[0, 1], (((1,), (1,)), ((), ())),
            preferred_element_type=jnp.float32,
        )

    part_body(
        (ROOT_PAGES + MID_PAGES) // CHUNK_PAGES, True, tbl, meta, q_ref, store_hbm, kv, sc, top, mass, acc, sem,
        begin, finish,
    )
    acc_out[0] = acc[...]
    top_out[0] = top[...]
    mass_out[0] = mass[...]


def shared_kernel(tbl, meta, q_ref, acc_in, top_in, mass_in, store_hbm, out_ref, kv, sc, top, mass, acc, sem):
    def begin(q, query_pos, masked, scale):
        top[...] = top_in[0]

    def finish(row_top):
        factor = jnp.exp(top_in[0] - row_top)
        mass[...] = mass_in[0] * factor
        acc[...] = acc_in[0] * factor[:, :1]

    part_body(0, False, tbl, meta, q_ref, store_hbm, kv, sc, top, mass, acc, sem, begin, finish)
    totals = jnp.sum(mass[...], -1, keepdims=True)
    out_ref[0] = (acc[...] / totals).astype(out_ref.dtype)


def part_call(kernel, tbl, meta, inputs, in_blocks, store, out_shapes):
    reqs, rows, head = inputs[0].shape
    page_shape = store.shape[1:]
    width = page_shape[-1]
    pages = tbl.shape[1]

    def block(shape):
        return pl.BlockSpec((1,) + shape[1:], lambda i, t, m: (i,) + (0,) * (len(shape) - 1))

    scratch = [
        pltpu.VMEM((2, pages) + page_shape, store.dtype),
        pltpu.VMEM((pages // CHUNK_PAGES, rows, CHUNK_PAGES * width), jnp.float32),
    ]
    if kernel is leaf_kernel:
        scratch.append(pltpu.VMEM((rows, width), jnp.float32))
    scratch += [
        pltpu.VMEM((rows, width), jnp.float32),
        pltpu.VMEM((rows, width), jnp.float32),
        pltpu.VMEM((rows, head), jnp.float32),
        pltpu.SemaphoreType.DMA((2,)),
    ]
    grid_spec = pltpu.PrefetchScalarGridSpec(
        num_scalar_prefetch=2,
        grid=(reqs,),
        in_specs=[block(x.shape) for x in inputs] + [pl.BlockSpec(memory_space=pl.ANY)],
        out_specs=[block(s.shape) for s in out_shapes],
        scratch_shapes=scratch,
    )
    keys_total = pages * width
    return pl.pallas_call(
        kernel,
        grid_spec=grid_spec,
        out_shape=out_shapes,
        compiler_params=pltpu.CompilerParams(dimension_semantics=("arbitrary",)),
        cost_estimate=pl.CostEstimate(
            flops=4 * reqs * rows * keys_total * head,
            transcendentals=reqs * rows * keys_total,
            bytes_accessed=reqs * pages * 2 * head * width * 2,
        ),
    )(tbl, meta, *inputs, store)


def paged_attention(tbl, meta, queries, fresh, shared_store, leaf_store):
    reqs, rows, head = queries.shape
    width = shared_store.shape[-1]
    shared_count = ROOT_PAGES + MID_PAGES
    state = part_call(
        leaf_kernel, tbl[:, shared_count:], meta, [queries, fresh], None, leaf_store,
        [
            jax.ShapeDtypeStruct((reqs, rows, head), jnp.float32),
            jax.ShapeDtypeStruct((reqs, rows, width), jnp.float32),
            jax.ShapeDtypeStruct((reqs, rows, width), jnp.float32),
        ],
    )
    (out,) = part_call(
        shared_kernel, tbl[:, :shared_count], meta, [queries] + list(state), None, shared_store,
        [jax.ShapeDtypeStruct((reqs, rows, head), jnp.bfloat16)],
    )
    return out


def spans(request_ids, root_len, mid_len, leaf_len, mid_parent, leaf_parent):
    mid_nodes = leaf_parent[request_ids]
    root_nodes = mid_parent[mid_nodes]
    return (root_nodes, mid_nodes, root_len[root_nodes], mid_len[mid_nodes], leaf_len[request_ids])


def shards(
    hidden,
    gain_attn,
    w_query,
    w_key,
    w_value,
    w_out,
    gain_ffn,
    w_gate,
    w_up,
    w_down,
    shared_pages,
    leaf_pages,
    root_table,
    mid_table,
    leaf_table,
    root_len,
    mid_len,
    leaf_len,
    mid_parent,
    leaf_parent,
    slot_request,
):
    new_rows, local_reqs, model_width = hidden.shape
    seq_count = lax.axis_size("seq")
    seq_index = lax.axis_index("seq")
    kv_local = leaf_pages.shape[1]
    group_size = QH // KVH
    pages_here = leaf_pages.shape[0]
    slot_ids = seq_index * local_reqs + jnp.arange(local_reqs, dtype=jnp.int32)
    requests = slot_request[slot_ids]
    root_nodes, mid_nodes, root_span, mid_span, leaf_span = spans(
        requests, root_len, mid_len, leaf_len, mid_parent, leaf_parent
    )
    context = root_span + mid_span + leaf_span
    new_index = jnp.arange(new_rows, dtype=jnp.int32)
    query_pos = context[None, :] + new_index[:, None]
    all_slots = slot_request.reshape(seq_count, local_reqs)
    page_store = lax.all_gather(shared_pages, "seq", axis=0, tiled=True)
    root_index = root_table[root_nodes]
    mid_index = mid_table[mid_nodes]
    normed = rms_norm(hidden, gain_attn).reshape(-1, model_width)
    query_proj = jnp.dot(normed, w_query, preferred_element_type=jnp.float32).reshape(
        new_rows, local_reqs, -1, HD
    )
    queries = (
        rotate(query_proj, query_pos[:, :, None])
        .astype(jnp.bfloat16)
        .reshape(new_rows, local_reqs, kv_local, group_size, HD)
    )
    key_proj = jnp.dot(normed, w_key, preferred_element_type=jnp.float32).reshape(
        new_rows, local_reqs, kv_local, HD
    )
    new_keys = rotate(key_proj, query_pos[:, :, None]).astype(jnp.bfloat16)
    new_values = (
        jnp.dot(normed, w_value, preferred_element_type=jnp.float32)
        .astype(jnp.bfloat16)
        .reshape(new_rows, local_reqs, kv_local, HD)
    )
    home_of = leaf_table[:, 0] // pages_here
    own_homes = home_of[requests]
    sender_match = home_of[all_slots] == seq_index
    sender_pick = jnp.argmax(sender_match, 1)
    sender_have = jnp.any(sender_match, 1)
    picked_request = jnp.take_along_axis(all_slots, sender_pick[:, None], 1)[:, 0]
    page_ids = jnp.where(
        sender_have[:, None], leaf_table[picked_request] - seq_index * pages_here, 0
    )
    leaf_slots = leaf_table.shape[1]
    outgoing = jnp.where(
        sender_have[:, None, None, None, None, None], jnp.take(leaf_pages, page_ids, axis=0), 0
    )
    arrived = lax.all_to_all(outgoing, "seq", split_axis=0, concat_axis=0, tiled=True)
    page_shape = arrived.shape[-3:]
    leaf_store = arrived.reshape((-1,) + page_shape)
    shared_store = page_store.reshape((-1,) + page_shape)
    tbl = jnp.concatenate(
        [
            root_index,
            mid_index,
            own_homes[:, None] * leaf_slots + jnp.arange(leaf_slots, dtype=jnp.int32)[None, :],
        ],
        1,
    ).astype(jnp.int32)
    meta = jnp.stack([root_span, mid_span, leaf_span, context], 1).astype(jnp.int32)
    fresh_pack = jnp.stack(
        [jnp.transpose(new_keys[:, :, 0], (1, 2, 0)), jnp.transpose(new_values[:, :, 0], (1, 2, 0))], 1
    )
    query_rows = jnp.transpose(queries[:, :, 0], (1, 2, 0, 3)).reshape(local_reqs, -1, HD)
    attended = paged_attention(tbl, meta, query_rows, fresh_pack, shared_store, leaf_store)
    attended = (
        jnp.transpose(attended.reshape(local_reqs, group_size, new_rows, HD), (2, 0, 1, 3))
        .reshape(new_rows * local_reqs, -1)
    )
    tp_count = lax.axis_size("tp")
    own_count = new_rows // tp_count
    attn_proj = (
        lax.psum_scatter(
            jnp.dot(attended, w_out, preferred_element_type=jnp.float32).astype(jnp.bfloat16),
            "tp",
            scatter_dimension=0,
            tiled=True,
        )
        .astype(jnp.float32)
        .reshape(own_count, local_reqs, model_width)
    )
    own_hidden = lax.dynamic_slice_in_dim(hidden, lax.axis_index("tp") * own_count, own_count, 0)
    resid = own_hidden.astype(jnp.float32) + attn_proj
    normed_own = rms_norm(resid, gain_ffn).reshape(-1, model_width)
    normed_ffn = lax.all_gather(normed_own, "tp", axis=0, tiled=True)
    gate_rows = jnp.dot(normed_ffn, w_gate, preferred_element_type=jnp.float32)
    up_rows = jnp.dot(normed_ffn, w_up, preferred_element_type=jnp.float32)
    activated = (jax.nn.silu(gate_rows) * up_rows).astype(jnp.bfloat16)
    ffn_proj = (
        lax.psum_scatter(
            jnp.dot(activated, w_down, preferred_element_type=jnp.float32).astype(jnp.bfloat16),
            "tp",
            scatter_dimension=0,
            tiled=True,
        )
        .astype(jnp.float32)
        .reshape(own_count, local_reqs, model_width)
    )
    return resid + ffn_proj


def solution(mesh):
    return jax.shard_map(
        shards,
        mesh=mesh,
        in_specs=(
            P(None, "seq", None),
            P(),
            P(None, "tp"),
            P(None, "tp"),
            P(None, "tp"),
            P("tp", None),
            P(),
            P(None, "tp"),
            P(None, "tp"),
            P("tp", None),
            P("seq", "tp", None, None, None),
            P("seq", "tp", None, None, None),
            P(),
            P(),
            P(),
            P(),
            P(),
            P(),
            P(),
            P(),
            P(),
        ),
        out_specs=P("tp", "seq", None),
        check_vma=False,
    )
```

```python
import jax
import jax.numpy as jnp
from jax import lax
from jax.sharding import PartitionSpec as P
from jax.experimental import pallas as pl
from jax.experimental.pallas import tpu as pltpu

QH = 32
KVH = 8
HD = 80
WINDOW = 4096


masked_score = -1e30
rope_base = 10000.0


def rms_norm(row_data, gain_vector):
    values = row_data.astype(jnp.float32)
    inverse_rms = lax.rsqrt(jnp.mean(values * values, -1, keepdims=True) + 1e-05)
    return (values * inverse_rms * gain_vector.astype(jnp.float32)).astype(jnp.bfloat16)


def rotate(vector, position):
    half_size = vector.shape[-1] // 2
    frequency = rope_base ** (-2.0 * jnp.arange(half_size, dtype=jnp.float32) / vector.shape[-1])
    angles = position.astype(jnp.float32)[..., None] * frequency
    cos_part = jnp.cos(angles)
    sin_part = jnp.sin(angles)
    first_half = vector[..., :half_size]
    second_half = vector[..., half_size:]
    return jnp.concatenate(
        [
            first_half * cos_part - second_half * sin_part,
            second_half * cos_part + first_half * sin_part,
        ],
        -1,
    )


def page_columns(pages):
    moved = jnp.moveaxis(pages, -5, -2)
    return moved.reshape(moved.shape[:-2] + (moved.shape[-2] * moved.shape[-1],))


def attend(queries, key_pack, key_pos, present, query_pos):
    scores = jnp.einsum(
        "nbkge,bket->nbkgt", queries, key_pack[:, :, 0], preferred_element_type=jnp.float32
    ) * queries.shape[-1] ** (-0.5)
    distance = query_pos[:, :, None] - key_pos[None, :, :]
    allowed = (present[None, :, :] & (distance >= 0) & (distance < WINDOW))[:, :, None, None, :]
    scores = jnp.where(allowed, scores, masked_score)
    maximum = jnp.max(scores, -1)
    weights = jnp.where(allowed, jnp.exp(scores - maximum[..., None]), 0.0)
    totals = jnp.sum(weights, -1)
    weighted = jnp.einsum(
        "nbkgt,bket->nbkge",
        weights.astype(jnp.bfloat16),
        key_pack[:, :, 1],
        preferred_element_type=jnp.float32,
    )
    return (weighted, maximum, totals)


def merge_parts(first, second):
    maximum = jnp.maximum(first[1], second[1])
    first_scale = jnp.exp(first[1] - maximum)
    second_scale = jnp.exp(second[1] - maximum)
    return (
        first[0] * first_scale[..., None] + second[0] * second_scale[..., None],
        maximum,
        first[2] * first_scale + second[2] * second_scale,
    )


ROOT_PAGES = 16
MID_PAGES = 16
LEAF_SLOTS = 8
CHUNK_PAGES = 8


def part_body(chunk0, group, tbl, meta, q_ref, store_hbm, kv, sc, top, mass, acc, sem, begin, finish):
    b = pl.program_id(0)
    requests = pl.num_programs(0)
    slot = b % 2
    shared_count = ROOT_PAGES + MID_PAGES
    page_count = kv.shape[1]
    width = kv.shape[-1]
    span = group * width

    def start_request(j, into):
        def page_body(p, carry):
            pltpu.make_async_copy(store_hbm.at[tbl[j, p]], kv.at[into, p], sem.at[into]).start()
            return carry

        lax.fori_loop(0, page_count, page_body, 0)

    @pl.when(b == 0)
    def _():
        start_request(0, 0)

    @pl.when(b + 1 < requests)
    def _():
        start_request(b + 1, 1 - slot)

    def wait_body(p, carry):
        pltpu.make_async_copy(store_hbm.at[0], kv.at[slot, p], sem.at[slot]).wait()
        return carry

    lax.fori_loop(0, page_count, wait_body, 0)

    root_span = meta[b, 0]
    mid_span = meta[b, 1]
    leaf_span = meta[b, 2]
    context = meta[b, 3]
    q = q_ref[0]
    rows = q.shape[0]
    query_pos = context + (lax.broadcasted_iota(jnp.int32, (rows, 1), 0) % width)
    lanes = lax.broadcasted_iota(jnp.int32, (1, span), 1)
    scale = HD ** (-0.5)

    def masked(s, key_pos, present):
        distance = query_pos - key_pos
        allowed = present & (distance >= 0) & (distance < WINDOW)
        return jnp.where(allowed, s, masked_score)

    def geometry(c):
        page = group * (chunk0 + c)
        in_root = page < ROOT_PAGES
        in_mid = page < shared_count
        first = jnp.where(
            in_root, page * width, jnp.where(in_mid, (page - ROOT_PAGES) * width, (page - shared_count) * width)
        )
        base = jnp.where(in_root, 0, jnp.where(in_mid, root_span, root_span + mid_span))
        limit = jnp.where(in_root, root_span, jnp.where(in_mid, mid_span, leaf_span))
        live = (first < limit) & (context - (base + first + span - 1) < WINDOW)
        return first, base, limit, live

    def pages_of(c, part):
        return jnp.concatenate([kv[slot, group * c + k, part] for k in range(group)], 1)

    begin(q, query_pos, masked, scale)

    def keep(c, s):
        sc[c] = s
        m = top[...]
        for k in range(group):
            m = jnp.maximum(m, s[:, k * width:(k + 1) * width])
        top[...] = m

    def max_body(c, carry):
        first, base, limit, live = geometry(c)
        full = (first + span <= limit) & (context + width - 1 - (base + first) < WINDOW)

        @pl.when(full)
        def _():
            keep(c, jnp.dot(q, pages_of(c, 0), preferred_element_type=jnp.float32) * scale)

        @pl.when(live & jnp.logical_not(full))
        def _():
            steps_in = first + lanes
            s = jnp.dot(q, pages_of(c, 0), preferred_element_type=jnp.float32) * scale
            keep(c, masked(s, base + steps_in, steps_in < limit))

        return carry

    chunks = page_count // group
    lax.fori_loop(0, chunks, max_body, 0)
    earlier = top[...]
    top[...] = jnp.broadcast_to(jnp.max(earlier, -1, keepdims=True), top.shape)
    row_top = top[...]
    finish(row_top)

    def sum_body(c, carry):
        first, base, limit, live = geometry(c)

        @pl.when(live)
        def _():
            s = sc[c]
            parts = [jnp.exp(s[:, k * width:(k + 1) * width] - row_top) for k in range(group)]
            total = mass[...]
            for part in parts:
                total = total + part
            mass[...] = total
            w = jnp.concatenate(parts, 1).astype(jnp.bfloat16)
            acc[...] = acc[...] + lax.dot_general(
                w, pages_of(c, 1), (((1,), (1,)), ((), ())), preferred_element_type=jnp.float32
            )

        return carry

    lax.fori_loop(0, chunks, sum_body, 0)


def leaf_kernel(tbl, meta, q_ref, fresh_ref, store_hbm, acc_out, top_out, mass_out, kv, sc, fresh_sc, top, mass, acc, sem):
    def begin(q, query_pos, masked, scale):
        width = fresh_sc.shape[-1]
        fresh_lanes = lax.broadcasted_iota(jnp.int32, (1, width), 1)
        fresh_scores = masked(
            jnp.dot(q, fresh_ref[0, 0], preferred_element_type=jnp.float32) * scale,
            meta[pl.program_id(0), 3] + fresh_lanes,
            fresh_lanes >= 0,
        )
        fresh_sc[...] = fresh_scores
        top[...] = fresh_scores

    def finish(row_top):
        fresh_w = jnp.exp(fresh_sc[...] - row_top)
        mass[...] = fresh_w
        acc[...] = lax.dot_general(
            fresh_w.astype(jnp.bfloat16), fresh_ref[0, 1], (((1,), (1,)), ((), ())),
            preferred_element_type=jnp.float32,
        )

    part_body(
        (ROOT_PAGES + MID_PAGES) // LEAF_SLOTS, LEAF_SLOTS, tbl, meta, q_ref, store_hbm, kv, sc, top, mass, acc,
        sem, begin, finish,
    )
    acc_out[0] = acc[...]
    top_out[0] = top[...]
    mass_out[0] = mass[...]


def shared_kernel(tbl, meta, q_ref, acc_in, top_in, mass_in, store_hbm, out_ref, kv, sc, top, mass, acc, sem):
    def begin(q, query_pos, masked, scale):
        top[...] = top_in[0]

    def finish(row_top):
        factor = jnp.exp(top_in[0] - row_top)
        mass[...] = mass_in[0] * factor
        acc[...] = acc_in[0] * factor[:, :1]

    part_body(0, ROOT_PAGES, tbl, meta, q_ref, store_hbm, kv, sc, top, mass, acc, sem, begin, finish)
    totals = jnp.sum(mass[...], -1, keepdims=True)
    out_ref[0] = (acc[...] / totals).astype(out_ref.dtype)


def part_call(kernel, tbl, meta, inputs, chunk, store, out_shapes):
    reqs, rows, head = inputs[0].shape
    page_shape = store.shape[1:]
    width = page_shape[-1]
    pages = tbl.shape[1]

    def block(shape):
        return pl.BlockSpec((1,) + shape[1:], lambda i, t, m: (i,) + (0,) * (len(shape) - 1))

    scratch = [
        pltpu.VMEM((2, pages) + page_shape, store.dtype),
        pltpu.VMEM((pages // chunk, rows, chunk * width), jnp.float32),
    ]
    if kernel is leaf_kernel:
        scratch.append(pltpu.VMEM((rows, width), jnp.float32))
    scratch += [
        pltpu.VMEM((rows, width), jnp.float32),
        pltpu.VMEM((rows, width), jnp.float32),
        pltpu.VMEM((rows, head), jnp.float32),
        pltpu.SemaphoreType.DMA((2,)),
    ]
    grid_spec = pltpu.PrefetchScalarGridSpec(
        num_scalar_prefetch=2,
        grid=(reqs,),
        in_specs=[block(x.shape) for x in inputs] + [pl.BlockSpec(memory_space=pl.ANY)],
        out_specs=[block(s.shape) for s in out_shapes],
        scratch_shapes=scratch,
    )
    keys_total = pages * width
    return pl.pallas_call(
        kernel,
        grid_spec=grid_spec,
        out_shape=out_shapes,
        compiler_params=pltpu.CompilerParams(dimension_semantics=("arbitrary",)),
        cost_estimate=pl.CostEstimate(
            flops=4 * reqs * rows * keys_total * head,
            transcendentals=reqs * rows * keys_total,
            bytes_accessed=reqs * pages * 2 * head * width * 2,
        ),
    )(tbl, meta, *inputs, store)


def paged_attention(tbl, meta, queries, fresh, shared_store, leaf_store):
    reqs, rows, head = queries.shape
    width = shared_store.shape[-1]
    shared_count = ROOT_PAGES + MID_PAGES
    state = part_call(
        leaf_kernel, tbl[:, shared_count:], meta, [queries, fresh], LEAF_SLOTS, leaf_store,
        [
            jax.ShapeDtypeStruct((reqs, rows, head), jnp.float32),
            jax.ShapeDtypeStruct((reqs, rows, width), jnp.float32),
            jax.ShapeDtypeStruct((reqs, rows, width), jnp.float32),
        ],
    )
    (out,) = part_call(
        shared_kernel, tbl[:, :shared_count], meta, [queries] + list(state), ROOT_PAGES, shared_store,
        [jax.ShapeDtypeStruct((reqs, rows, head), jnp.bfloat16)],
    )
    return out


def spans(request_ids, root_len, mid_len, leaf_len, mid_parent, leaf_parent):
    mid_nodes = leaf_parent[request_ids]
    root_nodes = mid_parent[mid_nodes]
    return (root_nodes, mid_nodes, root_len[root_nodes], mid_len[mid_nodes], leaf_len[request_ids])


def shards(
    hidden,
    gain_attn,
    w_query,
    w_key,
    w_value,
    w_out,
    gain_ffn,
    w_gate,
    w_up,
    w_down,
    shared_pages,
    leaf_pages,
    root_table,
    mid_table,
    leaf_table,
    root_len,
    mid_len,
    leaf_len,
    mid_parent,
    leaf_parent,
    slot_request,
):
    new_rows, local_reqs, model_width = hidden.shape
    seq_count = lax.axis_size("seq")
    seq_index = lax.axis_index("seq")
    kv_local = leaf_pages.shape[1]
    group_size = QH // KVH
    pages_here = leaf_pages.shape[0]
    slot_ids = seq_index * local_reqs + jnp.arange(local_reqs, dtype=jnp.int32)
    requests = slot_request[slot_ids]
    root_nodes, mid_nodes, root_span, mid_span, leaf_span = spans(
        requests, root_len, mid_len, leaf_len, mid_parent, leaf_parent
    )
    context = root_span + mid_span + leaf_span
    new_index = jnp.arange(new_rows, dtype=jnp.int32)
    query_pos = context[None, :] + new_index[:, None]
    all_slots = slot_request.reshape(seq_count, local_reqs)
    page_store = lax.all_gather(shared_pages, "seq", axis=0, tiled=True)
    root_index = root_table[root_nodes]
    mid_index = mid_table[mid_nodes]
    normed = rms_norm(hidden, gain_attn).reshape(-1, model_width)
    query_proj = jnp.dot(normed, w_query, preferred_element_type=jnp.float32).reshape(
        new_rows, local_reqs, -1, HD
    )
    queries = (
        rotate(query_proj, query_pos[:, :, None])
        .astype(jnp.bfloat16)
        .reshape(new_rows, local_reqs, kv_local, group_size, HD)
    )
    key_proj = jnp.dot(normed, w_key, preferred_element_type=jnp.float32).reshape(
        new_rows, local_reqs, kv_local, HD
    )
    new_keys = rotate(key_proj, query_pos[:, :, None]).astype(jnp.bfloat16)
    new_values = (
        jnp.dot(normed, w_value, preferred_element_type=jnp.float32)
        .astype(jnp.bfloat16)
        .reshape(new_rows, local_reqs, kv_local, HD)
    )
    home_of = leaf_table[:, 0] // pages_here
    own_homes = home_of[requests]
    sender_match = home_of[all_slots] == seq_index
    sender_pick = jnp.argmax(sender_match, 1)
    sender_have = jnp.any(sender_match, 1)
    picked_request = jnp.take_along_axis(all_slots, sender_pick[:, None], 1)[:, 0]
    page_ids = jnp.where(
        sender_have[:, None], leaf_table[picked_request] - seq_index * pages_here, 0
    )
    leaf_slots = leaf_table.shape[1]
    outgoing = jnp.where(
        sender_have[:, None, None, None, None, None], jnp.take(leaf_pages, page_ids, axis=0), 0
    )
    arrived = lax.all_to_all(outgoing, "seq", split_axis=0, concat_axis=0, tiled=True)
    page_shape = arrived.shape[-3:]
    leaf_store = arrived.reshape((-1,) + page_shape)
    shared_store = page_store.reshape((-1,) + page_shape)
    tbl = jnp.concatenate(
        [
            root_index,
            mid_index,
            own_homes[:, None] * leaf_slots + jnp.arange(leaf_slots, dtype=jnp.int32)[None, :],
        ],
        1,
    ).astype(jnp.int32)
    meta = jnp.stack([root_span, mid_span, leaf_span, context], 1).astype(jnp.int32)
    fresh_pack = jnp.stack(
        [jnp.transpose(new_keys[:, :, 0], (1, 2, 0)), jnp.transpose(new_values[:, :, 0], (1, 2, 0))], 1
    )
    query_rows = jnp.transpose(queries[:, :, 0], (1, 2, 0, 3)).reshape(local_reqs, -1, HD)
    attended = paged_attention(tbl, meta, query_rows, fresh_pack, shared_store, leaf_store)
    attended = (
        jnp.transpose(attended.reshape(local_reqs, group_size, new_rows, HD), (2, 0, 1, 3))
        .reshape(new_rows * local_reqs, -1)
    )
    tp_count = lax.axis_size("tp")
    own_count = new_rows // tp_count
    attn_proj = (
        lax.psum_scatter(
            jnp.dot(attended, w_out, preferred_element_type=jnp.float32).astype(jnp.bfloat16),
            "tp",
            scatter_dimension=0,
            tiled=True,
        )
        .astype(jnp.float32)
        .reshape(own_count, local_reqs, model_width)
    )
    own_hidden = lax.dynamic_slice_in_dim(hidden, lax.axis_index("tp") * own_count, own_count, 0)
    resid = own_hidden.astype(jnp.float32) + attn_proj
    normed_own = rms_norm(resid, gain_ffn).reshape(-1, model_width)
    normed_ffn = lax.all_gather(normed_own, "tp", axis=0, tiled=True)
    gate_rows = jnp.dot(normed_ffn, w_gate, preferred_element_type=jnp.float32)
    up_rows = jnp.dot(normed_ffn, w_up, preferred_element_type=jnp.float32)
    activated = (jax.nn.silu(gate_rows) * up_rows).astype(jnp.bfloat16)
    ffn_proj = (
        lax.psum_scatter(
            jnp.dot(activated, w_down, preferred_element_type=jnp.float32).astype(jnp.bfloat16),
            "tp",
            scatter_dimension=0,
            tiled=True,
        )
        .astype(jnp.float32)
        .reshape(own_count, local_reqs, model_width)
    )
    return resid + ffn_proj


def solution(mesh):
    return jax.shard_map(
        shards,
        mesh=mesh,
        in_specs=(
            P(None, "seq", None),
            P(),
            P(None, "tp"),
            P(None, "tp"),
            P(None, "tp"),
            P("tp", None),
            P(),
            P(None, "tp"),
            P(None, "tp"),
            P("tp", None),
            P("seq", "tp", None, None, None),
            P("seq", "tp", None, None, None),
            P(),
            P(),
            P(),
            P(),
            P(),
            P(),
            P(),
            P(),
            P(),
        ),
        out_specs=P("tp", "seq", None),
        check_vma=False,
    )
```

```python
import jax
import jax.numpy as jnp
from jax import lax
from jax.sharding import PartitionSpec as P
from jax.experimental import pallas as pl
from jax.experimental.pallas import tpu as pltpu

QH = 32
KVH = 8
HD = 80
WINDOW = 4096


masked_score = -1e30
rope_base = 10000.0


def rms_norm(row_data, gain_vector):
    values = row_data.astype(jnp.float32)
    inverse_rms = lax.rsqrt(jnp.mean(values * values, -1, keepdims=True) + 1e-05)
    return (values * inverse_rms * gain_vector.astype(jnp.float32)).astype(jnp.bfloat16)


def rotate(vector, position):
    half_size = vector.shape[-1] // 2
    frequency = rope_base ** (-2.0 * jnp.arange(half_size, dtype=jnp.float32) / vector.shape[-1])
    angles = position.astype(jnp.float32)[..., None] * frequency
    cos_part = jnp.cos(angles)
    sin_part = jnp.sin(angles)
    first_half = vector[..., :half_size]
    second_half = vector[..., half_size:]
    return jnp.concatenate(
        [
            first_half * cos_part - second_half * sin_part,
            second_half * cos_part + first_half * sin_part,
        ],
        -1,
    )


def page_columns(pages):
    moved = jnp.moveaxis(pages, -5, -2)
    return moved.reshape(moved.shape[:-2] + (moved.shape[-2] * moved.shape[-1],))


def attend(queries, key_pack, key_pos, present, query_pos):
    scores = jnp.einsum(
        "nbkge,bket->nbkgt", queries, key_pack[:, :, 0], preferred_element_type=jnp.float32
    ) * queries.shape[-1] ** (-0.5)
    distance = query_pos[:, :, None] - key_pos[None, :, :]
    allowed = (present[None, :, :] & (distance >= 0) & (distance < WINDOW))[:, :, None, None, :]
    scores = jnp.where(allowed, scores, masked_score)
    maximum = jnp.max(scores, -1)
    weights = jnp.where(allowed, jnp.exp(scores - maximum[..., None]), 0.0)
    totals = jnp.sum(weights, -1)
    weighted = jnp.einsum(
        "nbkgt,bket->nbkge",
        weights.astype(jnp.bfloat16),
        key_pack[:, :, 1],
        preferred_element_type=jnp.float32,
    )
    return (weighted, maximum, totals)


def merge_parts(first, second):
    maximum = jnp.maximum(first[1], second[1])
    first_scale = jnp.exp(first[1] - maximum)
    second_scale = jnp.exp(second[1] - maximum)
    return (
        first[0] * first_scale[..., None] + second[0] * second_scale[..., None],
        maximum,
        first[2] * first_scale + second[2] * second_scale,
    )


ROOT_PAGES = 16
MID_PAGES = 16
LEAF_SLOTS = 8
CHUNK_PAGES = 8


def part_body(chunk0, with_fresh, tbl, meta, q_ref, store_hbm, kv, sc, top, mass, acc, sem, begin, finish):
    b = pl.program_id(0)
    requests = pl.num_programs(0)
    slot = b % 2
    shared_count = ROOT_PAGES + MID_PAGES
    page_count = kv.shape[1]
    width = kv.shape[-1]
    group = CHUNK_PAGES
    span = group * width

    def start_request(j, into):
        def page_body(p, carry):
            pltpu.make_async_copy(store_hbm.at[tbl[j, p]], kv.at[into, p], sem.at[into]).start()
            return carry

        lax.fori_loop(0, page_count, page_body, 0)

    @pl.when(b == 0)
    def _():
        start_request(0, 0)

    @pl.when(b + 1 < requests)
    def _():
        start_request(b + 1, 1 - slot)

    def wait_body(p, carry):
        pltpu.make_async_copy(store_hbm.at[0], kv.at[slot, p], sem.at[slot]).wait()
        return carry

    lax.fori_loop(0, page_count, wait_body, 0)

    root_span = meta[b, 0]
    mid_span = meta[b, 1]
    leaf_span = meta[b, 2]
    context = meta[b, 3]
    q = q_ref[0]
    rows = q.shape[0]
    query_pos = context + (lax.broadcasted_iota(jnp.int32, (rows, 1), 0) % width)
    lanes = lax.broadcasted_iota(jnp.int32, (1, span), 1)
    scale = HD ** (-0.5)

    def masked(s, key_pos, present):
        distance = query_pos - key_pos
        allowed = present & (distance >= 0) & (distance < WINDOW)
        return jnp.where(allowed, s, masked_score)

    def geometry(c):
        page = group * (chunk0 + c)
        in_root = page < ROOT_PAGES
        in_mid = page < shared_count
        first = jnp.where(
            in_root, page * width, jnp.where(in_mid, (page - ROOT_PAGES) * width, (page - shared_count) * width)
        )
        base = jnp.where(in_root, 0, jnp.where(in_mid, root_span, root_span + mid_span))
        limit = jnp.where(in_root, root_span, jnp.where(in_mid, mid_span, leaf_span))
        live = (first < limit) & (context - (base + first + span - 1) < WINDOW)
        return first, base, limit, live

    def pages_of(c, part):
        return jnp.concatenate([kv[slot, group * c + k, part] for k in range(group)], 1)

    begin(q, query_pos, masked, scale)

    def keep(c, s):
        sc[c] = s
        m = top[...]
        for k in range(group):
            m = jnp.maximum(m, s[:, k * width:(k + 1) * width])
        top[...] = m

    def max_body(c, carry):
        first, base, limit, live = geometry(c)
        full = (first + span <= limit) & (context + width - 1 - (base + first) < WINDOW)

        @pl.when(full)
        def _():
            keep(c, jnp.dot(q, pages_of(c, 0), preferred_element_type=jnp.float32) * scale)

        @pl.when(live & jnp.logical_not(full))
        def _():
            steps_in = first + lanes
            s = jnp.dot(q, pages_of(c, 0), preferred_element_type=jnp.float32) * scale
            keep(c, masked(s, base + steps_in, steps_in < limit))

        return carry

    chunks = page_count // group
    lax.fori_loop(0, chunks, max_body, 0)
    earlier = top[...]
    top[...] = jnp.broadcast_to(jnp.max(earlier, -1, keepdims=True), top.shape)
    row_top = top[...]
    finish(row_top)

    def sum_body(c, carry):
        first, base, limit, live = geometry(c)

        @pl.when(live)
        def _():
            s = sc[c]
            parts = [jnp.exp(s[:, k * width:(k + 1) * width] - row_top) for k in range(group)]
            total = mass[...]
            for part in parts:
                total = total + part
            mass[...] = total
            w = jnp.concatenate(parts, 1).astype(jnp.bfloat16)
            acc[...] = acc[...] + lax.dot_general(
                w, pages_of(c, 1), (((1,), (1,)), ((), ())), preferred_element_type=jnp.float32
            )

        return carry

    lax.fori_loop(0, chunks, sum_body, 0)


def leaf_kernel(tbl, meta, q_ref, fresh_ref, store_hbm, acc_out, top_out, mass_out, kv, sc, fresh_sc, top, mass, acc, sem):
    def begin(q, query_pos, masked, scale):
        width = fresh_sc.shape[-1]
        fresh_lanes = lax.broadcasted_iota(jnp.int32, (1, width), 1)
        fresh_scores = masked(
            jnp.dot(q, fresh_ref[0, 0], preferred_element_type=jnp.float32) * scale,
            meta[pl.program_id(0), 3] + fresh_lanes,
            fresh_lanes >= 0,
        )
        fresh_sc[...] = fresh_scores
        top[...] = fresh_scores

    def finish(row_top):
        fresh_w = jnp.exp(fresh_sc[...] - row_top)
        mass[...] = fresh_w
        acc[...] = lax.dot_general(
            fresh_w.astype(jnp.bfloat16), fresh_ref[0, 1], (((1,), (1,)), ((), ())),
            preferred_element_type=jnp.float32,
        )

    part_body(
        (ROOT_PAGES + MID_PAGES) // CHUNK_PAGES, True, tbl, meta, q_ref, store_hbm, kv, sc, top, mass, acc, sem,
        begin, finish,
    )
    acc_out[0] = acc[...]
    top_out[0] = top[...]
    mass_out[0] = mass[...]


def shared_kernel(tbl, meta, q_ref, acc_in, top_in, mass_in, store_hbm, out_ref, kv, sc, top, mass, acc, sem):
    def begin(q, query_pos, masked, scale):
        top[...] = top_in[0]

    def finish(row_top):
        factor = jnp.exp(top_in[0] - row_top)
        mass[...] = mass_in[0] * factor
        acc[...] = acc_in[0] * factor[:, :1]

    part_body(0, False, tbl, meta, q_ref, store_hbm, kv, sc, top, mass, acc, sem, begin, finish)
    totals = jnp.sum(mass[...], -1, keepdims=True)
    out_ref[0] = (acc[...] / totals).astype(out_ref.dtype)


def part_call(kernel, tbl, meta, inputs, in_blocks, store, out_shapes):
    reqs, rows, head = inputs[0].shape
    page_shape = store.shape[1:]
    width = page_shape[-1]
    pages = tbl.shape[1]

    def block(shape):
        return pl.BlockSpec((1,) + shape[1:], lambda i, t, m: (i,) + (0,) * (len(shape) - 1))

    scratch = [
        pltpu.VMEM((2, pages) + page_shape, store.dtype),
        pltpu.VMEM((pages // CHUNK_PAGES, rows, CHUNK_PAGES * width), jnp.float32),
    ]
    if kernel is leaf_kernel:
        scratch.append(pltpu.VMEM((rows, width), jnp.float32))
    scratch += [
        pltpu.VMEM((rows, width), jnp.float32),
        pltpu.VMEM((rows, width), jnp.float32),
        pltpu.VMEM((rows, head), jnp.float32),
        pltpu.SemaphoreType.DMA((2,)),
    ]
    grid_spec = pltpu.PrefetchScalarGridSpec(
        num_scalar_prefetch=2,
        grid=(reqs,),
        in_specs=[block(x.shape) for x in inputs] + [pl.BlockSpec(memory_space=pl.ANY)],
        out_specs=[block(s.shape) for s in out_shapes],
        scratch_shapes=scratch,
    )
    keys_total = pages * width
    return pl.pallas_call(
        kernel,
        grid_spec=grid_spec,
        out_shape=out_shapes,
        compiler_params=pltpu.CompilerParams(dimension_semantics=("arbitrary",)),
        cost_estimate=pl.CostEstimate(
            flops=4 * reqs * rows * keys_total * head,
            transcendentals=reqs * rows * keys_total,
            bytes_accessed=reqs * pages * 2 * head * width * 2,
        ),
    )(tbl, meta, *inputs, store)


def paged_attention(tbl, meta, queries, fresh, shared_store, leaf_store):
    reqs, rows, head = queries.shape
    width = shared_store.shape[-1]
    shared_count = ROOT_PAGES + MID_PAGES
    state = part_call(
        leaf_kernel, tbl[:, shared_count:], meta, [queries, fresh], None, leaf_store,
        [
            jax.ShapeDtypeStruct((reqs, rows, head), jnp.float32),
            jax.ShapeDtypeStruct((reqs, rows, width), jnp.float32),
            jax.ShapeDtypeStruct((reqs, rows, width), jnp.float32),
        ],
    )
    (out,) = part_call(
        shared_kernel, tbl[:, :shared_count], meta, [queries] + list(state), None, shared_store,
        [jax.ShapeDtypeStruct((reqs, rows, head), jnp.bfloat16)],
    )
    return out


def tp_row_sum(partial):
    count = lax.axis_size("tp")
    blocks = partial.astype(jnp.bfloat16).reshape((count, -1) + partial.shape[1:])
    arrived = lax.all_to_all(blocks, "tp", 0, 0, tiled=True)
    return jnp.sum(arrived.astype(jnp.float32), 0)


def spans(request_ids, root_len, mid_len, leaf_len, mid_parent, leaf_parent):
    mid_nodes = leaf_parent[request_ids]
    root_nodes = mid_parent[mid_nodes]
    return (root_nodes, mid_nodes, root_len[root_nodes], mid_len[mid_nodes], leaf_len[request_ids])


def shards(
    hidden,
    gain_attn,
    w_query,
    w_key,
    w_value,
    w_out,
    gain_ffn,
    w_gate,
    w_up,
    w_down,
    shared_pages,
    leaf_pages,
    root_table,
    mid_table,
    leaf_table,
    root_len,
    mid_len,
    leaf_len,
    mid_parent,
    leaf_parent,
    slot_request,
):
    new_rows, local_reqs, model_width = hidden.shape
    seq_count = lax.axis_size("seq")
    seq_index = lax.axis_index("seq")
    kv_local = leaf_pages.shape[1]
    group_size = QH // KVH
    pages_here = leaf_pages.shape[0]
    slot_ids = seq_index * local_reqs + jnp.arange(local_reqs, dtype=jnp.int32)
    requests = slot_request[slot_ids]
    root_nodes, mid_nodes, root_span, mid_span, leaf_span = spans(
        requests, root_len, mid_len, leaf_len, mid_parent, leaf_parent
    )
    context = root_span + mid_span + leaf_span
    new_index = jnp.arange(new_rows, dtype=jnp.int32)
    query_pos = context[None, :] + new_index[:, None]
    all_slots = slot_request.reshape(seq_count, local_reqs)
    page_store = lax.all_gather(shared_pages, "seq", axis=0, tiled=True)
    root_index = root_table[root_nodes]
    mid_index = mid_table[mid_nodes]
    normed = rms_norm(hidden, gain_attn).reshape(-1, model_width)
    query_proj = jnp.dot(normed, w_query, preferred_element_type=jnp.float32).reshape(
        new_rows, local_reqs, -1, HD
    )
    queries = (
        rotate(query_proj, query_pos[:, :, None])
        .astype(jnp.bfloat16)
        .reshape(new_rows, local_reqs, kv_local, group_size, HD)
    )
    key_proj = jnp.dot(normed, w_key, preferred_element_type=jnp.float32).reshape(
        new_rows, local_reqs, kv_local, HD
    )
    new_keys = rotate(key_proj, query_pos[:, :, None]).astype(jnp.bfloat16)
    new_values = (
        jnp.dot(normed, w_value, preferred_element_type=jnp.float32)
        .astype(jnp.bfloat16)
        .reshape(new_rows, local_reqs, kv_local, HD)
    )
    home_of = leaf_table[:, 0] // pages_here
    own_homes = home_of[requests]
    sender_match = home_of[all_slots] == seq_index
    sender_pick = jnp.argmax(sender_match, 1)
    sender_have = jnp.any(sender_match, 1)
    picked_request = jnp.take_along_axis(all_slots, sender_pick[:, None], 1)[:, 0]
    page_ids = jnp.where(
        sender_have[:, None], leaf_table[picked_request] - seq_index * pages_here, 0
    )
    leaf_slots = leaf_table.shape[1]
    outgoing = jnp.where(
        sender_have[:, None, None, None, None, None], jnp.take(leaf_pages, page_ids, axis=0), 0
    )
    arrived = lax.all_to_all(outgoing, "seq", split_axis=0, concat_axis=0, tiled=True)
    page_shape = arrived.shape[-3:]
    leaf_store = arrived.reshape((-1,) + page_shape)
    shared_store = page_store.reshape((-1,) + page_shape)
    tbl = jnp.concatenate(
        [
            root_index,
            mid_index,
            own_homes[:, None] * leaf_slots + jnp.arange(leaf_slots, dtype=jnp.int32)[None, :],
        ],
        1,
    ).astype(jnp.int32)
    meta = jnp.stack([root_span, mid_span, leaf_span, context], 1).astype(jnp.int32)
    fresh_pack = jnp.stack(
        [jnp.transpose(new_keys[:, :, 0], (1, 2, 0)), jnp.transpose(new_values[:, :, 0], (1, 2, 0))], 1
    )
    query_rows = jnp.transpose(queries[:, :, 0], (1, 2, 0, 3)).reshape(local_reqs, -1, HD)
    attended = paged_attention(tbl, meta, query_rows, fresh_pack, shared_store, leaf_store)
    attended = (
        jnp.transpose(attended.reshape(local_reqs, group_size, new_rows, HD), (2, 0, 1, 3))
        .reshape(new_rows * local_reqs, -1)
    )
    tp_count = lax.axis_size("tp")
    own_count = new_rows // tp_count
    attn_proj = tp_row_sum(jnp.dot(attended, w_out, preferred_element_type=jnp.float32)).reshape(
        own_count, local_reqs, model_width
    )
    own_hidden = lax.dynamic_slice_in_dim(hidden, lax.axis_index("tp") * own_count, own_count, 0)
    resid = own_hidden.astype(jnp.float32) + attn_proj
    normed_own = rms_norm(resid, gain_ffn).reshape(-1, model_width)
    normed_ffn = lax.all_gather(normed_own, "tp", axis=0, tiled=True)
    gate_rows = jnp.dot(normed_ffn, w_gate, preferred_element_type=jnp.float32)
    up_rows = jnp.dot(normed_ffn, w_up, preferred_element_type=jnp.float32)
    activated = (jax.nn.silu(gate_rows) * up_rows).astype(jnp.bfloat16)
    ffn_proj = tp_row_sum(jnp.dot(activated, w_down, preferred_element_type=jnp.float32)).reshape(
        own_count, local_reqs, model_width
    )
    return resid + ffn_proj


def solution(mesh):
    return jax.shard_map(
        shards,
        mesh=mesh,
        in_specs=(
            P(None, "seq", None),
            P(),
            P(None, "tp"),
            P(None, "tp"),
            P(None, "tp"),
            P("tp", None),
            P(),
            P(None, "tp"),
            P(None, "tp"),
            P("tp", None),
            P("seq", "tp", None, None, None),
            P("seq", "tp", None, None, None),
            P(),
            P(),
            P(),
            P(),
            P(),
            P(),
            P(),
            P(),
            P(),
        ),
        out_specs=P("tp", "seq", None),
        check_vma=False,
    )
```
